32 devices in a mesh: grp: 2 (over y), blk: 4 (over z), win: 2 (over x), freq: 2 (over core).
Axes of the slice: x: 2, y: 2, z: 4, core: 2. Of those that a mesh axis runs over, the one named last changes fastest.
Arguments:
- spectra: bfloat16 [1024, 2, 2, 2048], P(('grp', 'blk'), 'win', None, 'freq'), parts along dimension 0, may hold values from -600 to 600
- live_mask: int32 [1024, 2], P(('grp', 'blk'), 'win'), parts along dimension 0, may hold values 0 or 1
- pair_rows: int32 [8, 3, 2, 128], P('grp'), parts along dimension 0, may hold values from 0 to 127, as said below
- owner_map: int32 [8, 3], P('grp'), parts along dimension 0, may hold values from 0 to 3, as said below
Outputs:
- lag_stacks: bfloat16 [8, 4, 128, 512], P(('grp', 'blk'), None, ('win', 'freq')), parts along dimension 0
The draws below stay inside these ranges and needn't reach their ends.
There are 2 independent parts, one for each index of `grp`. The reference program is written for one: setup_inputs(seed, part) draws one part's arguments, and reference() takes and returns one part's arrays. A program takes and returns all parts, laid end to end along the dimension named above; each array names one. Nothing has to cross between parts.
Inputs may be any that keep to these rules, and one draw needn't show every extreme that they name: pair_rows[b, k, 0, p] is a channel of block b and pair_rows[b, k, 1, p] a channel of block (b + k) mod 4, both counted within their block; the two channels lie 1 to 256 channels apart along the loop. The 3 entries of a row of owner_map are different.
All inputs are finite; a program needn't handle non-finite values. No bound on the sum of `live_mask` on one device may be relied on, other than what follows from the above.
Results may differ from the reference program's by a relative error of at most 0.0068.
Values may be sent and summed in bfloat16 or wider, within the bound.
No kernel may reach another device: no remote copies, remote signals or barrier semaphores. Data moves between devices by JAX's collectives and lax.ppermute only.
A program may use at most 64 MiB of HBM per device.

```python
import math
import jax
import jax.numpy as jnp
from jax import lax

CH = 128
NF = 2048
NLAG = 512
SAMPLES = 12000
LAG_STRIDE = 3
PAIRS = 128
BLOCKS = 4
CHANNELS = 512
WINDOWS = 2
OFFSETS = 3


def draw_spectra(key, part):
    subkeys = jax.random.split(jax.random.fold_in(key, 3), 3)
    array_shape = (CHANNELS, WINDOWS, 2, NF)
    random_part = jnp.clip(jax.random.normal(subkeys[0], array_shape, jnp.float32), -5.0, 5.0)
    ramp_slope = jnp.log(3.0)
    channel_gain = jnp.exp(jax.random.uniform(subkeys[1], (CHANNELS, WINDOWS, 1, 1), jnp.float32, 0.0, jnp.log(10.0)))
    spectral_ramp = jnp.exp(ramp_slope * jnp.arange(NF, dtype=jnp.float32) / (NF - 1))
    bin_rough = jnp.exp(jax.random.uniform(subkeys[2], (NF,), jnp.float32, 0.0, jnp.log(10.0 / 3.0)))
    return (random_part * channel_gain * spectral_ramp * bin_rough).astype(jnp.bfloat16)


def draw_pair_rows(key, part):
    subkeys = jax.random.split(jax.random.fold_in(key, 9), 3)
    grid_shape = (BLOCKS, OFFSETS, PAIRS)
    first_pick = jax.random.randint(subkeys[0], grid_shape, 0, CH, dtype=jnp.int32)
    second_pick = jax.random.randint(subkeys[1], grid_shape, 0, CH, dtype=jnp.int32)
    spread_pick = jax.random.randint(subkeys[2], grid_shape, 0, 1 << 20, dtype=jnp.int32)
    offset_index = jnp.arange(OFFSETS, dtype=jnp.int32)[None, :, None]
    near_source = jnp.minimum(first_pick, CH - 2)
    near_partner = near_source + 1 + spread_pick % (CH - 1 - near_source)
    far_partner = spread_pick % (first_pick + 1)
    source_rows = jnp.where(offset_index == 0, near_source, first_pick)
    partner_rows = jnp.where(offset_index == 0, near_partner, jnp.where(offset_index == OFFSETS - 1, far_partner, second_pick))
    return jnp.stack([source_rows, partner_rows], axis=2).astype(jnp.int32)


def draw_owner_map(key, part):
    subkeys = jax.random.split(jax.random.fold_in(key, 5), 3)
    ranking = jax.random.permutation(subkeys[0], BLOCKS)
    popular = (ranking < max(BLOCKS // 4, 1)).astype(jnp.int32)
    scores = jax.random.randint(subkeys[1], (BLOCKS, BLOCKS), 0, 1 << 20, dtype=jnp.int32) + popular[None, :] * (1 << 21)
    scores = scores * BLOCKS + jnp.arange(BLOCKS, dtype=jnp.int32)[None, :]
    chosen = lax.top_k(scores, OFFSETS)[1].astype(jnp.int32)
    column_order = jax.random.permutation(subkeys[2], OFFSETS)
    return chosen[:, column_order].astype(jnp.int32)


def with_ends(array, own_key, smallest, largest):
    place = [jax.random.randint(jax.random.fold_in(own_key, axis), (), 0, length) for axis, length in enumerate(array.shape)]
    main_axis = array.shape.index(max(array.shape))
    beside = place[:main_axis] + [(place[main_axis] + 1) % array.shape[main_axis]] + place[main_axis + 1:]
    return array.at[tuple(place)].set(smallest).at[tuple(beside)].set(largest)


def setup_inputs(seed: int = 0, part: int = 0) -> dict:
    streams_of = jax.random.split(jax.random.key(seed), 5)
    part_keys = jax.random.split(jax.random.fold_in(streams_of[4], part), 5)
    spectra = draw_spectra(jax.random.fold_in(jax.random.fold_in(streams_of[4], part), 71), part)
    live_mask = with_ends((jax.random.randint(part_keys[1], (CHANNELS, WINDOWS), 0, 8) < 7).astype(jnp.int32), jax.random.fold_in(part_keys[1], 1), 0, 1)
    pair_rows = draw_pair_rows(jax.random.fold_in(jax.random.fold_in(streams_of[4], part), 71), part)
    owner_map = draw_owner_map(jax.random.fold_in(jax.random.fold_in(streams_of[4], part), 71), part)
    return dict(spectra=spectra, live_mask=live_mask, pair_rows=pair_rows, owner_map=owner_map)


def lag_table(first_bin, bin_count):
    bin_numbers = first_bin + jnp.arange(bin_count, dtype=jnp.int32)
    lag_numbers = (jnp.arange(NLAG, dtype=jnp.int32) - NLAG // 2) * LAG_STRIDE
    phase_index = (bin_numbers[:, None] + 1) * ((lag_numbers[None, :] + SAMPLES) % SAMPLES) % SAMPLES
    angles = phase_index.astype(jnp.float32) * (2.0 * math.pi / SAMPLES)
    return jnp.stack([jnp.cos(angles), -jnp.sin(angles)]).astype(jnp.bfloat16)

def whiten(spectra, live_mask):
    values = spectra.astype(jnp.float32)
    energy = values[:, :, 0] ** 2 + values[:, :, 1] ** 2
    mean_power = lax.optimization_barrier(jnp.sum(energy, axis=-1, keepdims=True)) / NF
    factor = live_mask.astype(jnp.float32)[:, :, None] / jnp.sqrt(energy + mean_power + 1e-06)
    return (values * factor[:, :, None, :]).astype(jnp.bfloat16)

def reference(spectra, live_mask, pair_rows, owner_map):
    whitened = whiten(spectra, live_mask)
    blocks = whitened.reshape(BLOCKS, CH, WINDOWS, 2, NF)
    table = lag_table(0, NF).astype(jnp.float32).reshape(2 * NF, NLAG)

    def per_block(block_id):
        source_block = lax.dynamic_index_in_dim(blocks, block_id, 0, keepdims=False)
        block_lists = lax.dynamic_index_in_dim(pair_rows, block_id, 0, keepdims=False)
        results = []
        for offset in range(OFFSETS):
            partner_id = ((block_id + offset) % BLOCKS).astype(jnp.int32)
            partner_block = lax.dynamic_index_in_dim(blocks, partner_id, 0, keepdims=False)
            source_rows = source_block[block_lists[offset, 0]].astype(jnp.float32)
            partner_rows = partner_block[block_lists[offset, 1]].astype(jnp.float32)
            cross_real = source_rows[:, :, 0] * partner_rows[:, :, 0] + source_rows[:, :, 1] * partner_rows[:, :, 1]
            cross_imag = source_rows[:, :, 1] * partner_rows[:, :, 0] - source_rows[:, :, 0] * partner_rows[:, :, 1]
            cross = jnp.stack([cross_real, cross_imag], axis=2).astype(jnp.bfloat16)
            cross = lax.optimization_barrier(cross).astype(jnp.float32)
            summed = lax.optimization_barrier(jnp.sum(cross, axis=1)).reshape(PAIRS, 2 * NF)
            results.append(jnp.dot(summed, table, precision=lax.Precision.HIGHEST, preferred_element_type=jnp.float32))
        return jnp.stack(results)
    correlations = lax.map(per_block, jnp.arange(BLOCKS, dtype=jnp.int32))
    scaled = correlations / math.sqrt(NF * WINDOWS)
    selector = (owner_map[:, :, None] == jnp.arange(BLOCKS, dtype=jnp.int32)[None, None, :]).astype(jnp.float32)
    routed = jnp.einsum('bko,bkpl->obpl', selector, scaled, precision=lax.Precision.HIGHEST)
    return routed.astype(jnp.bfloat16)
```

```python
import math

import jax
import jax.numpy as jnp
from jax import lax
from jax.sharding import PartitionSpec as P

NLAG = 512
SAMPLES = 12000
LAG_STRIDE = 3


def shifted(value, axis, steps):
    count = lax.axis_size(axis)
    pairs = [(source, (source + steps) % count) for source in range(count)]
    return lax.ppermute(value, axis, pairs)


def pair_sum(value, axis):
    if lax.axis_size(axis) == 2:
        return value + shifted(value, axis, 1)
    return lax.psum(value, axis)


def half_reduce(value, axis):
    count = lax.axis_size(axis)
    if count == 2:
        index = lax.axis_index(axis)
        halves = value.reshape((2, value.shape[0] // 2) + value.shape[1:])
        keep = lax.dynamic_index_in_dim(halves, index, 0, keepdims=False)
        send = lax.dynamic_index_in_dim(halves, 1 - index, 0, keepdims=False)
        return keep + shifted(send, axis, 1)
    return lax.psum_scatter(value, axis, scatter_dimension=0, tiled=True)


def lag_table(first_bin, bin_count):
    bin_numbers = first_bin + jnp.arange(bin_count, dtype=jnp.int32)
    lag_numbers = (jnp.arange(NLAG, dtype=jnp.int32) - NLAG // 2) * LAG_STRIDE
    phase_index = (
        (bin_numbers[:, None] + 1) * ((lag_numbers[None, :] + SAMPLES) % SAMPLES) % SAMPLES
    )
    angles = phase_index.astype(jnp.float32) * (2.0 * math.pi / SAMPLES)
    return jnp.stack([jnp.cos(angles), -jnp.sin(angles)]).astype(jnp.bfloat16)


def body(spectra, live_mask, pair_rows, owner_map):
    channels, windows, _, bin_count = spectra.shape
    real_in = spectra[:, :, 0].astype(jnp.float32)
    imag_in = spectra[:, :, 1].astype(jnp.float32)
    energy = real_in * real_in + imag_in * imag_in
    power_sums = pair_sum(jnp.sum(energy, axis=-1), "freq")
    all_bins = bin_count * lax.axis_size("freq")
    mean_power = power_sums / all_bins
    factor = live_mask.astype(jnp.float32)[:, :, None] / jnp.sqrt(
        energy + mean_power[:, :, None] + 1e-06
    )
    whitened = jnp.concatenate([real_in * factor, imag_in * factor], axis=-1).astype(jnp.bfloat16)
    block_count = lax.axis_size("blk")
    offsets = block_count // 2 + 1
    own_block = lax.axis_index("blk")
    lag_basis = lag_table(lax.axis_index("freq") * bin_count, bin_count).reshape(
        2 * bin_count, NLAG
    )
    lag_basis = jnp.tile(lag_basis, (windows, 1))
    pair_lists = pair_rows[own_block]
    win_count = lax.axis_size("win")
    freq_count = lax.axis_size("freq")
    row_count = pair_rows.shape[-1]
    slice_rows = row_count // (win_count * freq_count)
    source_flat = whitened.reshape(channels, windows * 2 * bin_count)
    current = whitened
    reduced = []
    for offset in range(offsets):
        if offset > 0:
            current = shifted(current, "blk", -1)
        partner_flat = current.reshape(channels, windows * 2 * bin_count)
        source_rows = jnp.take(source_flat, pair_lists[offset, 0], axis=0)
        partner_rows = jnp.take(partner_flat, pair_lists[offset, 1], axis=0)
        source_rows = source_rows.reshape(row_count, windows, 2 * bin_count)
        partner_rows = partner_rows.reshape(row_count, windows, 2 * bin_count)
        source_real = source_rows[..., :bin_count].astype(jnp.float32)
        source_imag = source_rows[..., bin_count:].astype(jnp.float32)
        partner_real = partner_rows[..., :bin_count].astype(jnp.float32)
        partner_imag = partner_rows[..., bin_count:].astype(jnp.float32)
        cross_real = source_real * partner_real + source_imag * partner_imag
        cross_imag = source_imag * partner_real - source_real * partner_imag
        cross = jnp.concatenate([cross_real, cross_imag], axis=-1).astype(jnp.bfloat16)
        cross = cross.reshape(row_count, windows * 2 * bin_count)
        correlated = jnp.dot(cross, lag_basis, preferred_element_type=jnp.float32)
        correlated = correlated.reshape(win_count, freq_count, slice_rows, NLAG)
        correlated = correlated.transpose(1, 0, 2, 3).reshape(row_count, NLAG)
        partial = half_reduce(correlated, "freq")
        reduced.append(half_reduce(partial, "win"))
    summed = jnp.stack(reduced, axis=1)
    all_windows = windows * win_count
    stacked = (summed / math.sqrt(all_bins * all_windows)).astype(jnp.bfloat16)
    own_owners = owner_map[own_block]
    selector = (own_owners[None, :] == jnp.arange(block_count, dtype=jnp.int32)[:, None]).astype(
        jnp.bfloat16
    )
    send_buffer = jnp.einsum(
        "ok,pkl->opl", selector, stacked, preferred_element_type=jnp.float32
    ).astype(jnp.bfloat16)
    received = lax.all_to_all(send_buffer, "blk", split_axis=0, concat_axis=0, tiled=True)
    return received[None]


def solution(mesh):
    return jax.shard_map(
        body,
        mesh=mesh,
        in_specs=(
            P(("grp", "blk"), "win", None, "freq"),
            P(("grp", "blk"), "win"),
            P("grp", None, None, None),
            P("grp", None),
        ),
        out_specs=P(("grp", "blk"), None, ("win", "freq"), None),
        check_vma=False,
    )
```

```python
import math

import jax
import jax.numpy as jnp
from jax import lax
from jax.sharding import PartitionSpec as P

NLAG = 512
SAMPLES = 12000
LAG_STRIDE = 3


def shifted(value, axis, steps):
    count = lax.axis_size(axis)
    pairs = [(source, (source + steps) % count) for source in range(count)]
    return lax.ppermute(value, axis, pairs)


def pair_sum(value, axis):
    if lax.axis_size(axis) == 2:
        return value + shifted(value, axis, 1)
    return lax.psum(value, axis)


def half_reduce(value, axis):
    count = lax.axis_size(axis)
    if count == 2:
        index = lax.axis_index(axis)
        halves = value.reshape((2, value.shape[0] // 2) + value.shape[1:])
        keep = lax.dynamic_index_in_dim(halves, index, 0, keepdims=False)
        send = lax.dynamic_index_in_dim(halves, 1 - index, 0, keepdims=False)
        return keep + shifted(send, axis, 1)
    return lax.psum_scatter(value, axis, scatter_dimension=0, tiled=True)


def lag_table(first_bin, bin_count):
    bin_numbers = first_bin + jnp.arange(bin_count, dtype=jnp.int32)
    lag_numbers = (jnp.arange(NLAG, dtype=jnp.int32) - NLAG // 2) * LAG_STRIDE
    phase_index = (
        (bin_numbers[:, None] + 1) * ((lag_numbers[None, :] + SAMPLES) % SAMPLES) % SAMPLES
    )
    angles = phase_index.astype(jnp.float32) * (2.0 * math.pi / SAMPLES)
    return jnp.stack([jnp.cos(angles), -jnp.sin(angles)]).astype(jnp.bfloat16)


def body(spectra, live_mask, pair_rows, owner_map):
    channels, windows, _, bin_count = spectra.shape
    real_in = spectra[:, :, 0].astype(jnp.float32)
    imag_in = spectra[:, :, 1].astype(jnp.float32)
    energy = real_in * real_in + imag_in * imag_in
    power_sums = pair_sum(jnp.sum(energy, axis=-1), "freq")
    all_bins = bin_count * lax.axis_size("freq")
    mean_power = power_sums / all_bins
    factor = live_mask.astype(jnp.float32)[:, :, None] / jnp.sqrt(
        energy + mean_power[:, :, None] + 1e-06
    )
    whitened = jnp.concatenate([real_in * factor, imag_in * factor], axis=-1).astype(jnp.bfloat16)
    block_count = lax.axis_size("blk")
    offsets = block_count // 2 + 1
    own_block = lax.axis_index("blk")
    first_bin, whitened = lax.optimization_barrier((lax.axis_index("freq") * bin_count, whitened))
    next_block = shifted(whitened, "blk", -1) if offsets > 1 else whitened
    lag_basis = lag_table(first_bin, bin_count).reshape(
        2 * bin_count, NLAG
    )
    lag_basis = jnp.tile(lag_basis, (windows, 1))
    pair_lists = pair_rows[own_block]
    win_count = lax.axis_size("win")
    freq_count = lax.axis_size("freq")
    row_count = pair_rows.shape[-1]
    slice_rows = row_count // (win_count * freq_count)
    source_flat = whitened.reshape(channels, windows * 2 * bin_count)
    current = whitened
    reduced = []
    for offset in range(offsets):
        partner_flat = current.reshape(channels, windows * 2 * bin_count)
        source_rows = jnp.take(source_flat, pair_lists[offset, 0], axis=0)
        partner_rows = jnp.take(partner_flat, pair_lists[offset, 1], axis=0)
        source_rows = source_rows.reshape(row_count, windows, 2 * bin_count)
        partner_rows = partner_rows.reshape(row_count, windows, 2 * bin_count)
        source_real = source_rows[..., :bin_count].astype(jnp.float32)
        source_imag = source_rows[..., bin_count:].astype(jnp.float32)
        partner_real = partner_rows[..., :bin_count].astype(jnp.float32)
        partner_imag = partner_rows[..., bin_count:].astype(jnp.float32)
        cross_real = source_real * partner_real + source_imag * partner_imag
        cross_imag = source_imag * partner_real - source_real * partner_imag
        cross = jnp.concatenate([cross_real, cross_imag], axis=-1).astype(jnp.bfloat16)
        cross = cross.reshape(row_count, windows * 2 * bin_count)
        correlated = jnp.dot(cross, lag_basis, preferred_element_type=jnp.float32)
        correlated = correlated.reshape(win_count, freq_count, slice_rows, NLAG)
        correlated = correlated.transpose(1, 0, 2, 3).reshape(row_count, NLAG)
        if offset + 1 < offsets:
            correlated, current = lax.optimization_barrier((correlated, next_block))
            if offset + 2 < offsets:
                next_block = shifted(current, "blk", -1)
        partial = half_reduce(correlated, "freq")
        reduced.append(half_reduce(partial, "win"))
    summed = jnp.stack(reduced, axis=1)
    all_windows = windows * win_count
    stacked = (summed / math.sqrt(all_bins * all_windows)).astype(jnp.bfloat16)
    own_owners = owner_map[own_block]
    selector = (own_owners[None, :] == jnp.arange(block_count, dtype=jnp.int32)[:, None]).astype(
        jnp.bfloat16
    )
    send_buffer = jnp.einsum(
        "ok,pkl->opl", selector, stacked, preferred_element_type=jnp.float32
    ).astype(jnp.bfloat16)
    if block_count > 4:
        received = lax.all_to_all(send_buffer, "blk", split_axis=0, concat_axis=0, tiled=True)
        return received[None]
    parts = []
    for distance in range(block_count):
        source = (own_block - distance) % block_count
        chunk = lax.dynamic_index_in_dim(send_buffer, (own_block + distance) % block_count, 0)
        if distance > 0:
            chunk = shifted(chunk, "blk", distance)
        parts.append((source, chunk))
    received = jnp.zeros_like(send_buffer)
    for source, chunk in parts:
        received = lax.dynamic_update_index_in_dim(received, chunk[0], source, 0)
    return received[None]


def solution(mesh):
    return jax.shard_map(
        body,
        mesh=mesh,
        in_specs=(
            P(("grp", "blk"), "win", None, "freq"),
            P(("grp", "blk"), "win"),
            P("grp", None, None, None),
            P("grp", None),
        ),
        out_specs=P(("grp", "blk"), None, ("win", "freq"), None),
        check_vma=False,
    )
```

```python
import math

import jax
import jax.numpy as jnp
from jax import lax
from jax.sharding import PartitionSpec as P

NLAG = 512
SAMPLES = 12000
LAG_STRIDE = 3


def shifted(value, axis, steps):
    count = lax.axis_size(axis)
    pairs = [(source, (source + steps) % count) for source in range(count)]
    return lax.ppermute(value, axis, pairs)


def pair_sum(value, axis):
    if lax.axis_size(axis) == 2:
        return value + shifted(value, axis, 1)
    return lax.psum(value, axis)


def half_reduce(value, axis):
    count = lax.axis_size(axis)
    if count == 2:
        index = lax.axis_index(axis)
        halves = value.reshape((2, value.shape[0] // 2) + value.shape[1:])
        keep = lax.dynamic_index_in_dim(halves, index, 0, keepdims=False)
        send = lax.dynamic_index_in_dim(halves, 1 - index, 0, keepdims=False)
        return keep + shifted(send, axis, 1)
    return lax.psum_scatter(value, axis, scatter_dimension=0, tiled=True)


def lag_table(first_bin, bin_count):
    lag_numbers = (jnp.arange(NLAG, dtype=jnp.int32) - NLAG // 2) * LAG_STRIDE
    lag_steps = (lag_numbers + SAMPLES) % SAMPLES
    split = 32 if bin_count % 32 == 0 else 1
    fine_bins = first_bin + 1 + jnp.arange(split, dtype=jnp.int32)
    coarse_bins = jnp.arange(bin_count // split, dtype=jnp.int32) * split
    scale = 2.0 * math.pi / SAMPLES
    fine = (fine_bins[:, None] * lag_steps[None, :]) % SAMPLES
    coarse = (coarse_bins[:, None] * lag_steps[None, :]) % SAMPLES
    fine_angle = fine.astype(jnp.float32) * scale
    coarse_angle = coarse.astype(jnp.float32) * scale
    fine_cos, fine_sin = jnp.cos(fine_angle)[None], jnp.sin(fine_angle)[None]
    coarse_cos, coarse_sin = jnp.cos(coarse_angle)[:, None], jnp.sin(coarse_angle)[:, None]
    cosine = coarse_cos * fine_cos - coarse_sin * fine_sin
    sine = coarse_sin * fine_cos + coarse_cos * fine_sin
    table = jnp.stack([cosine, -sine]).reshape(2, bin_count, NLAG)
    return table.astype(jnp.bfloat16)


def select_rows(block, rows):
    channel_ids = jnp.arange(block.shape[0], dtype=rows.dtype)
    one_hot = (rows[:, None] == channel_ids[None, :]).astype(block.dtype)
    return jnp.dot(one_hot, block, preferred_element_type=jnp.float32)


def body(spectra, live_mask, pair_rows, owner_map):
    channels, windows, _, bin_count = spectra.shape
    real_in = spectra[:, :, 0].astype(jnp.float32)
    imag_in = spectra[:, :, 1].astype(jnp.float32)
    energy = real_in * real_in + imag_in * imag_in
    power_sums = pair_sum(jnp.sum(energy, axis=-1), "freq")
    all_bins = bin_count * lax.axis_size("freq")
    mean_power = power_sums / all_bins
    factor = live_mask.astype(jnp.float32)[:, :, None] / jnp.sqrt(
        energy + mean_power[:, :, None] + 1e-06
    )
    whitened = jnp.concatenate([real_in * factor, imag_in * factor], axis=-1).astype(jnp.bfloat16)
    block_count = lax.axis_size("blk")
    offsets = block_count // 2 + 1
    own_block = lax.axis_index("blk")
    first_bin, whitened = lax.optimization_barrier((lax.axis_index("freq") * bin_count, whitened))
    next_block = shifted(whitened, "blk", -1) if offsets > 1 else whitened
    lag_basis = lag_table(first_bin, bin_count).reshape(
        2 * bin_count, NLAG
    )
    lag_basis = jnp.tile(lag_basis, (windows, 1))
    pair_lists = pair_rows[own_block]
    win_count = lax.axis_size("win")
    freq_count = lax.axis_size("freq")
    row_count = pair_rows.shape[-1]
    slice_rows = row_count // (win_count * freq_count)
    source_flat = whitened.reshape(channels, windows * 2 * bin_count)
    current = whitened
    reduced = []
    for offset in range(offsets):
        partner_flat = current.reshape(channels, windows * 2 * bin_count)
        source_rows = select_rows(source_flat, pair_lists[offset, 0])
        partner_rows = select_rows(partner_flat, pair_lists[offset, 1])
        source_rows = source_rows.reshape(row_count, windows, 2 * bin_count)
        partner_rows = partner_rows.reshape(row_count, windows, 2 * bin_count)
        source_real = source_rows[..., :bin_count]
        source_imag = source_rows[..., bin_count:]
        partner_real = partner_rows[..., :bin_count]
        partner_imag = partner_rows[..., bin_count:]
        cross_real = source_real * partner_real + source_imag * partner_imag
        cross_imag = source_imag * partner_real - source_real * partner_imag
        cross = jnp.concatenate([cross_real, cross_imag], axis=-1).astype(jnp.bfloat16)
        cross = cross.reshape(row_count, windows * 2 * bin_count)
        correlated = jnp.dot(cross, lag_basis, preferred_element_type=jnp.float32)
        correlated = correlated.reshape(win_count, freq_count, slice_rows, NLAG)
        correlated = correlated.transpose(1, 0, 2, 3).reshape(row_count, NLAG)
        if offset + 1 < offsets:
            correlated, current = lax.optimization_barrier((correlated, next_block))
            if offset + 2 < offsets:
                next_block = shifted(current, "blk", -1)
        partial = half_reduce(correlated, "freq")
        reduced.append(half_reduce(partial, "win"))
    summed = jnp.stack(reduced, axis=1)
    all_windows = windows * win_count
    stacked = (summed / math.sqrt(all_bins * all_windows)).astype(jnp.bfloat16)
    own_owners = owner_map[own_block]
    selector = (own_owners[None, :] == jnp.arange(block_count, dtype=jnp.int32)[:, None]).astype(
        jnp.bfloat16
    )
    send_buffer = jnp.einsum(
        "ok,pkl->opl", selector, stacked, preferred_element_type=jnp.float32
    ).astype(jnp.bfloat16)
    if block_count > 4:
        received = lax.all_to_all(send_buffer, "blk", split_axis=0, concat_axis=0, tiled=True)
        return received[None]
    parts = []
    for distance in range(block_count):
        source = (own_block - distance) % block_count
        chunk = lax.dynamic_index_in_dim(send_buffer, (own_block + distance) % block_count, 0)
        if distance > 0:
            chunk = shifted(chunk, "blk", distance)
        parts.append((source, chunk))
    received = jnp.zeros_like(send_buffer)
    for source, chunk in parts:
        received = lax.dynamic_update_index_in_dim(received, chunk[0], source, 0)
    return received[None]


def solution(mesh):
    return jax.shard_map(
        body,
        mesh=mesh,
        in_specs=(
            P(("grp", "blk"), "win", None, "freq"),
            P(("grp", "blk"), "win"),
            P("grp", None, None, None),
            P("grp", None),
        ),
        out_specs=P(("grp", "blk"), None, ("win", "freq"), None),
        check_vma=False,
    )
```

```python
import math

import jax
import jax.numpy as jnp
from jax import lax
from jax.sharding import PartitionSpec as P

NLAG = 512
SAMPLES = 12000
LAG_STRIDE = 3


def shifted(value, axis, steps):
    count = lax.axis_size(axis)
    pairs = [(source, (source + steps) % count) for source in range(count)]
    return lax.ppermute(value, axis, pairs)


def pair_sum(value, axis):
    if lax.axis_size(axis) == 2:
        return value + shifted(value, axis, 1)
    return lax.psum(value, axis)


def half_reduce(value, axis):
    count = lax.axis_size(axis)
    if count == 2:
        index = lax.axis_index(axis)
        halves = value.reshape((2, value.shape[0] // 2) + value.shape[1:])
        keep = lax.dynamic_index_in_dim(halves, index, 0, keepdims=False)
        send = lax.dynamic_index_in_dim(halves, 1 - index, 0, keepdims=False)
        return keep + shifted(send, axis, 1)
    return lax.psum_scatter(value, axis, scatter_dimension=0, tiled=True)


def slot_reduce(value):
    if lax.axis_size("win") != 2 or lax.axis_size("freq") != 2:
        return half_reduce(half_reduce(value, "freq"), "win")
    axes = ("win", "freq")
    own = lax.axis_index("win") * 2 + lax.axis_index("freq")
    slots = value.reshape((4, value.shape[0] // 4) + value.shape[1:])
    total = lax.dynamic_index_in_dim(slots, own, 0, keepdims=False)
    for mask in (1, 2, 3):
        send = lax.dynamic_index_in_dim(slots, own ^ mask, 0, keepdims=False)
        pairs = [(source, source ^ mask) for source in range(4)]
        total = total + lax.ppermute(send, axes, pairs)
    return total


def lag_table(first_bin, bin_count):
    lag_numbers = (jnp.arange(NLAG, dtype=jnp.int32) - NLAG // 2) * LAG_STRIDE
    lag_steps = (lag_numbers + SAMPLES) % SAMPLES
    split = 32 if bin_count % 32 == 0 else 1
    fine_bins = first_bin + 1 + jnp.arange(split, dtype=jnp.int32)
    coarse_bins = jnp.arange(bin_count // split, dtype=jnp.int32) * split
    scale = 2.0 * math.pi / SAMPLES
    fine = (fine_bins[:, None] * lag_steps[None, :]) % SAMPLES
    coarse = (coarse_bins[:, None] * lag_steps[None, :]) % SAMPLES
    fine_angle = fine.astype(jnp.float32) * scale
    coarse_angle = coarse.astype(jnp.float32) * scale
    fine_cos, fine_sin = jnp.cos(fine_angle)[None], jnp.sin(fine_angle)[None]
    coarse_cos, coarse_sin = jnp.cos(coarse_angle)[:, None], jnp.sin(coarse_angle)[:, None]
    cosine = coarse_cos * fine_cos - coarse_sin * fine_sin
    sine = coarse_sin * fine_cos + coarse_cos * fine_sin
    table = jnp.stack([cosine, -sine]).reshape(2, bin_count, NLAG)
    return table.astype(jnp.bfloat16)


def select_rows(block, rows):
    channel_ids = jnp.arange(block.shape[0], dtype=rows.dtype)
    one_hot = (rows[:, None] == channel_ids[None, :]).astype(block.dtype)
    return jnp.dot(one_hot, block, preferred_element_type=jnp.float32)


def whiten(raw, scales):
    real_in = raw[:, :, 0].astype(jnp.float32)
    imag_in = raw[:, :, 1].astype(jnp.float32)
    energy = real_in * real_in + imag_in * imag_in
    factor = scales[:, :, 1:2] / jnp.sqrt(energy + scales[:, :, 0:1] + 1e-06)
    whitened = jnp.concatenate([real_in * factor, imag_in * factor], axis=-1)
    return whitened.astype(jnp.bfloat16)


def body(spectra, live_mask, pair_rows, owner_map):
    channels, windows, _, bin_count = spectra.shape
    block_count = lax.axis_size("blk")
    offsets = block_count // 2 + 1
    own_block = lax.axis_index("blk")
    next_raw = shifted(spectra, "blk", -1) if offsets > 1 else spectra
    real_in = spectra[:, :, 0].astype(jnp.float32)
    imag_in = spectra[:, :, 1].astype(jnp.float32)
    energy = real_in * real_in + imag_in * imag_in
    power_sums = pair_sum(jnp.sum(energy, axis=-1), "freq")
    all_bins = bin_count * lax.axis_size("freq")
    mean_power = power_sums / all_bins
    scales = jnp.stack([mean_power, live_mask.astype(jnp.float32)], axis=-1)
    next_scales = shifted(scales, "blk", -1) if offsets > 1 else scales
    whitened = whiten(spectra, scales)
    first_bin, whitened = lax.optimization_barrier((lax.axis_index("freq") * bin_count, whitened))
    lag_basis = lag_table(first_bin, bin_count).reshape(2 * bin_count, NLAG)
    lag_basis = jnp.tile(lag_basis, (windows, 1))
    pair_lists = pair_rows[own_block]
    win_count = lax.axis_size("win")
    freq_count = lax.axis_size("freq")
    row_count = pair_rows.shape[-1]
    source_flat = whitened.reshape(channels, windows * 2 * bin_count)
    current = whitened
    reduced = []
    for offset in range(offsets):
        partner_flat = current.reshape(channels, windows * 2 * bin_count)
        source_rows = select_rows(source_flat, pair_lists[offset, 0])
        partner_rows = select_rows(partner_flat, pair_lists[offset, 1])
        source_rows = source_rows.reshape(row_count, windows, 2 * bin_count)
        partner_rows = partner_rows.reshape(row_count, windows, 2 * bin_count)
        source_real = source_rows[..., :bin_count]
        source_imag = source_rows[..., bin_count:]
        partner_real = partner_rows[..., :bin_count]
        partner_imag = partner_rows[..., bin_count:]
        cross_real = source_real * partner_real + source_imag * partner_imag
        cross_imag = source_imag * partner_real - source_real * partner_imag
        cross = jnp.concatenate([cross_real, cross_imag], axis=-1).astype(jnp.bfloat16)
        cross = cross.reshape(row_count, windows * 2 * bin_count)
        correlated = jnp.dot(cross, lag_basis, preferred_element_type=jnp.float32)
        if offset + 1 < offsets:
            correlated, raw_block, block_scales = lax.optimization_barrier(
                (correlated, next_raw, next_scales)
            )
            if offset + 2 < offsets:
                next_raw = shifted(raw_block, "blk", -1)
                next_scales = shifted(block_scales, "blk", -1)
            current = whiten(raw_block, block_scales)
        reduced.append(slot_reduce(correlated))
    summed = jnp.stack(reduced, axis=1)
    all_windows = windows * win_count
    stacked = (summed / math.sqrt(all_bins * all_windows)).astype(jnp.bfloat16)
    own_owners = owner_map[own_block]
    selector = (own_owners[None, :] == jnp.arange(block_count, dtype=jnp.int32)[:, None]).astype(
        jnp.bfloat16
    )
    send_buffer = jnp.einsum(
        "ok,pkl->opl", selector, stacked, preferred_element_type=jnp.float32
    ).astype(jnp.bfloat16)
    if block_count > 4:
        received = lax.all_to_all(send_buffer, "blk", split_axis=0, concat_axis=0, tiled=True)
        return received[None]
    parts = []
    for distance in range(block_count):
        source = (own_block - distance) % block_count
        chunk = lax.dynamic_index_in_dim(send_buffer, (own_block + distance) % block_count, 0)
        if distance > 0:
            chunk = shifted(chunk, "blk", distance)
        parts.append((source, chunk))
    received = jnp.zeros_like(send_buffer)
    for source, chunk in parts:
        received = lax.dynamic_update_index_in_dim(received, chunk[0], source, 0)
    return received[None]


def solution(mesh):
    return jax.shard_map(
        body,
        mesh=mesh,
        in_specs=(
            P(("grp", "blk"), "win", None, "freq"),
            P(("grp", "blk"), "win"),
            P("grp", None, None, None),
            P("grp", None),
        ),
        out_specs=P(("grp", "blk"), None, ("win", "freq"), None),
        check_vma=False,
    )
```

```python
import math

import jax
import jax.numpy as jnp
from jax import lax
from jax.sharding import PartitionSpec as P

NLAG = 512
SAMPLES = 12000
LAG_STRIDE = 3


def shifted(value, axis, steps):
    count = lax.axis_size(axis)
    pairs = [(source, (source + steps) % count) for source in range(count)]
    return lax.ppermute(value, axis, pairs)


def pair_sum(value, axis):
    if lax.axis_size(axis) == 2:
        return value + shifted(value, axis, 1)
    return lax.psum(value, axis)


def half_reduce(value, axis):
    count = lax.axis_size(axis)
    if count == 2:
        index = lax.axis_index(axis)
        halves = value.reshape((2, value.shape[0] // 2) + value.shape[1:])
        keep = lax.dynamic_index_in_dim(halves, index, 0, keepdims=False)
        send = lax.dynamic_index_in_dim(halves, 1 - index, 0, keepdims=False)
        return keep + shifted(send, axis, 1)
    return lax.psum_scatter(value, axis, scatter_dimension=0, tiled=True)


def slot_reduce(value):
    if lax.axis_size("win") != 2 or lax.axis_size("freq") != 2:
        return half_reduce(half_reduce(value, "freq"), "win")
    axes = ("win", "freq")
    own = lax.axis_index("win") * 2 + lax.axis_index("freq")
    slots = value.reshape((4, value.shape[0] // 4) + value.shape[1:])
    total = lax.dynamic_index_in_dim(slots, own, 0, keepdims=False)
    for mask in (1, 2, 3):
        send = lax.dynamic_index_in_dim(slots, own ^ mask, 0, keepdims=False)
        pairs = [(source, source ^ mask) for source in range(4)]
        total = total + lax.ppermute(send, axes, pairs)
    return total


def lag_table(first_bin, bin_count):
    lag_numbers = (jnp.arange(NLAG, dtype=jnp.int32) - NLAG // 2) * LAG_STRIDE
    lag_steps = (lag_numbers + SAMPLES) % SAMPLES
    split = 32 if bin_count % 32 == 0 else 1
    fine_bins = first_bin + 1 + jnp.arange(split, dtype=jnp.int32)
    coarse_bins = jnp.arange(bin_count // split, dtype=jnp.int32) * split
    scale = 2.0 * math.pi / SAMPLES
    fine = (fine_bins[:, None] * lag_steps[None, :]) % SAMPLES
    coarse = (coarse_bins[:, None] * lag_steps[None, :]) % SAMPLES
    fine_angle = fine.astype(jnp.float32) * scale
    coarse_angle = coarse.astype(jnp.float32) * scale
    fine_cos, fine_sin = jnp.cos(fine_angle)[None], jnp.sin(fine_angle)[None]
    coarse_cos, coarse_sin = jnp.cos(coarse_angle)[:, None], jnp.sin(coarse_angle)[:, None]
    cosine = coarse_cos * fine_cos - coarse_sin * fine_sin
    sine = coarse_sin * fine_cos + coarse_cos * fine_sin
    table = jnp.stack([cosine, -sine]).reshape(2, bin_count, NLAG)
    return table.astype(jnp.bfloat16)


def select_rows(block, rows):
    channel_ids = jnp.arange(block.shape[0], dtype=rows.dtype)
    one_hot = (rows[:, None] == channel_ids[None, :]).astype(block.dtype)
    return jnp.dot(one_hot, block, preferred_element_type=jnp.float32)


def whiten(raw, scales):
    real_in = raw[:, :, 0].astype(jnp.float32)
    imag_in = raw[:, :, 1].astype(jnp.float32)
    energy = real_in * real_in + imag_in * imag_in
    factor = scales[:, :, 1:2] / jnp.sqrt(energy + scales[:, :, 0:1] + 1e-06)
    whitened = jnp.concatenate([real_in * factor, imag_in * factor], axis=-1)
    return whitened.astype(jnp.bfloat16)


def body(spectra, live_mask, pair_rows, owner_map):
    channels, windows, _, bin_count = spectra.shape
    block_count = lax.axis_size("blk")
    offsets = block_count // 2 + 1
    own_block = lax.axis_index("blk")
    next_raw = shifted(spectra, "blk", -1) if offsets > 1 else spectra
    real_in = spectra[:, :, 0].astype(jnp.float32)
    imag_in = spectra[:, :, 1].astype(jnp.float32)
    energy = real_in * real_in + imag_in * imag_in
    power_sums = pair_sum(jnp.sum(energy, axis=-1), "freq")
    all_bins = bin_count * lax.axis_size("freq")
    mean_power = power_sums / all_bins
    scales = jnp.stack([mean_power, live_mask.astype(jnp.float32)], axis=-1)
    scale_pool = [scales] + [shifted(scales, "blk", -step) for step in range(1, offsets)]
    whitened = whiten(spectra, scales)
    first_bin, whitened = lax.optimization_barrier((lax.axis_index("freq") * bin_count, whitened))
    lag_basis = lag_table(first_bin, bin_count).reshape(2 * bin_count, NLAG)
    lag_basis = jnp.tile(lag_basis, (windows, 1))
    pair_lists = pair_rows[own_block]
    win_count = lax.axis_size("win")
    freq_count = lax.axis_size("freq")
    row_count = pair_rows.shape[-1]
    source_flat = whitened.reshape(channels, windows * 2 * bin_count)
    current = whitened
    reduced = []
    for offset in range(offsets):
        partner_flat = current.reshape(channels, windows * 2 * bin_count)
        source_rows = select_rows(source_flat, pair_lists[offset, 0])
        partner_rows = select_rows(partner_flat, pair_lists[offset, 1])
        source_rows = source_rows.reshape(row_count, windows, 2 * bin_count)
        partner_rows = partner_rows.reshape(row_count, windows, 2 * bin_count)
        source_real = source_rows[..., :bin_count]
        source_imag = source_rows[..., bin_count:]
        partner_real = partner_rows[..., :bin_count]
        partner_imag = partner_rows[..., bin_count:]
        cross_real = source_real * partner_real + source_imag * partner_imag
        cross_imag = source_imag * partner_real - source_real * partner_imag
        cross = jnp.concatenate([cross_real, cross_imag], axis=-1).astype(jnp.bfloat16)
        cross = cross.reshape(row_count, windows * 2 * bin_count)
        correlated = jnp.dot(cross, lag_basis, preferred_element_type=jnp.float32)
        result = slot_reduce(correlated)
        if offset + 1 < offsets:
            result, raw_block = lax.optimization_barrier((result, next_raw))
            if offset + 2 < offsets:
                next_raw = shifted(raw_block, "blk", -1)
            current = whiten(raw_block, scale_pool[offset + 1])
        reduced.append(result)
    summed = jnp.stack(reduced, axis=1)
    all_windows = windows * win_count
    stacked = (summed / math.sqrt(all_bins * all_windows)).astype(jnp.bfloat16)
    own_owners = owner_map[own_block]
    selector = (own_owners[None, :] == jnp.arange(block_count, dtype=jnp.int32)[:, None]).astype(
        jnp.bfloat16
    )
    send_buffer = jnp.einsum(
        "ok,pkl->opl", selector, stacked, preferred_element_type=jnp.float32
    ).astype(jnp.bfloat16)
    if block_count > 4:
        received = lax.all_to_all(send_buffer, "blk", split_axis=0, concat_axis=0, tiled=True)
        return received[None]
    parts = []
    for distance in range(block_count):
        source = (own_block - distance) % block_count
        chunk = lax.dynamic_index_in_dim(send_buffer, (own_block + distance) % block_count, 0)
        if distance > 0:
            chunk = shifted(chunk, "blk", distance)
        parts.append((source, chunk))
    received = jnp.zeros_like(send_buffer)
    for source, chunk in parts:
        received = lax.dynamic_update_index_in_dim(received, chunk[0], source, 0)
    return received[None]


def solution(mesh):
    return jax.shard_map(
        body,
        mesh=mesh,
        in_specs=(
            P(("grp", "blk"), "win", None, "freq"),
            P(("grp", "blk"), "win"),
            P("grp", None, None, None),
            P("grp", None),
        ),
        out_specs=P(("grp", "blk"), None, ("win", "freq"), None),
        check_vma=False,
    )
```

```python
import math

import jax
import jax.numpy as jnp
from jax import lax
from jax.sharding import PartitionSpec as P

NLAG = 512
SAMPLES = 12000
LAG_STRIDE = 3


def shifted(value, axis, steps):
    count = lax.axis_size(axis)
    pairs = [(source, (source + steps) % count) for source in range(count)]
    return lax.ppermute(value, axis, pairs)


def pair_sum(value, axis):
    if lax.axis_size(axis) == 2:
        return value + shifted(value, axis, 1)
    return lax.psum(value, axis)


def half_reduce(value, axis):
    count = lax.axis_size(axis)
    if count == 2:
        index = lax.axis_index(axis)
        halves = value.reshape((2, value.shape[0] // 2) + value.shape[1:])
        keep = lax.dynamic_index_in_dim(halves, index, 0, keepdims=False)
        send = lax.dynamic_index_in_dim(halves, 1 - index, 0, keepdims=False)
        return keep + shifted(send, axis, 1)
    return lax.psum_scatter(value, axis, scatter_dimension=0, tiled=True)


def slot_reduce(value):
    if lax.axis_size("win") != 2 or lax.axis_size("freq") != 2:
        return half_reduce(half_reduce(value, "freq"), "win")
    axes = ("win", "freq")
    own = lax.axis_index("win") * 2 + lax.axis_index("freq")
    slots = value.reshape((4, value.shape[0] // 4) + value.shape[1:])
    total = lax.dynamic_index_in_dim(slots, own, 0, keepdims=False)
    for mask in (1, 2, 3):
        send = lax.dynamic_index_in_dim(slots, own ^ mask, 0, keepdims=False)
        pairs = [(source, source ^ mask) for source in range(4)]
        total = total + lax.ppermute(send, axes, pairs)
    return total


def lag_table(first_bin, bin_count):
    lag_numbers = (jnp.arange(NLAG, dtype=jnp.int32) - NLAG // 2) * LAG_STRIDE
    lag_steps = (lag_numbers + SAMPLES) % SAMPLES
    split = 32 if bin_count % 32 == 0 else 1
    fine_bins = first_bin + 1 + jnp.arange(split, dtype=jnp.int32)
    coarse_bins = jnp.arange(bin_count // split, dtype=jnp.int32) * split
    scale = 2.0 * math.pi / SAMPLES
    fine = (fine_bins[:, None] * lag_steps[None, :]) % SAMPLES
    coarse = (coarse_bins[:, None] * lag_steps[None, :]) % SAMPLES
    fine_angle = fine.astype(jnp.float32) * scale
    coarse_angle = coarse.astype(jnp.float32) * scale
    fine_cos, fine_sin = jnp.cos(fine_angle)[None], jnp.sin(fine_angle)[None]
    coarse_cos, coarse_sin = jnp.cos(coarse_angle)[:, None], jnp.sin(coarse_angle)[:, None]
    cosine = coarse_cos * fine_cos - coarse_sin * fine_sin
    sine = coarse_sin * fine_cos + coarse_cos * fine_sin
    table = jnp.stack([cosine, -sine]).reshape(2, bin_count, NLAG)
    return table.astype(jnp.bfloat16)


def select_rows(block, rows):
    channel_ids = jnp.arange(block.shape[0], dtype=rows.dtype)
    one_hot = (rows[:, None] == channel_ids[None, :]).astype(block.dtype)
    return jnp.dot(one_hot, block, preferred_element_type=jnp.float32)


def whiten(raw, scales):
    real_in = raw[:, :, 0].astype(jnp.float32)
    imag_in = raw[:, :, 1].astype(jnp.float32)
    energy = real_in * real_in + imag_in * imag_in
    factor = scales[:, :, 1:2] / jnp.sqrt(energy + scales[:, :, 0:1] + 1e-06)
    whitened = jnp.concatenate([real_in * factor, imag_in * factor], axis=-1)
    return whitened.astype(jnp.bfloat16)


def body(spectra, live_mask, pair_rows, owner_map):
    channels, windows, _, bin_count = spectra.shape
    block_count = lax.axis_size("blk")
    offsets = block_count // 2 + 1
    own_block = lax.axis_index("blk")
    next_raw = shifted(spectra, "blk", -1) if offsets > 1 else spectra
    real_in = spectra[:, :, 0].astype(jnp.float32)
    imag_in = spectra[:, :, 1].astype(jnp.float32)
    energy = real_in * real_in + imag_in * imag_in
    power_sums = pair_sum(jnp.sum(energy, axis=-1), "freq")
    all_bins = bin_count * lax.axis_size("freq")
    mean_power = power_sums / all_bins
    scales = jnp.stack([mean_power, live_mask.astype(jnp.float32)], axis=-1)
    scale_pool = [scales] + [shifted(scales, "blk", -step) for step in range(1, offsets)]
    whitened = whiten(spectra, scales)
    first_bin, whitened = lax.optimization_barrier((lax.axis_index("freq") * bin_count, whitened))
    lag_basis = lag_table(first_bin, bin_count).reshape(2 * bin_count, NLAG)
    lag_basis = jnp.tile(lag_basis, (windows, 1))
    pair_lists = pair_rows[own_block]
    win_count = lax.axis_size("win")
    freq_count = lax.axis_size("freq")
    row_count = pair_rows.shape[-1]
    source_flat = whitened.reshape(channels, windows * 2 * bin_count)
    current = whitened
    reduced = []
    for offset in range(offsets):
        partner_flat = current.reshape(channels, windows * 2 * bin_count)
        source_rows = select_rows(source_flat, pair_lists[offset, 0])
        partner_rows = select_rows(partner_flat, pair_lists[offset, 1])
        source_rows = source_rows.reshape(row_count, windows, 2 * bin_count)
        partner_rows = partner_rows.reshape(row_count, windows, 2 * bin_count)
        source_real = source_rows[..., :bin_count]
        source_imag = source_rows[..., bin_count:]
        partner_real = partner_rows[..., :bin_count]
        partner_imag = partner_rows[..., bin_count:]
        cross_real = source_real * partner_real + source_imag * partner_imag
        cross_imag = source_imag * partner_real - source_real * partner_imag
        cross = jnp.concatenate([cross_real, cross_imag], axis=-1).astype(jnp.bfloat16)
        cross = cross.reshape(row_count, windows * 2 * bin_count)
        correlated = jnp.dot(cross, lag_basis, preferred_element_type=jnp.float32)
        if offset + 1 < offsets:
            correlated, raw_block = lax.optimization_barrier((correlated, next_raw))
            if offset + 2 < offsets:
                next_raw = shifted(raw_block, "blk", -1)
            current = whiten(raw_block, scale_pool[offset + 1])
            correlated, current = lax.optimization_barrier((correlated, current))
        reduced.append(slot_reduce(correlated))
    summed = jnp.stack(reduced, axis=1)
    all_windows = windows * win_count
    stacked = (summed / math.sqrt(all_bins * all_windows)).astype(jnp.bfloat16)
    own_owners = owner_map[own_block]
    selector = (own_owners[None, :] == jnp.arange(block_count, dtype=jnp.int32)[:, None]).astype(
        jnp.bfloat16
    )
    send_buffer = jnp.einsum(
        "ok,pkl->opl", selector, stacked, preferred_element_type=jnp.float32
    ).astype(jnp.bfloat16)
    if block_count > 4:
        received = lax.all_to_all(send_buffer, "blk", split_axis=0, concat_axis=0, tiled=True)
        return received[None]
    parts = []
    for distance in range(block_count):
        source = (own_block - distance) % block_count
        chunk = lax.dynamic_index_in_dim(send_buffer, (own_block + distance) % block_count, 0)
        if distance > 0:
            chunk = shifted(chunk, "blk", distance)
        parts.append((source, chunk))
    received = jnp.zeros_like(send_buffer)
    for source, chunk in parts:
        received = lax.dynamic_update_index_in_dim(received, chunk[0], source, 0)
    return received[None]


def solution(mesh):
    return jax.shard_map(
        body,
        mesh=mesh,
        in_specs=(
            P(("grp", "blk"), "win", None, "freq"),
            P(("grp", "blk"), "win"),
            P("grp", None, None, None),
            P("grp", None),
        ),
        out_specs=P(("grp", "blk"), None, ("win", "freq"), None),
        check_vma=False,
    )
```

```python
import math

import jax
import jax.numpy as jnp
from jax import lax
from jax.sharding import PartitionSpec as P

NLAG = 512
SAMPLES = 12000
LAG_STRIDE = 3


def shifted(value, axis, steps):
    count = lax.axis_size(axis)
    pairs = [(source, (source + steps) % count) for source in range(count)]
    return lax.ppermute(value, axis, pairs)


def pair_sum(value, axis):
    if lax.axis_size(axis) == 2:
        return value + shifted(value, axis, 1)
    return lax.psum(value, axis)


def half_reduce(value, axis):
    count = lax.axis_size(axis)
    if count == 2:
        index = lax.axis_index(axis)
        halves = value.reshape((2, value.shape[0] // 2) + value.shape[1:])
        keep = lax.dynamic_index_in_dim(halves, index, 0, keepdims=False)
        send = lax.dynamic_index_in_dim(halves, 1 - index, 0, keepdims=False)
        return keep + shifted(send, axis, 1)
    return lax.psum_scatter(value, axis, scatter_dimension=0, tiled=True)


def slot_reduce(value):
    if lax.axis_size("win") != 2 or lax.axis_size("freq") != 2:
        return half_reduce(half_reduce(value, "freq"), "win")
    axes = ("win", "freq")
    own = lax.axis_index("win") * 2 + lax.axis_index("freq")
    slots = value.reshape((4, value.shape[0] // 4) + value.shape[1:])
    total = lax.dynamic_index_in_dim(slots, own, 0, keepdims=False)
    for mask in (1, 2, 3):
        send = lax.dynamic_index_in_dim(slots, own ^ mask, 0, keepdims=False)
        pairs = [(source, source ^ mask) for source in range(4)]
        total = total + lax.ppermute(send, axes, pairs)
    return total


def lag_table(first_bin, bin_count):
    lag_numbers = (jnp.arange(NLAG, dtype=jnp.int32) - NLAG // 2) * LAG_STRIDE
    lag_steps = (lag_numbers + SAMPLES) % SAMPLES
    split = 32 if bin_count % 32 == 0 else 1
    fine_bins = first_bin + 1 + jnp.arange(split, dtype=jnp.int32)
    coarse_bins = jnp.arange(bin_count // split, dtype=jnp.int32) * split
    scale = 2.0 * math.pi / SAMPLES
    fine = (fine_bins[:, None] * lag_steps[None, :]) % SAMPLES
    coarse = (coarse_bins[:, None] * lag_steps[None, :]) % SAMPLES
    fine_angle = fine.astype(jnp.float32) * scale
    coarse_angle = coarse.astype(jnp.float32) * scale
    fine_cos, fine_sin = jnp.cos(fine_angle)[None], jnp.sin(fine_angle)[None]
    coarse_cos, coarse_sin = jnp.cos(coarse_angle)[:, None], jnp.sin(coarse_angle)[:, None]
    cosine = coarse_cos * fine_cos - coarse_sin * fine_sin
    sine = coarse_sin * fine_cos + coarse_cos * fine_sin
    table = jnp.stack([cosine, -sine]).reshape(2, bin_count, NLAG)
    return table.astype(jnp.bfloat16)


def select_rows(block, rows):
    channel_ids = jnp.arange(block.shape[0], dtype=rows.dtype)
    one_hot = (rows[:, None] == channel_ids[None, :]).astype(block.dtype)
    return jnp.dot(one_hot, block, preferred_element_type=jnp.float32)


def whiten(raw, scales):
    real_in = raw[:, :, 0].astype(jnp.float32)
    imag_in = raw[:, :, 1].astype(jnp.float32)
    energy = real_in * real_in + imag_in * imag_in
    factor = scales[:, :, 1:2] / jnp.sqrt(energy + scales[:, :, 0:1] + 1e-06)
    whitened = jnp.concatenate([real_in * factor, imag_in * factor], axis=-1)
    return whitened.astype(jnp.bfloat16)


def body(spectra, live_mask, pair_rows, owner_map):
    channels, windows, _, bin_count = spectra.shape
    block_count = lax.axis_size("blk")
    offsets = block_count // 2 + 1
    own_block = lax.axis_index("blk")
    next_raw = shifted(spectra, "blk", -1) if offsets > 1 else spectra
    real_in = spectra[:, :, 0].astype(jnp.float32)
    imag_in = spectra[:, :, 1].astype(jnp.float32)
    energy = real_in * real_in + imag_in * imag_in
    power_sums = pair_sum(jnp.sum(energy, axis=-1), "freq")
    all_bins = bin_count * lax.axis_size("freq")
    mean_power = power_sums / all_bins
    scales = jnp.stack([mean_power, live_mask.astype(jnp.float32)], axis=-1)
    scale_pool = [scales] + [shifted(scales, "blk", -step) for step in range(1, offsets)]
    whitened = whiten(spectra, scales)
    first_bin, whitened = lax.optimization_barrier((lax.axis_index("freq") * bin_count, whitened))
    lag_basis = lag_table(first_bin, bin_count).reshape(2 * bin_count, NLAG)
    lag_basis = jnp.tile(lag_basis, (windows, 1))
    pair_lists = pair_rows[own_block]
    win_count = lax.axis_size("win")
    freq_count = lax.axis_size("freq")
    row_count = pair_rows.shape[-1]
    source_flat = whitened.reshape(channels, windows * 2 * bin_count)
    current = whitened
    reduced = []
    for offset in range(offsets):
        partner_flat = current.reshape(channels, windows * 2 * bin_count)
        source_rows = select_rows(source_flat, pair_lists[offset, 0])
        partner_rows = select_rows(partner_flat, pair_lists[offset, 1])
        source_rows = source_rows.reshape(row_count, windows, 2 * bin_count)
        partner_rows = partner_rows.reshape(row_count, windows, 2 * bin_count)
        source_real = source_rows[..., :bin_count]
        source_imag = source_rows[..., bin_count:]
        partner_real = partner_rows[..., :bin_count]
        partner_imag = partner_rows[..., bin_count:]
        cross_real = source_real * partner_real + source_imag * partner_imag
        cross_imag = source_imag * partner_real - source_real * partner_imag
        cross = jnp.concatenate([cross_real, cross_imag], axis=-1).astype(jnp.bfloat16)
        cross = cross.reshape(row_count, windows * 2 * bin_count)
        correlated = jnp.dot(cross, lag_basis, preferred_element_type=jnp.float32)
        if offset + 2 < offsets:
            correlated, raw_block = lax.optimization_barrier((correlated, next_raw))
            next_raw = shifted(raw_block, "blk", -1)
            current = whiten(raw_block, scale_pool[offset + 1])
            correlated, current = lax.optimization_barrier((correlated, current))
        elif offset + 1 < offsets:
            current = whiten(next_raw, scale_pool[offset + 1])
        reduced.append(slot_reduce(correlated))
    summed = jnp.stack(reduced, axis=1)
    all_windows = windows * win_count
    stacked = (summed / math.sqrt(all_bins * all_windows)).astype(jnp.bfloat16)
    own_owners = owner_map[own_block]
    selector = (own_owners[None, :] == jnp.arange(block_count, dtype=jnp.int32)[:, None]).astype(
        jnp.bfloat16
    )
    send_buffer = jnp.einsum(
        "ok,pkl->opl", selector, stacked, preferred_element_type=jnp.float32
    ).astype(jnp.bfloat16)
    if block_count > 4:
        received = lax.all_to_all(send_buffer, "blk", split_axis=0, concat_axis=0, tiled=True)
        return received[None]
    parts = []
    for distance in range(block_count):
        source = (own_block - distance) % block_count
        chunk = lax.dynamic_index_in_dim(send_buffer, (own_block + distance) % block_count, 0)
        if distance > 0:
            chunk = shifted(chunk, "blk", distance)
        parts.append((source, chunk))
    received = jnp.zeros_like(send_buffer)
    for source, chunk in parts:
        received = lax.dynamic_update_index_in_dim(received, chunk[0], source, 0)
    return received[None]


def solution(mesh):
    return jax.shard_map(
        body,
        mesh=mesh,
        in_specs=(
            P(("grp", "blk"), "win", None, "freq"),
            P(("grp", "blk"), "win"),
            P("grp", None, None, None),
            P("grp", None),
        ),
        out_specs=P(("grp", "blk"), None, ("win", "freq"), None),
        check_vma=False,
    )
```

```python
import math

import jax
import jax.numpy as jnp
from jax import lax
from jax.sharding import PartitionSpec as P

NLAG = 512
SAMPLES = 12000
LAG_STRIDE = 3


def shifted(value, axis, steps):
    count = lax.axis_size(axis)
    pairs = [(source, (source + steps) % count) for source in range(count)]
    return lax.ppermute(value, axis, pairs)


def pair_sum(value, axis):
    if lax.axis_size(axis) == 2:
        return value + shifted(value, axis, 1)
    return lax.psum(value, axis)


def half_reduce(value, axis):
    count = lax.axis_size(axis)
    if count == 2:
        index = lax.axis_index(axis)
        halves = value.reshape((2, value.shape[0] // 2) + value.shape[1:])
        keep = lax.dynamic_index_in_dim(halves, index, 0, keepdims=False)
        send = lax.dynamic_index_in_dim(halves, 1 - index, 0, keepdims=False)
        return keep + shifted(send, axis, 1)
    return lax.psum_scatter(value, axis, scatter_dimension=0, tiled=True)


def slot_reduce(value):
    if lax.axis_size("win") != 2 or lax.axis_size("freq") != 2:
        return half_reduce(half_reduce(value, "freq"), "win")
    axes = ("win", "freq")
    own = lax.axis_index("win") * 2 + lax.axis_index("freq")
    slots = value.reshape((4, value.shape[0] // 4) + value.shape[1:])
    total = lax.dynamic_index_in_dim(slots, own, 0, keepdims=False)
    for mask in (1, 2, 3):
        send = lax.dynamic_index_in_dim(slots, own ^ mask, 0, keepdims=False)
        pairs = [(source, source ^ mask) for source in range(4)]
        total = total + lax.ppermute(send, axes, pairs)
    return total


def lag_table(first_bin, bin_count):
    lag_numbers = (jnp.arange(NLAG, dtype=jnp.int32) - NLAG // 2) * LAG_STRIDE
    lag_steps = (lag_numbers + SAMPLES) % SAMPLES
    split = 32 if bin_count % 32 == 0 else 1
    fine_bins = first_bin + 1 + jnp.arange(split, dtype=jnp.int32)
    coarse_bins = jnp.arange(bin_count // split, dtype=jnp.int32) * split
    scale = 2.0 * math.pi / SAMPLES
    fine = (fine_bins[:, None] * lag_steps[None, :]) % SAMPLES
    coarse = (coarse_bins[:, None] * lag_steps[None, :]) % SAMPLES
    fine_angle = fine.astype(jnp.float32) * scale
    coarse_angle = coarse.astype(jnp.float32) * scale
    fine_cos, fine_sin = jnp.cos(fine_angle)[None], jnp.sin(fine_angle)[None]
    coarse_cos, coarse_sin = jnp.cos(coarse_angle)[:, None], jnp.sin(coarse_angle)[:, None]
    cosine = coarse_cos * fine_cos - coarse_sin * fine_sin
    sine = coarse_sin * fine_cos + coarse_cos * fine_sin
    table = jnp.stack([cosine, -sine]).reshape(2, bin_count, NLAG)
    return table.astype(jnp.bfloat16)


def select_rows(block, rows):
    channel_ids = jnp.arange(block.shape[0], dtype=rows.dtype)
    one_hot = (rows[:, None] == channel_ids[None, :]).astype(block.dtype)
    return jnp.dot(one_hot, block, preferred_element_type=jnp.float32)


def whiten(raw, scales):
    real_in = raw[:, :, 0].astype(jnp.float32)
    imag_in = raw[:, :, 1].astype(jnp.float32)
    energy = real_in * real_in + imag_in * imag_in
    factor = scales[:, :, 1:2] / jnp.sqrt(energy + scales[:, :, 0:1] + 1e-06)
    whitened = jnp.concatenate([real_in * factor, imag_in * factor], axis=-1)
    return whitened.astype(jnp.bfloat16)


def body(spectra, live_mask, pair_rows, owner_map):
    channels, windows, _, bin_count = spectra.shape
    block_count = lax.axis_size("blk")
    offsets = block_count // 2 + 1
    own_block = lax.axis_index("blk")
    next_raw = shifted(spectra, "blk", -1) if offsets > 1 else spectra
    real_in = spectra[:, :, 0].astype(jnp.float32)
    imag_in = spectra[:, :, 1].astype(jnp.float32)
    energy = real_in * real_in + imag_in * imag_in
    power_sums = pair_sum(jnp.sum(energy, axis=-1), "freq")
    all_bins = bin_count * lax.axis_size("freq")
    mean_power = power_sums / all_bins
    scales = jnp.stack([mean_power, live_mask.astype(jnp.float32)], axis=-1)
    scale_pool = [scales] + [shifted(scales, "blk", -step) for step in range(1, offsets)]
    whitened = whiten(spectra, scales)
    first_bin, whitened = lax.optimization_barrier((lax.axis_index("freq") * bin_count, whitened))
    lag_basis = lag_table(first_bin, bin_count).reshape(2 * bin_count, NLAG)
    lag_basis = jnp.tile(lag_basis, (windows, 1))
    pair_lists = pair_rows[own_block]
    win_count = lax.axis_size("win")
    freq_count = lax.axis_size("freq")
    row_count = pair_rows.shape[-1]
    source_flat = whitened.reshape(channels, windows * 2 * bin_count)
    current = whitened
    reduced = []
    for offset in range(offsets):
        partner_flat = current.reshape(channels, windows * 2 * bin_count)
        source_rows = select_rows(source_flat, pair_lists[offset, 0])
        partner_rows = select_rows(partner_flat, pair_lists[offset, 1])
        source_rows = source_rows.reshape(row_count, windows, 2 * bin_count)
        partner_rows = partner_rows.reshape(row_count, windows, 2 * bin_count)
        source_real = source_rows[..., :bin_count]
        source_imag = source_rows[..., bin_count:]
        partner_real = partner_rows[..., :bin_count]
        partner_imag = partner_rows[..., bin_count:]
        cross_real = source_real * partner_real + source_imag * partner_imag
        cross_imag = source_imag * partner_real - source_real * partner_imag
        cross = jnp.concatenate([cross_real, cross_imag], axis=-1).astype(jnp.bfloat16)
        cross = cross.reshape(row_count, windows * 2 * bin_count)
        correlated = jnp.dot(cross, lag_basis, preferred_element_type=jnp.float32)
        if offset + 2 < offsets:
            correlated, raw_block = lax.optimization_barrier((correlated, next_raw))
            next_raw = shifted(raw_block, "blk", -1)
            current = whiten(raw_block, scale_pool[offset + 1])
            correlated, current = lax.optimization_barrier((correlated, current))
        elif offset + 1 < offsets:
            current = whiten(next_raw, scale_pool[offset + 1])
        reduced.append(slot_reduce(correlated))
    all_windows = windows * win_count
    scale = 1.0 / math.sqrt(all_bins * all_windows)
    own_owners = owner_map[own_block]
    if block_count > 4:
        summed = jnp.stack(reduced, axis=1)
        stacked = (summed * scale).astype(jnp.bfloat16)
        selector = (
            own_owners[None, :] == jnp.arange(block_count, dtype=jnp.int32)[:, None]
        ).astype(jnp.bfloat16)
        send_buffer = jnp.einsum(
            "ok,pkl->opl", selector, stacked, preferred_element_type=jnp.float32
        ).astype(jnp.bfloat16)
        received = lax.all_to_all(send_buffer, "blk", split_axis=0, concat_axis=0, tiled=True)
        return received[None]
    targets = (own_block + jnp.arange(block_count, dtype=jnp.int32)) % block_count
    masks = (own_owners[:, None] == targets[None, :]).astype(jnp.float32)
    send_buffer = None
    for offset, result in enumerate(reduced):
        stacked = (result * scale).astype(jnp.bfloat16).astype(jnp.float32)
        term = masks[offset][:, None, None] * stacked[None]
        send_buffer = term if send_buffer is None else send_buffer + term
    send_buffer = send_buffer.astype(jnp.bfloat16)
    parts = [send_buffer[0]]
    for distance in range(1, block_count):
        parts.append(shifted(send_buffer[distance], "blk", distance))
    reversed_parts = [parts[(-index) % block_count] for index in range(block_count)]
    doubled = jnp.stack(reversed_parts + reversed_parts)
    received = lax.dynamic_slice_in_dim(doubled, block_count - own_block, block_count)
    return received[None]


def solution(mesh):
    return jax.shard_map(
        body,
        mesh=mesh,
        in_specs=(
            P(("grp", "blk"), "win", None, "freq"),
            P(("grp", "blk"), "win"),
            P("grp", None, None, None),
            P("grp", None),
        ),
        out_specs=P(("grp", "blk"), None, ("win", "freq"), None),
        check_vma=False,
    )
```

```python
import math

import jax
import jax.numpy as jnp
from jax import lax
from jax.sharding import PartitionSpec as P

NLAG = 512
SAMPLES = 12000
LAG_STRIDE = 3


def shifted(value, axis, steps):
    count = lax.axis_size(axis)
    pairs = [(source, (source + steps) % count) for source in range(count)]
    return lax.ppermute(value, axis, pairs)


def pair_sum(value, axis):
    if lax.axis_size(axis) == 2:
        return value + shifted(value, axis, 1)
    return lax.psum(value, axis)


def half_reduce(value, axis):
    count = lax.axis_size(axis)
    if count == 2:
        index = lax.axis_index(axis)
        halves = value.reshape((2, value.shape[0] // 2) + value.shape[1:])
        keep = lax.dynamic_index_in_dim(halves, index, 0, keepdims=False)
        send = lax.dynamic_index_in_dim(halves, 1 - index, 0, keepdims=False)
        return keep + shifted(send, axis, 1)
    return lax.psum_scatter(value, axis, scatter_dimension=0, tiled=True)


def slot_reduce(value):
    if lax.axis_size("win") != 2 or lax.axis_size("freq") != 2:
        return half_reduce(half_reduce(value, "freq"), "win")
    axes = ("win", "freq")
    own = lax.axis_index("win") * 2 + lax.axis_index("freq")
    slots = value.reshape((4, value.shape[0] // 4) + value.shape[1:])
    total = lax.dynamic_index_in_dim(slots, own, 0, keepdims=False)
    for mask in (1, 2, 3):
        send = lax.dynamic_index_in_dim(slots, own ^ mask, 0, keepdims=False)
        pairs = [(source, source ^ mask) for source in range(4)]
        total = total + lax.ppermute(send, axes, pairs)
    return total


def lag_table(first_bin, bin_count):
    lag_numbers = (jnp.arange(NLAG, dtype=jnp.int32) - NLAG // 2) * LAG_STRIDE
    lag_steps = (lag_numbers + SAMPLES) % SAMPLES
    split = 32 if bin_count % 32 == 0 else 1
    fine_bins = first_bin + 1 + jnp.arange(split, dtype=jnp.int32)
    coarse_bins = jnp.arange(bin_count // split, dtype=jnp.int32) * split
    scale = 2.0 * math.pi / SAMPLES
    fine = (fine_bins[:, None] * lag_steps[None, :]) % SAMPLES
    coarse = (coarse_bins[:, None] * lag_steps[None, :]) % SAMPLES
    fine_angle = fine.astype(jnp.float32) * scale
    coarse_angle = coarse.astype(jnp.float32) * scale
    fine_cos, fine_sin = jnp.cos(fine_angle)[None], jnp.sin(fine_angle)[None]
    coarse_cos, coarse_sin = jnp.cos(coarse_angle)[:, None], jnp.sin(coarse_angle)[:, None]
    cosine = coarse_cos * fine_cos - coarse_sin * fine_sin
    sine = coarse_sin * fine_cos + coarse_cos * fine_sin
    table = jnp.stack([cosine, -sine]).reshape(2, bin_count, NLAG)
    return table.astype(jnp.bfloat16)


def select_rows(block, rows):
    channel_ids = jnp.arange(block.shape[0], dtype=rows.dtype)
    one_hot = (rows[:, None] == channel_ids[None, :]).astype(block.dtype)
    return jnp.dot(one_hot, block, preferred_element_type=jnp.float32)


def slot_exchange(chunks, axes, group, target_of):
    own = lax.axis_index(axes[-1]) + lax.axis_size(axes[-1]) * lax.axis_index(axes[-2])
    received = []
    for mask in range(4):
        send = lax.dynamic_index_in_dim(chunks, own ^ mask, 0, keepdims=False)
        pairs = [(source, target_of(source, mask)) for source in range(group)]
        if all(source == target for source, target in pairs):
            received.append(send)
        else:
            received.append(lax.ppermute(send, axes, pairs))
    return received


def slot_correlation(source_parts, partner_parts, full_basis, bin_count):
    crosses = []
    for source_rows, partner_rows in zip(source_parts, partner_parts):
        source_rows = source_rows.astype(jnp.float32)
        partner_rows = partner_rows.astype(jnp.float32)
        source_real, source_imag = source_rows[:, :bin_count], source_rows[:, bin_count:]
        partner_real, partner_imag = partner_rows[:, :bin_count], partner_rows[:, bin_count:]
        cross_real = source_real * partner_real + source_imag * partner_imag
        cross_imag = source_imag * partner_real - source_real * partner_imag
        crosses.append(jnp.concatenate([cross_real, cross_imag], axis=-1).astype(jnp.bfloat16))
    cross = jnp.concatenate(crosses, axis=-1)
    return jnp.dot(cross, full_basis, preferred_element_type=jnp.float32)


def whiten(raw, scales):
    real_in = raw[:, :, 0].astype(jnp.float32)
    imag_in = raw[:, :, 1].astype(jnp.float32)
    energy = real_in * real_in + imag_in * imag_in
    factor = scales[:, :, 1:2] / jnp.sqrt(energy + scales[:, :, 0:1] + 1e-06)
    whitened = jnp.concatenate([real_in * factor, imag_in * factor], axis=-1)
    return whitened.astype(jnp.bfloat16)


def body(spectra, live_mask, pair_rows, owner_map):
    channels, windows, _, bin_count = spectra.shape
    block_count = lax.axis_size("blk")
    offsets = block_count // 2 + 1
    own_block = lax.axis_index("blk")
    next_raw = shifted(spectra, "blk", -1) if offsets > 1 else spectra
    real_in = spectra[:, :, 0].astype(jnp.float32)
    imag_in = spectra[:, :, 1].astype(jnp.float32)
    energy = real_in * real_in + imag_in * imag_in
    power_sums = pair_sum(jnp.sum(energy, axis=-1), "freq")
    all_bins = bin_count * lax.axis_size("freq")
    mean_power = power_sums / all_bins
    scales = jnp.stack([mean_power, live_mask.astype(jnp.float32)], axis=-1)
    scale_pool = [scales] + [shifted(scales, "blk", -step) for step in range(1, offsets)]
    whitened = whiten(spectra, scales)
    first_bin, whitened = lax.optimization_barrier((lax.axis_index("freq") * bin_count, whitened))
    own_table = lag_table(first_bin, bin_count).reshape(2 * bin_count, NLAG)
    lag_basis = jnp.tile(own_table, (windows, 1))
    pair_lists = pair_rows[own_block]
    win_count = lax.axis_size("win")
    freq_count = lax.axis_size("freq")
    row_count = pair_rows.shape[-1]
    source_flat = whitened.reshape(channels, windows * 2 * bin_count)
    special = win_count == 2 and freq_count == 2 and windows == 1 and offsets >= 3
    if special:
        slot_rows = row_count // 4
        other_table = lag_table((1 - lax.axis_index("freq")) * bin_count, bin_count)
        other_table = other_table.reshape(2 * bin_count, NLAG)
        full_basis = jnp.concatenate([own_table, other_table, own_table, other_table], axis=0)
        own_rows = select_rows(source_flat, pair_lists[offsets - 1, 0]).astype(jnp.bfloat16)
        own_rows = own_rows.reshape(4, slot_rows, 2 * bin_count)
        source_parts = slot_exchange(
            own_rows, ("win", "freq"), 4, lambda source, mask: source ^ mask
        )
        left_lists = pair_rows[(own_block - 1) % block_count]
    current = whitened
    reduced = []
    for offset in range(offsets):
        if special and offset == offsets - 1:
            reduced.append(
                slot_correlation(source_parts, partner_parts, full_basis, bin_count)
            )
            break
        partner_flat = current.reshape(channels, windows * 2 * bin_count)
        source_rows = select_rows(source_flat, pair_lists[offset, 0])
        partner_rows = select_rows(partner_flat, pair_lists[offset, 1])
        source_rows = source_rows.reshape(row_count, windows, 2 * bin_count)
        partner_rows = partner_rows.reshape(row_count, windows, 2 * bin_count)
        source_real = source_rows[..., :bin_count]
        source_imag = source_rows[..., bin_count:]
        partner_real = partner_rows[..., :bin_count]
        partner_imag = partner_rows[..., bin_count:]
        cross_real = source_real * partner_real + source_imag * partner_imag
        cross_imag = source_imag * partner_real - source_real * partner_imag
        cross = jnp.concatenate([cross_real, cross_imag], axis=-1).astype(jnp.bfloat16)
        cross = cross.reshape(row_count, windows * 2 * bin_count)
        correlated = jnp.dot(cross, lag_basis, preferred_element_type=jnp.float32)
        if offset + 2 < offsets:
            correlated, raw_block = lax.optimization_barrier((correlated, next_raw))
            forward = special and offset + 3 == offsets
            if not forward:
                next_raw = shifted(raw_block, "blk", -1)
            current = whiten(raw_block, scale_pool[offset + 1])
            if forward:
                current_flat = current.reshape(channels, windows * 2 * bin_count)
                left_rows = select_rows(current_flat, left_lists[offsets - 1, 1])
                left_rows = left_rows.astype(jnp.bfloat16).reshape(4, slot_rows, 2 * bin_count)
                partner_parts = slot_exchange(
                    left_rows,
                    ("blk", "win", "freq"),
                    4 * block_count,
                    lambda source, mask: ((source // 4 - 1) % block_count) * 4 + ((source % 4) ^ mask),
                )
            correlated, current = lax.optimization_barrier((correlated, current))
        elif offset + 1 < offsets and not special:
            current = whiten(next_raw, scale_pool[offset + 1])
        reduced.append(slot_reduce(correlated))
    all_windows = windows * win_count
    scale = 1.0 / math.sqrt(all_bins * all_windows)
    own_owners = owner_map[own_block]
    if block_count > 4:
        summed = jnp.stack(reduced, axis=1)
        stacked = (summed * scale).astype(jnp.bfloat16)
        selector = (
            own_owners[None, :] == jnp.arange(block_count, dtype=jnp.int32)[:, None]
        ).astype(jnp.bfloat16)
        send_buffer = jnp.einsum(
            "ok,pkl->opl", selector, stacked, preferred_element_type=jnp.float32
        ).astype(jnp.bfloat16)
        received = lax.all_to_all(send_buffer, "blk", split_axis=0, concat_axis=0, tiled=True)
        return received[None]
    targets = (own_block + jnp.arange(block_count, dtype=jnp.int32)) % block_count
    masks = (own_owners[:, None] == targets[None, :]).astype(jnp.float32)
    send_buffer = None
    for offset, result in enumerate(reduced):
        stacked = (result * scale).astype(jnp.bfloat16).astype(jnp.float32)
        term = masks[offset][:, None, None] * stacked[None]
        send_buffer = term if send_buffer is None else send_buffer + term
    send_buffer = send_buffer.astype(jnp.bfloat16)
    parts = [send_buffer[0]]
    for distance in range(1, block_count):
        parts.append(shifted(send_buffer[distance], "blk", distance))
    reversed_parts = [parts[(-index) % block_count] for index in range(block_count)]
    doubled = jnp.stack(reversed_parts + reversed_parts)
    received = lax.dynamic_slice_in_dim(doubled, block_count - own_block, block_count)
    return received[None]


def solution(mesh):
    return jax.shard_map(
        body,
        mesh=mesh,
        in_specs=(
            P(("grp", "blk"), "win", None, "freq"),
            P(("grp", "blk"), "win"),
            P("grp", None, None, None),
            P("grp", None),
        ),
        out_specs=P(("grp", "blk"), None, ("win", "freq"), None),
        check_vma=False,
    )
```

```python
import math

import jax
import jax.numpy as jnp
from jax import lax
from jax.sharding import PartitionSpec as P

NLAG = 512
SAMPLES = 12000
LAG_STRIDE = 3


def shifted(value, axis, steps):
    count = lax.axis_size(axis)
    pairs = [(source, (source + steps) % count) for source in range(count)]
    return lax.ppermute(value, axis, pairs)


def pair_sum(value, axis):
    if lax.axis_size(axis) == 2:
        return value + shifted(value, axis, 1)
    return lax.psum(value, axis)


def half_reduce(value, axis):
    count = lax.axis_size(axis)
    if count == 2:
        index = lax.axis_index(axis)
        halves = value.reshape((2, value.shape[0] // 2) + value.shape[1:])
        keep = lax.dynamic_index_in_dim(halves, index, 0, keepdims=False)
        send = lax.dynamic_index_in_dim(halves, 1 - index, 0, keepdims=False)
        return keep + shifted(send, axis, 1)
    return lax.psum_scatter(value, axis, scatter_dimension=0, tiled=True)


def slot_reduce(value):
    if lax.axis_size("win") != 2 or lax.axis_size("freq") != 2:
        return half_reduce(half_reduce(value, "freq"), "win")
    axes = ("win", "freq")
    own = lax.axis_index("win") * 2 + lax.axis_index("freq")
    slots = value.reshape((4, value.shape[0] // 4) + value.shape[1:])
    total = lax.dynamic_index_in_dim(slots, own, 0, keepdims=False)
    for mask in (1, 2, 3):
        send = lax.dynamic_index_in_dim(slots, own ^ mask, 0, keepdims=False)
        pairs = [(source, source ^ mask) for source in range(4)]
        total = total + lax.ppermute(send, axes, pairs)
    return total


def lag_table(first_bin, bin_count):
    lag_numbers = (jnp.arange(NLAG, dtype=jnp.int32) - NLAG // 2) * LAG_STRIDE
    lag_steps = (lag_numbers + SAMPLES) % SAMPLES
    split = 32 if bin_count % 32 == 0 else 1
    fine_bins = first_bin + 1 + jnp.arange(split, dtype=jnp.int32)
    coarse_bins = jnp.arange(bin_count // split, dtype=jnp.int32) * split
    scale = 2.0 * math.pi / SAMPLES
    fine = (fine_bins[:, None] * lag_steps[None, :]) % SAMPLES
    coarse = (coarse_bins[:, None] * lag_steps[None, :]) % SAMPLES
    fine_angle = fine.astype(jnp.float32) * scale
    coarse_angle = coarse.astype(jnp.float32) * scale
    fine_cos, fine_sin = jnp.cos(fine_angle)[None], jnp.sin(fine_angle)[None]
    coarse_cos, coarse_sin = jnp.cos(coarse_angle)[:, None], jnp.sin(coarse_angle)[:, None]
    cosine = coarse_cos * fine_cos - coarse_sin * fine_sin
    sine = coarse_sin * fine_cos + coarse_cos * fine_sin
    table = jnp.stack([cosine, -sine]).reshape(2, bin_count, NLAG)
    return table.astype(jnp.bfloat16)


def select_rows(block, rows):
    channel_ids = jnp.arange(block.shape[0], dtype=rows.dtype)
    one_hot = (rows[:, None] == channel_ids[None, :]).astype(block.dtype)
    return jnp.dot(one_hot, block, preferred_element_type=jnp.float32)


def slot_exchange(chunks, axes, group, target_of):
    own = lax.axis_index(axes[-1]) + lax.axis_size(axes[-1]) * lax.axis_index(axes[-2])
    received = []
    for mask in range(4):
        send = lax.dynamic_index_in_dim(chunks, own ^ mask, 0, keepdims=False)
        pairs = [(source, target_of(source, mask)) for source in range(group)]
        if all(source == target for source, target in pairs):
            received.append(send)
        else:
            received.append(lax.ppermute(send, axes, pairs))
    return received


def slot_correlation(source_parts, partner_parts, full_basis, bin_count):
    crosses = []
    for source_rows, partner_rows in zip(source_parts, partner_parts):
        source_rows = source_rows.astype(jnp.float32)
        partner_rows = partner_rows.astype(jnp.float32)
        source_real, source_imag = source_rows[:, :bin_count], source_rows[:, bin_count:]
        partner_real, partner_imag = partner_rows[:, :bin_count], partner_rows[:, bin_count:]
        cross_real = source_real * partner_real + source_imag * partner_imag
        cross_imag = source_imag * partner_real - source_real * partner_imag
        crosses.append(jnp.concatenate([cross_real, cross_imag], axis=-1).astype(jnp.bfloat16))
    cross = jnp.concatenate(crosses, axis=-1)
    return jnp.dot(cross, full_basis, preferred_element_type=jnp.float32)


def whiten(raw, scales):
    real_in = raw[:, :, 0].astype(jnp.float32)
    imag_in = raw[:, :, 1].astype(jnp.float32)
    energy = real_in * real_in + imag_in * imag_in
    factor = scales[:, :, 1:2] / jnp.sqrt(energy + scales[:, :, 0:1] + 1e-06)
    whitened = jnp.concatenate([real_in * factor, imag_in * factor], axis=-1)
    return whitened.astype(jnp.bfloat16)


def body(spectra, live_mask, pair_rows, owner_map):
    channels, windows, _, bin_count = spectra.shape
    block_count = lax.axis_size("blk")
    offsets = block_count // 2 + 1
    own_block = lax.axis_index("blk")
    next_raw = shifted(spectra, "blk", -1) if offsets > 1 else spectra
    real_in = spectra[:, :, 0].astype(jnp.float32)
    imag_in = spectra[:, :, 1].astype(jnp.float32)
    energy = real_in * real_in + imag_in * imag_in
    power_sums = pair_sum(jnp.sum(energy, axis=-1), "freq")
    all_bins = bin_count * lax.axis_size("freq")
    mean_power = power_sums / all_bins
    scales = jnp.stack([mean_power, live_mask.astype(jnp.float32)], axis=-1)
    scale_pool = [scales] + [shifted(scales, "blk", -step) for step in range(1, offsets)]
    whitened = whiten(spectra, scales)
    first_bin, whitened = lax.optimization_barrier((lax.axis_index("freq") * bin_count, whitened))
    own_table = lag_table(first_bin, bin_count).reshape(2 * bin_count, NLAG)
    lag_basis = jnp.tile(own_table, (windows, 1))
    pair_lists = pair_rows[own_block]
    win_count = lax.axis_size("win")
    freq_count = lax.axis_size("freq")
    row_count = pair_rows.shape[-1]
    source_flat = whitened.reshape(channels, windows * 2 * bin_count)
    special = win_count == 2 and freq_count == 2 and windows == 1 and offsets >= 3
    if special:
        slot_rows = row_count // 4
        other_table = lag_table((1 - lax.axis_index("freq")) * bin_count, bin_count)
        other_table = other_table.reshape(2 * bin_count, NLAG)
        full_basis = jnp.concatenate([own_table, other_table, own_table, other_table], axis=0)
        own_rows = select_rows(source_flat, pair_lists[offsets - 1, 0]).astype(jnp.bfloat16)
        own_rows = own_rows.reshape(4, slot_rows, 2 * bin_count)
        source_parts = slot_exchange(
            own_rows, ("win", "freq"), 4, lambda source, mask: source ^ mask
        )
        left_lists = pair_rows[(own_block - 1) % block_count]
    current = whitened
    reduced = []
    pending = []
    for offset in range(offsets):
        if special and offset == offsets - 1:
            reduced.append(
                slot_correlation(source_parts, partner_parts, full_basis, bin_count)
            )
            break
        partner_flat = current.reshape(channels, windows * 2 * bin_count)
        source_rows = select_rows(source_flat, pair_lists[offset, 0])
        partner_rows = select_rows(partner_flat, pair_lists[offset, 1])
        source_rows = source_rows.reshape(row_count, windows, 2 * bin_count)
        partner_rows = partner_rows.reshape(row_count, windows, 2 * bin_count)
        source_real = source_rows[..., :bin_count]
        source_imag = source_rows[..., bin_count:]
        partner_real = partner_rows[..., :bin_count]
        partner_imag = partner_rows[..., bin_count:]
        cross_real = source_real * partner_real + source_imag * partner_imag
        cross_imag = source_imag * partner_real - source_real * partner_imag
        cross = jnp.concatenate([cross_real, cross_imag], axis=-1).astype(jnp.bfloat16)
        cross = cross.reshape(row_count, windows * 2 * bin_count)
        correlated = jnp.dot(cross, lag_basis, preferred_element_type=jnp.float32)
        if offset + 2 < offsets:
            correlated, raw_block = lax.optimization_barrier((correlated, next_raw))
            forward = special and offset + 3 == offsets
            if not forward:
                next_raw = shifted(raw_block, "blk", -1)
            current = whiten(raw_block, scale_pool[offset + 1])
            if forward:
                current_flat = current.reshape(channels, windows * 2 * bin_count)
                left_rows = select_rows(current_flat, left_lists[offsets - 1, 1])
                left_rows = left_rows.astype(jnp.bfloat16).reshape(4, slot_rows, 2 * bin_count)
                partner_parts = slot_exchange(
                    left_rows,
                    ("blk", "win", "freq"),
                    4 * block_count,
                    lambda source, mask: ((source // 4 - 1) % block_count) * 4 + ((source % 4) ^ mask),
                )
            correlated, current = lax.optimization_barrier((correlated, current))
        elif offset + 1 < offsets and not special:
            current = whiten(next_raw, scale_pool[offset + 1])
        if special:
            pending.append(correlated)
            if offset + 2 == offsets:
                merged, _ = lax.optimization_barrier((jnp.stack(pending, axis=1), left_rows))
                merged = merged.reshape((2, 2, slot_rows) + merged.shape[1:])
                merged = merged.transpose(1, 0, 2, 3, 4).reshape((row_count,) + merged.shape[3:])
                merged = half_reduce(half_reduce(merged, "freq"), "win")
                reduced.extend(merged[:, index] for index in range(len(pending)))
            continue
        reduced.append(slot_reduce(correlated))
    all_windows = windows * win_count
    scale = 1.0 / math.sqrt(all_bins * all_windows)
    own_owners = owner_map[own_block]
    if block_count > 4:
        summed = jnp.stack(reduced, axis=1)
        stacked = (summed * scale).astype(jnp.bfloat16)
        selector = (
            own_owners[None, :] == jnp.arange(block_count, dtype=jnp.int32)[:, None]
        ).astype(jnp.bfloat16)
        send_buffer = jnp.einsum(
            "ok,pkl->opl", selector, stacked, preferred_element_type=jnp.float32
        ).astype(jnp.bfloat16)
        received = lax.all_to_all(send_buffer, "blk", split_axis=0, concat_axis=0, tiled=True)
        return received[None]
    targets = (own_block + jnp.arange(block_count, dtype=jnp.int32)) % block_count
    masks = (own_owners[:, None] == targets[None, :]).astype(jnp.float32)
    send_buffer = None
    for offset, result in enumerate(reduced):
        stacked = (result * scale).astype(jnp.bfloat16).astype(jnp.float32)
        term = masks[offset][:, None, None] * stacked[None]
        send_buffer = term if send_buffer is None else send_buffer + term
    send_buffer = send_buffer.astype(jnp.bfloat16)
    parts = [send_buffer[0]]
    for distance in range(1, block_count):
        parts.append(shifted(send_buffer[distance], "blk", distance))
    reversed_parts = [parts[(-index) % block_count] for index in range(block_count)]
    doubled = jnp.stack(reversed_parts + reversed_parts)
    received = lax.dynamic_slice_in_dim(doubled, block_count - own_block, block_count)
    return received[None]


def solution(mesh):
    return jax.shard_map(
        body,
        mesh=mesh,
        in_specs=(
            P(("grp", "blk"), "win", None, "freq"),
            P(("grp", "blk"), "win"),
            P("grp", None, None, None),
            P("grp", None),
        ),
        out_specs=P(("grp", "blk"), None, ("win", "freq"), None),
        check_vma=False,
    )
```

```python
import math

import jax
import jax.numpy as jnp
from jax import lax
from jax.sharding import PartitionSpec as P

NLAG = 512
SAMPLES = 12000
LAG_STRIDE = 3


def shifted(value, axis, steps):
    count = lax.axis_size(axis)
    pairs = [(source, (source + steps) % count) for source in range(count)]
    return lax.ppermute(value, axis, pairs)


def pair_sum(value, axis):
    if lax.axis_size(axis) == 2:
        return value + shifted(value, axis, 1)
    return lax.psum(value, axis)


def half_reduce(value, axis):
    count = lax.axis_size(axis)
    if count == 2:
        index = lax.axis_index(axis)
        halves = value.reshape((2, value.shape[0] // 2) + value.shape[1:])
        keep = lax.dynamic_index_in_dim(halves, index, 0, keepdims=False)
        send = lax.dynamic_index_in_dim(halves, 1 - index, 0, keepdims=False)
        return keep + shifted(send, axis, 1)
    return lax.psum_scatter(value, axis, scatter_dimension=0, tiled=True)


def slot_reduce(value):
    if lax.axis_size("win") != 2 or lax.axis_size("freq") != 2:
        return half_reduce(half_reduce(value, "freq"), "win")
    axes = ("win", "freq")
    own = lax.axis_index("win") * 2 + lax.axis_index("freq")
    slots = value.reshape((4, value.shape[0] // 4) + value.shape[1:])
    total = lax.dynamic_index_in_dim(slots, own, 0, keepdims=False)
    for mask in (1, 2, 3):
        send = lax.dynamic_index_in_dim(slots, own ^ mask, 0, keepdims=False)
        pairs = [(source, source ^ mask) for source in range(4)]
        total = total + lax.ppermute(send, axes, pairs)
    return total


def lag_table(first_bin, bin_count):
    lag_numbers = (jnp.arange(NLAG, dtype=jnp.int32) - NLAG // 2) * LAG_STRIDE
    lag_steps = (lag_numbers + SAMPLES) % SAMPLES
    split = 32 if bin_count % 32 == 0 else 1
    fine_bins = first_bin + 1 + jnp.arange(split, dtype=jnp.int32)
    coarse_bins = jnp.arange(bin_count // split, dtype=jnp.int32) * split
    scale = 2.0 * math.pi / SAMPLES
    fine = (fine_bins[:, None] * lag_steps[None, :]) % SAMPLES
    coarse = (coarse_bins[:, None] * lag_steps[None, :]) % SAMPLES
    fine_angle = fine.astype(jnp.float32) * scale
    coarse_angle = coarse.astype(jnp.float32) * scale
    fine_cos, fine_sin = jnp.cos(fine_angle)[None], jnp.sin(fine_angle)[None]
    coarse_cos, coarse_sin = jnp.cos(coarse_angle)[:, None], jnp.sin(coarse_angle)[:, None]
    cosine = coarse_cos * fine_cos - coarse_sin * fine_sin
    sine = coarse_sin * fine_cos + coarse_cos * fine_sin
    table = jnp.stack([cosine, -sine]).reshape(2, bin_count, NLAG)
    return table.astype(jnp.bfloat16)


def select_rows(block, rows):
    channel_ids = jnp.arange(block.shape[0], dtype=rows.dtype)
    one_hot = (rows[:, None] == channel_ids[None, :]).astype(block.dtype)
    return jnp.dot(one_hot, block, preferred_element_type=jnp.float32)


def slot_exchange(chunks, axes, group, target_of):
    own = lax.axis_index(axes[-1]) + lax.axis_size(axes[-1]) * lax.axis_index(axes[-2])
    received = []
    for mask in range(4):
        send = lax.dynamic_index_in_dim(chunks, own ^ mask, 0, keepdims=False)
        pairs = [(source, target_of(source, mask)) for source in range(group)]
        if all(source == target for source, target in pairs):
            received.append(send)
        else:
            received.append(lax.ppermute(send, axes, pairs))
    return received


def slot_correlation(source_parts, partner_parts, full_basis, bin_count):
    crosses = []
    for source_rows, partner_rows in zip(source_parts, partner_parts):
        source_rows = source_rows.astype(jnp.float32)
        partner_rows = partner_rows.astype(jnp.float32)
        source_real, source_imag = source_rows[:, :bin_count], source_rows[:, bin_count:]
        partner_real, partner_imag = partner_rows[:, :bin_count], partner_rows[:, bin_count:]
        cross_real = source_real * partner_real + source_imag * partner_imag
        cross_imag = source_imag * partner_real - source_real * partner_imag
        crosses.append(jnp.concatenate([cross_real, cross_imag], axis=-1).astype(jnp.bfloat16))
    cross = jnp.concatenate(crosses, axis=-1)
    return jnp.dot(cross, full_basis, preferred_element_type=jnp.float32)


def whiten(raw, scales):
    real_in = raw[:, :, 0].astype(jnp.float32)
    imag_in = raw[:, :, 1].astype(jnp.float32)
    energy = real_in * real_in + imag_in * imag_in
    factor = scales[:, :, 1:2] / jnp.sqrt(energy + scales[:, :, 0:1] + 1e-06)
    whitened = jnp.concatenate([real_in * factor, imag_in * factor], axis=-1)
    return whitened.astype(jnp.bfloat16)


def body(spectra, live_mask, pair_rows, owner_map):
    channels, windows, _, bin_count = spectra.shape
    block_count = lax.axis_size("blk")
    offsets = block_count // 2 + 1
    own_block = lax.axis_index("blk")
    next_raw = shifted(spectra, "blk", -1) if offsets > 1 else spectra
    real_in = spectra[:, :, 0].astype(jnp.float32)
    imag_in = spectra[:, :, 1].astype(jnp.float32)
    energy = real_in * real_in + imag_in * imag_in
    power_sums = pair_sum(jnp.sum(energy, axis=-1), "freq")
    all_bins = bin_count * lax.axis_size("freq")
    mean_power = power_sums / all_bins
    scales = jnp.stack([mean_power, live_mask.astype(jnp.float32)], axis=-1)
    scale_pool = [scales] + [shifted(scales, "blk", -step) for step in range(1, offsets)]
    whitened = whiten(spectra, scales)
    first_bin, whitened = lax.optimization_barrier((lax.axis_index("freq") * bin_count, whitened))
    own_table = lag_table(first_bin, bin_count).reshape(2 * bin_count, NLAG)
    lag_basis = jnp.tile(own_table, (windows, 1))
    pair_lists = pair_rows[own_block]
    win_count = lax.axis_size("win")
    freq_count = lax.axis_size("freq")
    row_count = pair_rows.shape[-1]
    source_flat = whitened.reshape(channels, windows * 2 * bin_count)
    special = win_count == 2 and freq_count == 2 and windows == 1 and offsets >= 3
    if special:
        slot_rows = row_count // 4
        other_table = lag_table((1 - lax.axis_index("freq")) * bin_count, bin_count)
        other_table = other_table.reshape(2 * bin_count, NLAG)
        full_basis = jnp.concatenate([own_table, other_table, own_table, other_table], axis=0)
        own_rows = select_rows(source_flat, pair_lists[offsets - 1, 0]).astype(jnp.bfloat16)
        own_rows = own_rows.reshape(4, slot_rows, 2 * bin_count)
        source_parts = slot_exchange(
            own_rows, ("win", "freq"), 4, lambda source, mask: source ^ mask
        )
        left_lists = pair_rows[(own_block - 1) % block_count]
    current = whitened
    reduced = []
    pending = []
    for offset in range(offsets):
        if special and offset == offsets - 1:
            reduced.append(
                slot_correlation(source_parts, partner_parts, full_basis, bin_count)
            )
            break
        partner_flat = current.reshape(channels, windows * 2 * bin_count)
        source_rows = select_rows(source_flat, pair_lists[offset, 0])
        partner_rows = select_rows(partner_flat, pair_lists[offset, 1])
        source_rows = source_rows.reshape(row_count, windows, 2 * bin_count)
        partner_rows = partner_rows.reshape(row_count, windows, 2 * bin_count)
        source_real = source_rows[..., :bin_count]
        source_imag = source_rows[..., bin_count:]
        partner_real = partner_rows[..., :bin_count]
        partner_imag = partner_rows[..., bin_count:]
        cross_real = source_real * partner_real + source_imag * partner_imag
        cross_imag = source_imag * partner_real - source_real * partner_imag
        cross = jnp.concatenate([cross_real, cross_imag], axis=-1).astype(jnp.bfloat16)
        cross = cross.reshape(row_count, windows * 2 * bin_count)
        correlated = jnp.dot(cross, lag_basis, preferred_element_type=jnp.float32)
        if offset + 2 < offsets:
            correlated, raw_block = lax.optimization_barrier((correlated, next_raw))
            forward = special and offset + 3 == offsets
            if not forward:
                next_raw = shifted(raw_block, "blk", -1)
            current = whiten(raw_block, scale_pool[offset + 1])
            correlated, current = lax.optimization_barrier((correlated, current))
        elif offset + 1 < offsets and not special:
            current = whiten(next_raw, scale_pool[offset + 1])
        if special:
            pending.append(correlated)
            if offset + 2 == offsets:
                correlated, current = lax.optimization_barrier((correlated, current))
                current_flat = current.reshape(channels, windows * 2 * bin_count)
                left_rows = select_rows(current_flat, left_lists[offsets - 1, 1])
                left_rows = left_rows.astype(jnp.bfloat16).reshape(4, slot_rows, 2 * bin_count)
                partner_parts = slot_exchange(
                    left_rows,
                    ("blk", "win", "freq"),
                    4 * block_count,
                    lambda source, mask: ((source // 4 - 1) % block_count) * 4 + ((source % 4) ^ mask),
                )
                pending[-1] = correlated
                merged, _ = lax.optimization_barrier((jnp.stack(pending, axis=1), left_rows))
                merged = merged.reshape((2, 2, slot_rows) + merged.shape[1:])
                merged = merged.transpose(1, 0, 2, 3, 4).reshape((row_count,) + merged.shape[3:])
                merged = half_reduce(half_reduce(merged, "freq"), "win")
                reduced.extend(merged[:, index] for index in range(len(pending)))
            continue
        reduced.append(slot_reduce(correlated))
    all_windows = windows * win_count
    scale = 1.0 / math.sqrt(all_bins * all_windows)
    own_owners = owner_map[own_block]
    if block_count > 4:
        summed = jnp.stack(reduced, axis=1)
        stacked = (summed * scale).astype(jnp.bfloat16)
        selector = (
            own_owners[None, :] == jnp.arange(block_count, dtype=jnp.int32)[:, None]
        ).astype(jnp.bfloat16)
        send_buffer = jnp.einsum(
            "ok,pkl->opl", selector, stacked, preferred_element_type=jnp.float32
        ).astype(jnp.bfloat16)
        received = lax.all_to_all(send_buffer, "blk", split_axis=0, concat_axis=0, tiled=True)
        return received[None]
    targets = (own_block + jnp.arange(block_count, dtype=jnp.int32)) % block_count
    masks = (own_owners[:, None] == targets[None, :]).astype(jnp.float32)
    send_buffer = None
    for offset, result in enumerate(reduced):
        stacked = (result * scale).astype(jnp.bfloat16).astype(jnp.float32)
        term = masks[offset][:, None, None] * stacked[None]
        send_buffer = term if send_buffer is None else send_buffer + term
    send_buffer = send_buffer.astype(jnp.bfloat16)
    parts = [send_buffer[0]]
    for distance in range(1, block_count):
        parts.append(shifted(send_buffer[distance], "blk", distance))
    reversed_parts = [parts[(-index) % block_count] for index in range(block_count)]
    doubled = jnp.stack(reversed_parts + reversed_parts)
    received = lax.dynamic_slice_in_dim(doubled, block_count - own_block, block_count)
    return received[None]


def solution(mesh):
    return jax.shard_map(
        body,
        mesh=mesh,
        in_specs=(
            P(("grp", "blk"), "win", None, "freq"),
            P(("grp", "blk"), "win"),
            P("grp", None, None, None),
            P("grp", None),
        ),
        out_specs=P(("grp", "blk"), None, ("win", "freq"), None),
        check_vma=False,
    )
```

```python
import math

import jax
import jax.numpy as jnp
from jax import lax
from jax.sharding import PartitionSpec as P

NLAG = 512
SAMPLES = 12000
LAG_STRIDE = 3


def shifted(value, axis, steps):
    count = lax.axis_size(axis)
    pairs = [(source, (source + steps) % count) for source in range(count)]
    return lax.ppermute(value, axis, pairs)


def pair_sum(value, axis):
    if lax.axis_size(axis) == 2:
        return value + shifted(value, axis, 1)
    return lax.psum(value, axis)


def half_reduce(value, axis):
    count = lax.axis_size(axis)
    if count == 2:
        index = lax.axis_index(axis)
        halves = value.reshape((2, value.shape[0] // 2) + value.shape[1:])
        keep = lax.dynamic_index_in_dim(halves, index, 0, keepdims=False)
        send = lax.dynamic_index_in_dim(halves, 1 - index, 0, keepdims=False)
        return keep + shifted(send, axis, 1)
    return lax.psum_scatter(value, axis, scatter_dimension=0, tiled=True)


def slot_reduce(value):
    if lax.axis_size("win") != 2 or lax.axis_size("freq") != 2:
        return half_reduce(half_reduce(value, "freq"), "win")
    axes = ("win", "freq")
    own = lax.axis_index("win") * 2 + lax.axis_index("freq")
    slots = value.reshape((4, value.shape[0] // 4) + value.shape[1:])
    total = lax.dynamic_index_in_dim(slots, own, 0, keepdims=False)
    for mask in (1, 2, 3):
        send = lax.dynamic_index_in_dim(slots, own ^ mask, 0, keepdims=False)
        pairs = [(source, source ^ mask) for source in range(4)]
        total = total + lax.ppermute(send, axes, pairs)
    return total


def lag_table(first_bin, bin_count):
    lag_numbers = (jnp.arange(NLAG, dtype=jnp.int32) - NLAG // 2) * LAG_STRIDE
    lag_steps = (lag_numbers + SAMPLES) % SAMPLES
    split = 32 if bin_count % 32 == 0 else 1
    fine_bins = first_bin + 1 + jnp.arange(split, dtype=jnp.int32)
    coarse_bins = jnp.arange(bin_count // split, dtype=jnp.int32) * split
    scale = 2.0 * math.pi / SAMPLES
    fine = (fine_bins[:, None] * lag_steps[None, :]) % SAMPLES
    coarse = (coarse_bins[:, None] * lag_steps[None, :]) % SAMPLES
    fine_angle = fine.astype(jnp.float32) * scale
    coarse_angle = coarse.astype(jnp.float32) * scale
    fine_cos, fine_sin = jnp.cos(fine_angle)[None], jnp.sin(fine_angle)[None]
    coarse_cos, coarse_sin = jnp.cos(coarse_angle)[:, None], jnp.sin(coarse_angle)[:, None]
    cosine = coarse_cos * fine_cos - coarse_sin * fine_sin
    sine = coarse_sin * fine_cos + coarse_cos * fine_sin
    table = jnp.stack([cosine, -sine]).reshape(2, bin_count, NLAG)
    return table.astype(jnp.bfloat16)


def select_rows(block, rows):
    channel_ids = jnp.arange(block.shape[0], dtype=rows.dtype)
    one_hot = (rows[:, None] == channel_ids[None, :]).astype(block.dtype)
    return jnp.dot(one_hot, block, preferred_element_type=jnp.float32)


def whiten(raw, scales):
    real_in = raw[:, :, 0].astype(jnp.float32)
    imag_in = raw[:, :, 1].astype(jnp.float32)
    energy = real_in * real_in + imag_in * imag_in
    factor = scales[:, :, 1:2] / jnp.sqrt(energy + scales[:, :, 0:1] + 1e-06)
    whitened = jnp.concatenate([real_in * factor, imag_in * factor], axis=-1)
    return whitened.astype(jnp.bfloat16)


def body(spectra, live_mask, pair_rows, owner_map):
    channels, windows, _, bin_count = spectra.shape
    block_count = lax.axis_size("blk")
    offsets = block_count // 2 + 1
    own_block = lax.axis_index("blk")
    next_raw = shifted(spectra, "blk", -1) if offsets > 1 else spectra
    real_in = spectra[:, :, 0].astype(jnp.float32)
    imag_in = spectra[:, :, 1].astype(jnp.float32)
    energy = real_in * real_in + imag_in * imag_in
    power_sums = pair_sum(jnp.sum(energy, axis=-1), "freq")
    all_bins = bin_count * lax.axis_size("freq")
    mean_power = power_sums / all_bins
    scales = jnp.stack([mean_power, live_mask.astype(jnp.float32)], axis=-1)
    scale_pool = [scales] + [shifted(scales, "blk", -step) for step in range(1, offsets)]
    whitened = whiten(spectra, scales)
    first_bin, whitened = lax.optimization_barrier((lax.axis_index("freq") * bin_count, whitened))
    lag_basis = lag_table(first_bin, bin_count).reshape(2 * bin_count, NLAG)
    lag_basis = jnp.tile(lag_basis, (windows, 1))
    pair_lists = pair_rows[own_block]
    win_count = lax.axis_size("win")
    freq_count = lax.axis_size("freq")
    row_count = pair_rows.shape[-1]
    source_flat = whitened.reshape(channels, windows * 2 * bin_count)
    current = whitened
    reduced = []
    for offset in range(offsets):
        partner_flat = current.reshape(channels, windows * 2 * bin_count)
        source_rows = select_rows(source_flat, pair_lists[offset, 0])
        partner_rows = select_rows(partner_flat, pair_lists[offset, 1])
        source_rows = source_rows.reshape(row_count, windows, 2 * bin_count)
        partner_rows = partner_rows.reshape(row_count, windows, 2 * bin_count)
        source_real = source_rows[..., :bin_count]
        source_imag = source_rows[..., bin_count:]
        partner_real = partner_rows[..., :bin_count]
        partner_imag = partner_rows[..., bin_count:]
        cross_real = source_real * partner_real + source_imag * partner_imag
        cross_imag = source_imag * partner_real - source_real * partner_imag
        cross = jnp.concatenate([cross_real, cross_imag], axis=-1).astype(jnp.bfloat16)
        cross = cross.reshape(row_count, windows * 2 * bin_count)
        correlated = jnp.dot(cross, lag_basis, preferred_element_type=jnp.float32)
        if offset + 2 < offsets:
            correlated, raw_block = lax.optimization_barrier((correlated, next_raw))
            next_raw = shifted(raw_block, "blk", -1)
            current = whiten(raw_block, scale_pool[offset + 1])
            correlated, current = lax.optimization_barrier((correlated, current))
        elif offset + 1 < offsets:
            current = whiten(next_raw, scale_pool[offset + 1])
        reduced.append(slot_reduce(correlated))
    all_windows = windows * win_count
    scale = 1.0 / math.sqrt(all_bins * all_windows)
    own_owners = owner_map[own_block]
    if block_count > 4:
        summed = jnp.stack(reduced, axis=1)
        stacked = (summed * scale).astype(jnp.bfloat16)
        selector = (
            own_owners[None, :] == jnp.arange(block_count, dtype=jnp.int32)[:, None]
        ).astype(jnp.bfloat16)
        send_buffer = jnp.einsum(
            "ok,pkl->opl", selector, stacked, preferred_element_type=jnp.float32
        ).astype(jnp.bfloat16)
        received = lax.all_to_all(send_buffer, "blk", split_axis=0, concat_axis=0, tiled=True)
        return received[None]
    targets = (own_block + jnp.arange(block_count, dtype=jnp.int32)) % block_count
    masks = (own_owners[:, None] == targets[None, :]).astype(jnp.float32)
    send_buffer = None
    for offset, result in enumerate(reduced):
        stacked = (result * scale).astype(jnp.bfloat16).astype(jnp.float32)
        term = masks[offset][:, None, None] * stacked[None]
        send_buffer = term if send_buffer is None else send_buffer + term
    send_buffer = send_buffer.astype(jnp.bfloat16)
    if block_count == 4:
        by_owner = jnp.take(send_buffer, (jnp.arange(block_count) - own_block) % block_count, axis=0)
        received = lax.all_to_all(by_owner, "blk", split_axis=0, concat_axis=0, tiled=True)
        return received[None]
    parts = [send_buffer[0]]
    for distance in range(1, block_count):
        parts.append(shifted(send_buffer[distance], "blk", distance))
    reversed_parts = [parts[(-index) % block_count] for index in range(block_count)]
    doubled = jnp.stack(reversed_parts + reversed_parts)
    received = lax.dynamic_slice_in_dim(doubled, block_count - own_block, block_count)
    return received[None]


def solution(mesh):
    return jax.shard_map(
        body,
        mesh=mesh,
        in_specs=(
            P(("grp", "blk"), "win", None, "freq"),
            P(("grp", "blk"), "win"),
            P("grp", None, None, None),
            P("grp", None),
        ),
        out_specs=P(("grp", "blk"), None, ("win", "freq"), None),
        check_vma=False,
    )
```

```python
import math

import jax
import jax.numpy as jnp
from jax import lax
from jax.sharding import PartitionSpec as P

NLAG = 512
SAMPLES = 12000
LAG_STRIDE = 3


def shifted(value, axis, steps):
    count = lax.axis_size(axis)
    pairs = [(source, (source + steps) % count) for source in range(count)]
    return lax.ppermute(value, axis, pairs)


def pair_sum(value, axis):
    if lax.axis_size(axis) == 2:
        return value + shifted(value, axis, 1)
    return lax.psum(value, axis)


def half_reduce(value, axis):
    count = lax.axis_size(axis)
    if count == 2:
        index = lax.axis_index(axis)
        halves = value.reshape((2, value.shape[0] // 2) + value.shape[1:])
        keep = lax.dynamic_index_in_dim(halves, index, 0, keepdims=False)
        send = lax.dynamic_index_in_dim(halves, 1 - index, 0, keepdims=False)
        return keep + shifted(send, axis, 1)
    return lax.psum_scatter(value, axis, scatter_dimension=0, tiled=True)


def slot_reduce(value):
    if lax.axis_size("win") != 2 or lax.axis_size("freq") != 2:
        return half_reduce(half_reduce(value, "freq"), "win")
    axes = ("win", "freq")
    own = lax.axis_index("win") * 2 + lax.axis_index("freq")
    slots = value.reshape((4, value.shape[0] // 4) + value.shape[1:])
    total = lax.dynamic_index_in_dim(slots, own, 0, keepdims=False)
    for mask in (1, 2, 3):
        send = lax.dynamic_index_in_dim(slots, own ^ mask, 0, keepdims=False)
        pairs = [(source, source ^ mask) for source in range(4)]
        total = total + lax.ppermute(send, axes, pairs)
    return total


def lag_table(first_bin, bin_count):
    lag_numbers = (jnp.arange(NLAG, dtype=jnp.int32) - NLAG // 2) * LAG_STRIDE
    lag_steps = (lag_numbers + SAMPLES) % SAMPLES
    split = 32 if bin_count % 32 == 0 else 1
    fine_bins = first_bin + 1 + jnp.arange(split, dtype=jnp.int32)
    coarse_bins = jnp.arange(bin_count // split, dtype=jnp.int32) * split
    scale = 2.0 * math.pi / SAMPLES
    fine = (fine_bins[:, None] * lag_steps[None, :]) % SAMPLES
    coarse = (coarse_bins[:, None] * lag_steps[None, :]) % SAMPLES
    fine_angle = fine.astype(jnp.float32) * scale
    coarse_angle = coarse.astype(jnp.float32) * scale
    fine_cos, fine_sin = jnp.cos(fine_angle)[None], jnp.sin(fine_angle)[None]
    coarse_cos, coarse_sin = jnp.cos(coarse_angle)[:, None], jnp.sin(coarse_angle)[:, None]
    cosine = coarse_cos * fine_cos - coarse_sin * fine_sin
    sine = coarse_sin * fine_cos + coarse_cos * fine_sin
    table = jnp.stack([cosine, -sine]).reshape(2, bin_count, NLAG)
    return table.astype(jnp.bfloat16)


def select_rows(block, rows):
    channel_ids = jnp.arange(block.shape[0], dtype=rows.dtype)
    one_hot = (rows[:, None] == channel_ids[None, :]).astype(block.dtype)
    return jnp.dot(one_hot, block, preferred_element_type=jnp.float32)


def whiten(raw, scales):
    real_in = raw[:, :, 0].astype(jnp.float32)
    imag_in = raw[:, :, 1].astype(jnp.float32)
    energy = real_in * real_in + imag_in * imag_in
    factor = scales[:, :, 1:2] / jnp.sqrt(energy + scales[:, :, 0:1] + 1e-06)
    whitened = jnp.concatenate([real_in * factor, imag_in * factor], axis=-1)
    return whitened.astype(jnp.bfloat16)


def body(spectra, live_mask, pair_rows, owner_map):
    channels, windows, _, bin_count = spectra.shape
    block_count = lax.axis_size("blk")
    offsets = block_count // 2 + 1
    own_block = lax.axis_index("blk")
    halves = 2 if channels % 16 == 0 else 1
    half_rows = channels // halves
    raw_halves = [spectra[index * half_rows:(index + 1) * half_rows] for index in range(halves)]
    next_raw = [shifted(half, "blk", -1) for half in raw_halves] if offsets > 1 else raw_halves
    real_in = spectra[:, :, 0].astype(jnp.float32)
    imag_in = spectra[:, :, 1].astype(jnp.float32)
    energy = real_in * real_in + imag_in * imag_in
    power_sums = pair_sum(jnp.sum(energy, axis=-1), "freq")
    all_bins = bin_count * lax.axis_size("freq")
    mean_power = power_sums / all_bins
    scales = jnp.stack([mean_power, live_mask.astype(jnp.float32)], axis=-1)
    scale_pool = [scales] + [shifted(scales, "blk", -step) for step in range(1, offsets)]
    whitened = whiten(spectra, scales)
    first_bin, whitened = lax.optimization_barrier((lax.axis_index("freq") * bin_count, whitened))
    lag_basis = lag_table(first_bin, bin_count).reshape(2 * bin_count, NLAG)
    lag_basis = jnp.tile(lag_basis, (windows, 1))
    pair_lists = pair_rows[own_block]
    win_count = lax.axis_size("win")
    freq_count = lax.axis_size("freq")
    row_count = pair_rows.shape[-1]
    source_flat = whitened.reshape(channels, windows * 2 * bin_count)
    current = whitened
    reduced = []
    for offset in range(offsets):
        partner_flat = current.reshape(channels, windows * 2 * bin_count)
        source_rows = select_rows(source_flat, pair_lists[offset, 0])
        partner_rows = select_rows(partner_flat, pair_lists[offset, 1])
        source_rows = source_rows.reshape(row_count, windows, 2 * bin_count)
        partner_rows = partner_rows.reshape(row_count, windows, 2 * bin_count)
        source_real = source_rows[..., :bin_count]
        source_imag = source_rows[..., bin_count:]
        partner_real = partner_rows[..., :bin_count]
        partner_imag = partner_rows[..., bin_count:]
        cross_real = source_real * partner_real + source_imag * partner_imag
        cross_imag = source_imag * partner_real - source_real * partner_imag
        cross = jnp.concatenate([cross_real, cross_imag], axis=-1).astype(jnp.bfloat16)
        cross = cross.reshape(row_count, windows * 2 * bin_count)
        correlated = jnp.dot(cross, lag_basis, preferred_element_type=jnp.float32)
        if offset + 2 < offsets:
            correlated, first_half = lax.optimization_barrier((correlated, next_raw[0]))
            forwarded = [shifted(first_half, "blk", -1)]
            received = [first_half]
            for half in next_raw[1:]:
                forwarded.append(shifted(half, "blk", -1))
                received.append(half)
            next_raw = forwarded
            raw_block = jnp.concatenate(received, axis=0) if halves > 1 else received[0]
            current = whiten(raw_block, scale_pool[offset + 1])
            correlated, current = lax.optimization_barrier((correlated, current))
        elif offset + 1 < offsets:
            raw_block = jnp.concatenate(next_raw, axis=0) if halves > 1 else next_raw[0]
            current = whiten(raw_block, scale_pool[offset + 1])
        reduced.append(slot_reduce(correlated))
    all_windows = windows * win_count
    scale = 1.0 / math.sqrt(all_bins * all_windows)
    own_owners = owner_map[own_block]
    if block_count > 4:
        summed = jnp.stack(reduced, axis=1)
        stacked = (summed * scale).astype(jnp.bfloat16)
        selector = (
            own_owners[None, :] == jnp.arange(block_count, dtype=jnp.int32)[:, None]
        ).astype(jnp.bfloat16)
        send_buffer = jnp.einsum(
            "ok,pkl->opl", selector, stacked, preferred_element_type=jnp.float32
        ).astype(jnp.bfloat16)
        received = lax.all_to_all(send_buffer, "blk", split_axis=0, concat_axis=0, tiled=True)
        return received[None]
    targets = (own_block + jnp.arange(block_count, dtype=jnp.int32)) % block_count
    masks = (own_owners[:, None] == targets[None, :]).astype(jnp.float32)
    send_buffer = None
    for offset, result in enumerate(reduced):
        stacked = (result * scale).astype(jnp.bfloat16).astype(jnp.float32)
        term = masks[offset][:, None, None] * stacked[None]
        send_buffer = term if send_buffer is None else send_buffer + term
    send_buffer = send_buffer.astype(jnp.bfloat16)
    parts = [send_buffer[0]]
    for distance in range(1, block_count):
        parts.append(shifted(send_buffer[distance], "blk", distance))
    reversed_parts = [parts[(-index) % block_count] for index in range(block_count)]
    doubled = jnp.stack(reversed_parts + reversed_parts)
    received = lax.dynamic_slice_in_dim(doubled, block_count - own_block, block_count)
    return received[None]


def solution(mesh):
    return jax.shard_map(
        body,
        mesh=mesh,
        in_specs=(
            P(("grp", "blk"), "win", None, "freq"),
            P(("grp", "blk"), "win"),
            P("grp", None, None, None),
            P("grp", None),
        ),
        out_specs=P(("grp", "blk"), None, ("win", "freq"), None),
        check_vma=False,
    )
```

```python
import math

import jax
import jax.numpy as jnp
from jax import lax
from jax.sharding import PartitionSpec as P

NLAG = 512
SAMPLES = 12000
LAG_STRIDE = 3


def shifted(value, axis, steps):
    count = lax.axis_size(axis)
    pairs = [(source, (source + steps) % count) for source in range(count)]
    return lax.ppermute(value, axis, pairs)


def pair_sum(value, axis):
    if lax.axis_size(axis) == 2:
        return value + shifted(value, axis, 1)
    return lax.psum(value, axis)


def half_reduce(value, axis):
    count = lax.axis_size(axis)
    if count == 2:
        index = lax.axis_index(axis)
        halves = value.reshape((2, value.shape[0] // 2) + value.shape[1:])
        keep = lax.dynamic_index_in_dim(halves, index, 0, keepdims=False)
        send = lax.dynamic_index_in_dim(halves, 1 - index, 0, keepdims=False)
        return keep + shifted(send, axis, 1)
    return lax.psum_scatter(value, axis, scatter_dimension=0, tiled=True)


def slot_reduce(value):
    if lax.axis_size("win") != 2 or lax.axis_size("freq") != 2:
        return half_reduce(half_reduce(value, "freq"), "win")
    axes = ("win", "freq")
    own = lax.axis_index("win") * 2 + lax.axis_index("freq")
    slots = value.reshape((4, value.shape[0] // 4) + value.shape[1:])
    total = lax.dynamic_index_in_dim(slots, own, 0, keepdims=False)
    for mask in (3, 2, 1):
        send = lax.dynamic_index_in_dim(slots, own ^ mask, 0, keepdims=False)
        pairs = [(source, source ^ mask) for source in range(4)]
        total = total + lax.ppermute(send, axes, pairs)
    return total


def lag_table(first_bin, bin_count):
    lag_numbers = (jnp.arange(NLAG, dtype=jnp.int32) - NLAG // 2) * LAG_STRIDE
    lag_steps = (lag_numbers + SAMPLES) % SAMPLES
    split = 32 if bin_count % 32 == 0 else 1
    fine_bins = first_bin + 1 + jnp.arange(split, dtype=jnp.int32)
    coarse_bins = jnp.arange(bin_count // split, dtype=jnp.int32) * split
    scale = 2.0 * math.pi / SAMPLES
    fine = (fine_bins[:, None] * lag_steps[None, :]) % SAMPLES
    coarse = (coarse_bins[:, None] * lag_steps[None, :]) % SAMPLES
    fine_angle = fine.astype(jnp.float32) * scale
    coarse_angle = coarse.astype(jnp.float32) * scale
    fine_cos, fine_sin = jnp.cos(fine_angle)[None], jnp.sin(fine_angle)[None]
    coarse_cos, coarse_sin = jnp.cos(coarse_angle)[:, None], jnp.sin(coarse_angle)[:, None]
    cosine = coarse_cos * fine_cos - coarse_sin * fine_sin
    sine = coarse_sin * fine_cos + coarse_cos * fine_sin
    table = jnp.stack([cosine, -sine]).reshape(2, bin_count, NLAG)
    return table.astype(jnp.bfloat16)


def select_rows(block, rows):
    channel_ids = jnp.arange(block.shape[0], dtype=rows.dtype)
    one_hot = (rows[:, None] == channel_ids[None, :]).astype(block.dtype)
    return jnp.dot(one_hot, block, preferred_element_type=jnp.float32)


def whiten(raw, scales):
    real_in = raw[:, :, 0].astype(jnp.float32)
    imag_in = raw[:, :, 1].astype(jnp.float32)
    energy = real_in * real_in + imag_in * imag_in
    factor = scales[:, :, 1:2] / jnp.sqrt(energy + scales[:, :, 0:1] + 1e-06)
    whitened = jnp.concatenate([real_in * factor, imag_in * factor], axis=-1)
    return whitened.astype(jnp.bfloat16)


def body(spectra, live_mask, pair_rows, owner_map):
    channels, windows, _, bin_count = spectra.shape
    block_count = lax.axis_size("blk")
    offsets = block_count // 2 + 1
    own_block = lax.axis_index("blk")
    next_raw = shifted(spectra, "blk", -1) if offsets > 1 else spectra
    real_in = spectra[:, :, 0].astype(jnp.float32)
    imag_in = spectra[:, :, 1].astype(jnp.float32)
    energy = real_in * real_in + imag_in * imag_in
    power_sums = pair_sum(jnp.sum(energy, axis=-1), "freq")
    all_bins = bin_count * lax.axis_size("freq")
    mean_power = power_sums / all_bins
    scales = jnp.stack([mean_power, live_mask.astype(jnp.float32)], axis=-1)
    scale_pool = [scales] + [shifted(scales, "blk", -step) for step in range(1, offsets)]
    whitened = whiten(spectra, scales)
    first_bin, whitened = lax.optimization_barrier((lax.axis_index("freq") * bin_count, whitened))
    lag_basis = lag_table(first_bin, bin_count).reshape(2 * bin_count, NLAG)
    lag_basis = jnp.tile(lag_basis, (windows, 1))
    pair_lists = pair_rows[own_block]
    win_count = lax.axis_size("win")
    freq_count = lax.axis_size("freq")
    row_count = pair_rows.shape[-1]
    source_flat = whitened.reshape(channels, windows * 2 * bin_count)
    current = whitened
    reduced = []
    for offset in range(offsets):
        partner_flat = current.reshape(channels, windows * 2 * bin_count)
        source_rows = select_rows(source_flat, pair_lists[offset, 0])
        partner_rows = select_rows(partner_flat, pair_lists[offset, 1])
        source_rows = source_rows.reshape(row_count, windows, 2 * bin_count)
        partner_rows = partner_rows.reshape(row_count, windows, 2 * bin_count)
        source_real = source_rows[..., :bin_count]
        source_imag = source_rows[..., bin_count:]
        partner_real = partner_rows[..., :bin_count]
        partner_imag = partner_rows[..., bin_count:]
        cross_real = source_real * partner_real + source_imag * partner_imag
        cross_imag = source_imag * partner_real - source_real * partner_imag
        cross = jnp.concatenate([cross_real, cross_imag], axis=-1).astype(jnp.bfloat16)
        cross = cross.reshape(row_count, windows * 2 * bin_count)
        correlated = jnp.dot(cross, lag_basis, preferred_element_type=jnp.float32)
        if offset + 2 < offsets:
            correlated, raw_block = lax.optimization_barrier((correlated, next_raw))
            next_raw = shifted(raw_block, "blk", -1)
            current = whiten(raw_block, scale_pool[offset + 1])
            correlated, current = lax.optimization_barrier((correlated, current))
        elif offset + 1 < offsets:
            current = whiten(next_raw, scale_pool[offset + 1])
        reduced.append(slot_reduce(correlated))
    all_windows = windows * win_count
    scale = 1.0 / math.sqrt(all_bins * all_windows)
    own_owners = owner_map[own_block]
    if block_count > 4:
        summed = jnp.stack(reduced, axis=1)
        stacked = (summed * scale).astype(jnp.bfloat16)
        selector = (
            own_owners[None, :] == jnp.arange(block_count, dtype=jnp.int32)[:, None]
        ).astype(jnp.bfloat16)
        send_buffer = jnp.einsum(
            "ok,pkl->opl", selector, stacked, preferred_element_type=jnp.float32
        ).astype(jnp.bfloat16)
        received = lax.all_to_all(send_buffer, "blk", split_axis=0, concat_axis=0, tiled=True)
        return received[None]
    targets = (own_block + jnp.arange(block_count, dtype=jnp.int32)) % block_count
    masks = (own_owners[:, None] == targets[None, :]).astype(jnp.float32)
    send_buffer = None
    for offset, result in enumerate(reduced):
        stacked = (result * scale).astype(jnp.bfloat16).astype(jnp.float32)
        term = masks[offset][:, None, None] * stacked[None]
        send_buffer = term if send_buffer is None else send_buffer + term
    send_buffer = send_buffer.astype(jnp.bfloat16)
    parts = [send_buffer[0]]
    for distance in range(1, block_count):
        parts.append(shifted(send_buffer[distance], "blk", distance))
    reversed_parts = [parts[(-index) % block_count] for index in range(block_count)]
    doubled = jnp.stack(reversed_parts + reversed_parts)
    received = lax.dynamic_slice_in_dim(doubled, block_count - own_block, block_count)
    return received[None]


def solution(mesh):
    return jax.shard_map(
        body,
        mesh=mesh,
        in_specs=(
            P(("grp", "blk"), "win", None, "freq"),
            P(("grp", "blk"), "win"),
            P("grp", None, None, None),
            P("grp", None),
        ),
        out_specs=P(("grp", "blk"), None, ("win", "freq"), None),
        check_vma=False,
    )
```

```python
import math

import jax
import jax.numpy as jnp
from jax import lax
from jax.sharding import PartitionSpec as P

NLAG = 512
SAMPLES = 12000
LAG_STRIDE = 3


def shifted(value, axis, steps):
    count = lax.axis_size(axis)
    pairs = [(source, (source + steps) % count) for source in range(count)]
    return lax.ppermute(value, axis, pairs)


def pair_sum(value, axis):
    if lax.axis_size(axis) == 2:
        return value + shifted(value, axis, 1)
    return lax.psum(value, axis)


def half_reduce(value, axis):
    count = lax.axis_size(axis)
    if count == 2:
        index = lax.axis_index(axis)
        halves = value.reshape((2, value.shape[0] // 2) + value.shape[1:])
        keep = lax.dynamic_index_in_dim(halves, index, 0, keepdims=False)
        send = lax.dynamic_index_in_dim(halves, 1 - index, 0, keepdims=False)
        return keep + shifted(send, axis, 1)
    return lax.psum_scatter(value, axis, scatter_dimension=0, tiled=True)


def slot_reduce(value):
    if lax.axis_size("win") != 2 or lax.axis_size("freq") != 2:
        return half_reduce(half_reduce(value, "freq"), "win")
    axes = ("win", "freq")
    own = lax.axis_index("win") * 2 + lax.axis_index("freq")
    slots = value.reshape((4, value.shape[0] // 4) + value.shape[1:])
    total = lax.dynamic_index_in_dim(slots, own, 0, keepdims=False)
    for mask in (1, 2, 3):
        send = lax.dynamic_index_in_dim(slots, own ^ mask, 0, keepdims=False)
        pairs = [(source, source ^ mask) for source in range(4)]
        received = lax.ppermute(send.astype(jnp.bfloat16), axes, pairs)
        total = total + received.astype(jnp.float32)
    return total


def lag_table(first_bin, bin_count):
    lag_numbers = (jnp.arange(NLAG, dtype=jnp.int32) - NLAG // 2) * LAG_STRIDE
    lag_steps = (lag_numbers + SAMPLES) % SAMPLES
    split = 32 if bin_count % 32 == 0 else 1
    fine_bins = first_bin + 1 + jnp.arange(split, dtype=jnp.int32)
    coarse_bins = jnp.arange(bin_count // split, dtype=jnp.int32) * split
    scale = 2.0 * math.pi / SAMPLES
    fine = (fine_bins[:, None] * lag_steps[None, :]) % SAMPLES
    coarse = (coarse_bins[:, None] * lag_steps[None, :]) % SAMPLES
    fine_angle = fine.astype(jnp.float32) * scale
    coarse_angle = coarse.astype(jnp.float32) * scale
    fine_cos, fine_sin = jnp.cos(fine_angle)[None], jnp.sin(fine_angle)[None]
    coarse_cos, coarse_sin = jnp.cos(coarse_angle)[:, None], jnp.sin(coarse_angle)[:, None]
    cosine = coarse_cos * fine_cos - coarse_sin * fine_sin
    sine = coarse_sin * fine_cos + coarse_cos * fine_sin
    table = jnp.stack([cosine, -sine]).reshape(2, bin_count, NLAG)
    return table.astype(jnp.bfloat16)


def select_rows(block, rows):
    channel_ids = jnp.arange(block.shape[0], dtype=rows.dtype)
    one_hot = (rows[:, None] == channel_ids[None, :]).astype(block.dtype)
    return jnp.dot(one_hot, block, preferred_element_type=jnp.float32)


def whiten(raw, scales):
    real_in = raw[:, :, 0].astype(jnp.float32)
    imag_in = raw[:, :, 1].astype(jnp.float32)
    energy = real_in * real_in + imag_in * imag_in
    factor = scales[:, :, 1:2] / jnp.sqrt(energy + scales[:, :, 0:1] + 1e-06)
    whitened = jnp.concatenate([real_in * factor, imag_in * factor], axis=-1)
    return whitened.astype(jnp.bfloat16)


def body(spectra, live_mask, pair_rows, owner_map):
    channels, windows, _, bin_count = spectra.shape
    block_count = lax.axis_size("blk")
    offsets = block_count // 2 + 1
    own_block = lax.axis_index("blk")
    next_raw = shifted(spectra, "blk", -1) if offsets > 1 else spectra
    real_in = spectra[:, :, 0].astype(jnp.float32)
    imag_in = spectra[:, :, 1].astype(jnp.float32)
    energy = real_in * real_in + imag_in * imag_in
    power_sums = pair_sum(jnp.sum(energy, axis=-1), "freq")
    all_bins = bin_count * lax.axis_size("freq")
    mean_power = power_sums / all_bins
    scales = jnp.stack([mean_power, live_mask.astype(jnp.float32)], axis=-1)
    scale_pool = [scales] + [shifted(scales, "blk", -step) for step in range(1, offsets)]
    whitened = whiten(spectra, scales)
    first_bin, whitened = lax.optimization_barrier((lax.axis_index("freq") * bin_count, whitened))
    lag_basis = lag_table(first_bin, bin_count).reshape(2 * bin_count, NLAG)
    lag_basis = jnp.tile(lag_basis, (windows, 1))
    pair_lists = pair_rows[own_block]
    win_count = lax.axis_size("win")
    freq_count = lax.axis_size("freq")
    row_count = pair_rows.shape[-1]
    source_flat = whitened.reshape(channels, windows * 2 * bin_count)
    current = whitened
    reduced = []
    for offset in range(offsets):
        partner_flat = current.reshape(channels, windows * 2 * bin_count)
        source_rows = select_rows(source_flat, pair_lists[offset, 0])
        partner_rows = select_rows(partner_flat, pair_lists[offset, 1])
        source_rows = source_rows.reshape(row_count, windows, 2 * bin_count)
        partner_rows = partner_rows.reshape(row_count, windows, 2 * bin_count)
        source_real = source_rows[..., :bin_count]
        source_imag = source_rows[..., bin_count:]
        partner_real = partner_rows[..., :bin_count]
        partner_imag = partner_rows[..., bin_count:]
        cross_real = source_real * partner_real + source_imag * partner_imag
        cross_imag = source_imag * partner_real - source_real * partner_imag
        cross = jnp.concatenate([cross_real, cross_imag], axis=-1).astype(jnp.bfloat16)
        cross = cross.reshape(row_count, windows * 2 * bin_count)
        correlated = jnp.dot(cross, lag_basis, preferred_element_type=jnp.float32)
        if offset + 2 < offsets:
            correlated, raw_block = lax.optimization_barrier((correlated, next_raw))
            next_raw = shifted(raw_block, "blk", -1)
            current = whiten(raw_block, scale_pool[offset + 1])
            correlated, current = lax.optimization_barrier((correlated, current))
        elif offset + 1 < offsets:
            current = whiten(next_raw, scale_pool[offset + 1])
        reduced.append(slot_reduce(correlated))
    all_windows = windows * win_count
    scale = 1.0 / math.sqrt(all_bins * all_windows)
    own_owners = owner_map[own_block]
    if block_count > 4:
        summed = jnp.stack(reduced, axis=1)
        stacked = (summed * scale).astype(jnp.bfloat16)
        selector = (
            own_owners[None, :] == jnp.arange(block_count, dtype=jnp.int32)[:, None]
        ).astype(jnp.bfloat16)
        send_buffer = jnp.einsum(
            "ok,pkl->opl", selector, stacked, preferred_element_type=jnp.float32
        ).astype(jnp.bfloat16)
        received = lax.all_to_all(send_buffer, "blk", split_axis=0, concat_axis=0, tiled=True)
        return received[None]
    targets = (own_block + jnp.arange(block_count, dtype=jnp.int32)) % block_count
    masks = (own_owners[:, None] == targets[None, :]).astype(jnp.float32)
    send_buffer = None
    for offset, result in enumerate(reduced):
        stacked = (result * scale).astype(jnp.bfloat16).astype(jnp.float32)
        term = masks[offset][:, None, None] * stacked[None]
        send_buffer = term if send_buffer is None else send_buffer + term
    send_buffer = send_buffer.astype(jnp.bfloat16)
    parts = [send_buffer[0]]
    for distance in range(1, block_count):
        parts.append(shifted(send_buffer[distance], "blk", distance))
    reversed_parts = [parts[(-index) % block_count] for index in range(block_count)]
    doubled = jnp.stack(reversed_parts + reversed_parts)
    received = lax.dynamic_slice_in_dim(doubled, block_count - own_block, block_count)
    return received[None]


def solution(mesh):
    return jax.shard_map(
        body,
        mesh=mesh,
        in_specs=(
            P(("grp", "blk"), "win", None, "freq"),
            P(("grp", "blk"), "win"),
            P("grp", None, None, None),
            P("grp", None),
        ),
        out_specs=P(("grp", "blk"), None, ("win", "freq"), None),
        check_vma=False,
    )
```

```python
import math

import jax
import jax.numpy as jnp
from jax import lax
from jax.sharding import PartitionSpec as P

NLAG = 512
SAMPLES = 12000
LAG_STRIDE = 3


def shifted(value, axis, steps):
    count = lax.axis_size(axis)
    pairs = [(source, (source + steps) % count) for source in range(count)]
    return lax.ppermute(value, axis, pairs)


def chain_shift(value, axis):
    count = lax.axis_size(axis)
    if count < 4:
        return shifted(value, axis, -1)
    inner = lax.ppermute(value, axis, [(source, source - 1) for source in range(1, count)])
    wrap = lax.ppermute(value, axis, [(0, count - 1)])
    return lax.select(lax.axis_index(axis) == count - 1, wrap, inner)


def pair_sum(value, axis):
    if lax.axis_size(axis) == 2:
        return value + shifted(value, axis, 1)
    return lax.psum(value, axis)


def half_reduce(value, axis):
    count = lax.axis_size(axis)
    if count == 2:
        index = lax.axis_index(axis)
        halves = value.reshape((2, value.shape[0] // 2) + value.shape[1:])
        keep = lax.dynamic_index_in_dim(halves, index, 0, keepdims=False)
        send = lax.dynamic_index_in_dim(halves, 1 - index, 0, keepdims=False)
        return keep + shifted(send, axis, 1)
    return lax.psum_scatter(value, axis, scatter_dimension=0, tiled=True)


def slot_reduce(value):
    if lax.axis_size("win") != 2 or lax.axis_size("freq") != 2:
        return half_reduce(half_reduce(value, "freq"), "win")
    axes = ("win", "freq")
    own = lax.axis_index("win") * 2 + lax.axis_index("freq")
    slots = value.reshape((4, value.shape[0] // 4) + value.shape[1:])
    total = lax.dynamic_index_in_dim(slots, own, 0, keepdims=False)
    for mask in (1, 2, 3):
        send = lax.dynamic_index_in_dim(slots, own ^ mask, 0, keepdims=False)
        pairs = [(source, source ^ mask) for source in range(4)]
        total = total + lax.ppermute(send, axes, pairs)
    return total


def lag_table(first_bin, bin_count):
    lag_numbers = (jnp.arange(NLAG, dtype=jnp.int32) - NLAG // 2) * LAG_STRIDE
    lag_steps = (lag_numbers + SAMPLES) % SAMPLES
    split = 32 if bin_count % 32 == 0 else 1
    fine_bins = first_bin + 1 + jnp.arange(split, dtype=jnp.int32)
    coarse_bins = jnp.arange(bin_count // split, dtype=jnp.int32) * split
    scale = 2.0 * math.pi / SAMPLES
    fine = (fine_bins[:, None] * lag_steps[None, :]) % SAMPLES
    coarse = (coarse_bins[:, None] * lag_steps[None, :]) % SAMPLES
    fine_angle = fine.astype(jnp.float32) * scale
    coarse_angle = coarse.astype(jnp.float32) * scale
    fine_cos, fine_sin = jnp.cos(fine_angle)[None], jnp.sin(fine_angle)[None]
    coarse_cos, coarse_sin = jnp.cos(coarse_angle)[:, None], jnp.sin(coarse_angle)[:, None]
    cosine = coarse_cos * fine_cos - coarse_sin * fine_sin
    sine = coarse_sin * fine_cos + coarse_cos * fine_sin
    table = jnp.stack([cosine, -sine]).reshape(2, bin_count, NLAG)
    return table.astype(jnp.bfloat16)


def select_rows(block, rows):
    channel_ids = jnp.arange(block.shape[0], dtype=rows.dtype)
    one_hot = (rows[:, None] == channel_ids[None, :]).astype(block.dtype)
    return jnp.dot(one_hot, block, preferred_element_type=jnp.float32)


def whiten(raw, scales):
    real_in = raw[:, :, 0].astype(jnp.float32)
    imag_in = raw[:, :, 1].astype(jnp.float32)
    energy = real_in * real_in + imag_in * imag_in
    factor = scales[:, :, 1:2] / jnp.sqrt(energy + scales[:, :, 0:1] + 1e-06)
    whitened = jnp.concatenate([real_in * factor, imag_in * factor], axis=-1)
    return whitened.astype(jnp.bfloat16)


def body(spectra, live_mask, pair_rows, owner_map):
    channels, windows, _, bin_count = spectra.shape
    block_count = lax.axis_size("blk")
    offsets = block_count // 2 + 1
    own_block = lax.axis_index("blk")
    next_raw = chain_shift(spectra, "blk") if offsets > 1 else spectra
    real_in = spectra[:, :, 0].astype(jnp.float32)
    imag_in = spectra[:, :, 1].astype(jnp.float32)
    energy = real_in * real_in + imag_in * imag_in
    power_sums = pair_sum(jnp.sum(energy, axis=-1), "freq")
    all_bins = bin_count * lax.axis_size("freq")
    mean_power = power_sums / all_bins
    scales = jnp.stack([mean_power, live_mask.astype(jnp.float32)], axis=-1)
    scale_pool = [scales] + [shifted(scales, "blk", -step) for step in range(1, offsets)]
    whitened = whiten(spectra, scales)
    first_bin, whitened = lax.optimization_barrier((lax.axis_index("freq") * bin_count, whitened))
    lag_basis = lag_table(first_bin, bin_count).reshape(2 * bin_count, NLAG)
    lag_basis = jnp.tile(lag_basis, (windows, 1))
    pair_lists = pair_rows[own_block]
    win_count = lax.axis_size("win")
    freq_count = lax.axis_size("freq")
    row_count = pair_rows.shape[-1]
    source_flat = whitened.reshape(channels, windows * 2 * bin_count)
    current = whitened
    reduced = []
    for offset in range(offsets):
        partner_flat = current.reshape(channels, windows * 2 * bin_count)
        source_rows = select_rows(source_flat, pair_lists[offset, 0])
        partner_rows = select_rows(partner_flat, pair_lists[offset, 1])
        source_rows = source_rows.reshape(row_count, windows, 2 * bin_count)
        partner_rows = partner_rows.reshape(row_count, windows, 2 * bin_count)
        source_real = source_rows[..., :bin_count]
        source_imag = source_rows[..., bin_count:]
        partner_real = partner_rows[..., :bin_count]
        partner_imag = partner_rows[..., bin_count:]
        cross_real = source_real * partner_real + source_imag * partner_imag
        cross_imag = source_imag * partner_real - source_real * partner_imag
        cross = jnp.concatenate([cross_real, cross_imag], axis=-1).astype(jnp.bfloat16)
        cross = cross.reshape(row_count, windows * 2 * bin_count)
        correlated = jnp.dot(cross, lag_basis, preferred_element_type=jnp.float32)
        if offset + 2 < offsets:
            correlated, raw_block = lax.optimization_barrier((correlated, next_raw))
            next_raw = chain_shift(raw_block, "blk")
            current = whiten(raw_block, scale_pool[offset + 1])
            correlated, current = lax.optimization_barrier((correlated, current))
        elif offset + 1 < offsets:
            current = whiten(next_raw, scale_pool[offset + 1])
        reduced.append(slot_reduce(correlated))
    all_windows = windows * win_count
    scale = 1.0 / math.sqrt(all_bins * all_windows)
    own_owners = owner_map[own_block]
    if block_count > 4:
        summed = jnp.stack(reduced, axis=1)
        stacked = (summed * scale).astype(jnp.bfloat16)
        selector = (
            own_owners[None, :] == jnp.arange(block_count, dtype=jnp.int32)[:, None]
        ).astype(jnp.bfloat16)
        send_buffer = jnp.einsum(
            "ok,pkl->opl", selector, stacked, preferred_element_type=jnp.float32
        ).astype(jnp.bfloat16)
        received = lax.all_to_all(send_buffer, "blk", split_axis=0, concat_axis=0, tiled=True)
        return received[None]
    targets = (own_block + jnp.arange(block_count, dtype=jnp.int32)) % block_count
    masks = (own_owners[:, None] == targets[None, :]).astype(jnp.float32)
    send_buffer = None
    for offset, result in enumerate(reduced):
        stacked = (result * scale).astype(jnp.bfloat16).astype(jnp.float32)
        term = masks[offset][:, None, None] * stacked[None]
        send_buffer = term if send_buffer is None else send_buffer + term
    send_buffer = send_buffer.astype(jnp.bfloat16)
    parts = [send_buffer[0]]
    for distance in range(1, block_count):
        parts.append(shifted(send_buffer[distance], "blk", distance))
    reversed_parts = [parts[(-index) % block_count] for index in range(block_count)]
    doubled = jnp.stack(reversed_parts + reversed_parts)
    received = lax.dynamic_slice_in_dim(doubled, block_count - own_block, block_count)
    return received[None]


def solution(mesh):
    return jax.shard_map(
        body,
        mesh=mesh,
        in_specs=(
            P(("grp", "blk"), "win", None, "freq"),
            P(("grp", "blk"), "win"),
            P("grp", None, None, None),
            P("grp", None),
        ),
        out_specs=P(("grp", "blk"), None, ("win", "freq"), None),
        check_vma=False,
    )
```

```python
import math

import jax
import jax.numpy as jnp
from jax import lax
from jax.sharding import PartitionSpec as P

NLAG = 512
SAMPLES = 12000
LAG_STRIDE = 3


def shifted(value, axis, steps):
    count = lax.axis_size(axis)
    pairs = [(source, (source + steps) % count) for source in range(count)]
    return lax.ppermute(value, axis, pairs)


def pair_sum(value, axis):
    if lax.axis_size(axis) == 2:
        return value + shifted(value, axis, 1)
    return lax.psum(value, axis)


def half_reduce(value, axis):
    count = lax.axis_size(axis)
    if count == 2:
        index = lax.axis_index(axis)
        halves = value.reshape((2, value.shape[0] // 2) + value.shape[1:])
        keep = lax.dynamic_index_in_dim(halves, index, 0, keepdims=False)
        send = lax.dynamic_index_in_dim(halves, 1 - index, 0, keepdims=False)
        return keep + shifted(send, axis, 1)
    return lax.psum_scatter(value, axis, scatter_dimension=0, tiled=True)


def slot_reduce(value):
    if lax.axis_size("win") != 2 or lax.axis_size("freq") != 2:
        return half_reduce(half_reduce(value, "freq"), "win")
    axes = ("win", "freq")
    own = lax.axis_index("win") * 2 + lax.axis_index("freq")
    slots = value.reshape((4, value.shape[0] // 4) + value.shape[1:])
    total = lax.dynamic_index_in_dim(slots, own, 0, keepdims=False)
    for mask in (1, 2, 3):
        send = lax.dynamic_index_in_dim(slots, own ^ mask, 0, keepdims=False)
        pairs = [(source, source ^ mask) for source in range(4)]
        total = total + lax.ppermute(send, axes, pairs)
    return total


def lag_table(first_bin, bin_count):
    lag_numbers = (jnp.arange(NLAG, dtype=jnp.int32) - NLAG // 2) * LAG_STRIDE
    lag_steps = (lag_numbers + SAMPLES) % SAMPLES
    split = 32 if bin_count % 32 == 0 else 1
    fine_bins = first_bin + 1 + jnp.arange(split, dtype=jnp.int32)
    coarse_bins = jnp.arange(bin_count // split, dtype=jnp.int32) * split
    scale = 2.0 * math.pi / SAMPLES
    fine = (fine_bins[:, None] * lag_steps[None, :]) % SAMPLES
    coarse = (coarse_bins[:, None] * lag_steps[None, :]) % SAMPLES
    fine_angle = fine.astype(jnp.float32) * scale
    coarse_angle = coarse.astype(jnp.float32) * scale
    fine_cos, fine_sin = jnp.cos(fine_angle)[None], jnp.sin(fine_angle)[None]
    coarse_cos, coarse_sin = jnp.cos(coarse_angle)[:, None], jnp.sin(coarse_angle)[:, None]
    cosine = coarse_cos * fine_cos - coarse_sin * fine_sin
    sine = coarse_sin * fine_cos + coarse_cos * fine_sin
    table = jnp.stack([cosine, -sine]).reshape(2, bin_count, NLAG)
    return table.astype(jnp.bfloat16)


def select_rows(block, rows):
    channel_ids = jnp.arange(block.shape[0], dtype=rows.dtype)
    one_hot = (rows[:, None] == channel_ids[None, :]).astype(block.dtype)
    return jnp.dot(one_hot, block, preferred_element_type=jnp.float32)


def whiten(raw, scales):
    real_in = raw[:, :, 0].astype(jnp.float32)
    imag_in = raw[:, :, 1].astype(jnp.float32)
    energy = real_in * real_in + imag_in * imag_in
    factor = scales[:, :, 1:2] / jnp.sqrt(energy + scales[:, :, 0:1] + 1e-06)
    whitened = jnp.concatenate([real_in * factor, imag_in * factor], axis=-1)
    return whitened.astype(jnp.bfloat16)


def body(spectra, live_mask, pair_rows, owner_map):
    channels, windows, _, bin_count = spectra.shape
    block_count = lax.axis_size("blk")
    offsets = block_count // 2 + 1
    own_block = lax.axis_index("blk")
    next_raw = shifted(spectra, "blk", -1) if offsets > 1 else spectra
    real_in = spectra[:, :, 0].astype(jnp.float32)
    imag_in = spectra[:, :, 1].astype(jnp.float32)
    energy = real_in * real_in + imag_in * imag_in
    power_sums = pair_sum(jnp.sum(energy, axis=-1), "freq")
    all_bins = bin_count * lax.axis_size("freq")
    mean_power = power_sums / all_bins
    scales = jnp.stack([mean_power, live_mask.astype(jnp.float32)], axis=-1)
    scale_pool = [scales] + [shifted(scales, "blk", -step) for step in range(1, offsets)]
    whitened = whiten(spectra, scales)
    first_bin, whitened = lax.optimization_barrier((lax.axis_index("freq") * bin_count, whitened))
    lag_basis = lag_table(first_bin, bin_count).reshape(2 * bin_count, NLAG)
    lag_basis = jnp.tile(lag_basis, (windows, 1))
    pair_lists = pair_rows[own_block]
    win_count = lax.axis_size("win")
    freq_count = lax.axis_size("freq")
    row_count = pair_rows.shape[-1]
    source_flat = whitened.reshape(channels, windows * 2 * bin_count)
    current = whitened
    reduced = []
    for offset in range(offsets):
        partner_flat = current.reshape(channels, windows * 2 * bin_count)
        source_rows = select_rows(source_flat, pair_lists[offset, 0])
        partner_rows = select_rows(partner_flat, pair_lists[offset, 1])
        source_rows = source_rows.reshape(row_count, windows, 2 * bin_count)
        partner_rows = partner_rows.reshape(row_count, windows, 2 * bin_count)
        source_real = source_rows[..., :bin_count]
        source_imag = source_rows[..., bin_count:]
        partner_real = partner_rows[..., :bin_count]
        partner_imag = partner_rows[..., bin_count:]
        cross_real = source_real * partner_real + source_imag * partner_imag
        cross_imag = source_imag * partner_real - source_real * partner_imag
        cross = jnp.concatenate([cross_real, cross_imag], axis=-1).astype(jnp.bfloat16)
        cross = cross.reshape(row_count, windows * 2 * bin_count)
        correlated = jnp.dot(cross, lag_basis, preferred_element_type=jnp.float32)
        if offset + 2 < offsets:
            correlated, raw_block = lax.optimization_barrier((correlated, next_raw))
            next_raw = shifted(raw_block, "blk", -1)
            current = whiten(raw_block, scale_pool[offset + 1])
            correlated, current = lax.optimization_barrier((correlated, current))
        elif offset + 1 < offsets:
            current = whiten(next_raw, scale_pool[offset + 1])
        reduced.append(slot_reduce(correlated))
    all_windows = windows * win_count
    scale = 1.0 / math.sqrt(all_bins * all_windows)
    own_owners = owner_map[own_block]
    if block_count > 4:
        summed = jnp.stack(reduced, axis=1)
        stacked = (summed * scale).astype(jnp.bfloat16)
        selector = (
            own_owners[None, :] == jnp.arange(block_count, dtype=jnp.int32)[:, None]
        ).astype(jnp.bfloat16)
        send_buffer = jnp.einsum(
            "ok,pkl->opl", selector, stacked, preferred_element_type=jnp.float32
        ).astype(jnp.bfloat16)
        received = lax.all_to_all(send_buffer, "blk", split_axis=0, concat_axis=0, tiled=True)
        return received[None]
    targets = (own_block + jnp.arange(block_count, dtype=jnp.int32)) % block_count
    masks = (own_owners[:, None] == targets[None, :]).astype(jnp.float32)
    send_buffer = None
    for offset, result in enumerate(reduced):
        stacked = (result * scale).astype(jnp.bfloat16).astype(jnp.float32)
        term = masks[offset][:, None, None] * stacked[None]
        send_buffer = term if send_buffer is None else send_buffer + term
    send_buffer = send_buffer.astype(jnp.bfloat16)
    parts = [send_buffer[0]]
    for distance in range(1, block_count):
        parts.append(shifted(send_buffer[distance], "blk", distance))
    sources = (own_block - jnp.arange(block_count, dtype=jnp.int32)) % block_count
    placement = (sources[None, :] == jnp.arange(block_count, dtype=jnp.int32)[:, None])
    flat_parts = jnp.stack(parts).reshape(block_count, -1)
    received = jnp.dot(
        placement.astype(jnp.bfloat16), flat_parts, preferred_element_type=jnp.float32
    ).astype(jnp.bfloat16)
    return received.reshape(send_buffer.shape)[None]


def solution(mesh):
    return jax.shard_map(
        body,
        mesh=mesh,
        in_specs=(
            P(("grp", "blk"), "win", None, "freq"),
            P(("grp", "blk"), "win"),
            P("grp", None, None, None),
            P("grp", None),
        ),
        out_specs=P(("grp", "blk"), None, ("win", "freq"), None),
        check_vma=False,
    )
```

```python
import math

import jax
import jax.numpy as jnp
from jax import lax
from jax.sharding import PartitionSpec as P

NLAG = 512
SAMPLES = 12000
LAG_STRIDE = 3


def shifted(value, axis, steps):
    count = lax.axis_size(axis)
    pairs = [(source, (source + steps) % count) for source in range(count)]
    return lax.ppermute(value, axis, pairs)


def pair_sum(value, axis):
    if lax.axis_size(axis) == 2:
        return value + shifted(value, axis, 1)
    return lax.psum(value, axis)


def half_reduce(value, axis):
    count = lax.axis_size(axis)
    if count == 2:
        index = lax.axis_index(axis)
        halves = value.reshape((2, value.shape[0] // 2) + value.shape[1:])
        keep = lax.dynamic_index_in_dim(halves, index, 0, keepdims=False)
        send = lax.dynamic_index_in_dim(halves, 1 - index, 0, keepdims=False)
        return keep + shifted(send, axis, 1)
    return lax.psum_scatter(value, axis, scatter_dimension=0, tiled=True)


def slot_reduce(value):
    if lax.axis_size("win") != 2 or lax.axis_size("freq") != 2:
        return half_reduce(half_reduce(value, "freq"), "win")
    axes = ("win", "freq")
    own = lax.axis_index("win") * 2 + lax.axis_index("freq")
    slots = value.reshape((4, value.shape[0] // 4) + value.shape[1:])
    total = lax.dynamic_index_in_dim(slots, own, 0, keepdims=False)
    for mask in (1, 2, 3):
        send = lax.dynamic_index_in_dim(slots, own ^ mask, 0, keepdims=False)
        pairs = [(source, source ^ mask) for source in range(4)]
        total = total + lax.ppermute(send, axes, pairs)
    return total


def lag_table(first_bin, bin_count):
    lag_numbers = (jnp.arange(NLAG, dtype=jnp.int32) - NLAG // 2) * LAG_STRIDE
    lag_steps = (lag_numbers + SAMPLES) % SAMPLES
    split = 32 if bin_count % 32 == 0 else 1
    fine_bins = first_bin + 1 + jnp.arange(split, dtype=jnp.int32)
    coarse_bins = jnp.arange(bin_count // split, dtype=jnp.int32) * split
    scale = 2.0 * math.pi / SAMPLES
    fine = (fine_bins[:, None] * lag_steps[None, :]) % SAMPLES
    coarse = (coarse_bins[:, None] * lag_steps[None, :]) % SAMPLES
    fine_angle = fine.astype(jnp.float32) * scale
    coarse_angle = coarse.astype(jnp.float32) * scale
    fine_cos, fine_sin = jnp.cos(fine_angle)[None], jnp.sin(fine_angle)[None]
    coarse_cos, coarse_sin = jnp.cos(coarse_angle)[:, None], jnp.sin(coarse_angle)[:, None]
    cosine = coarse_cos * fine_cos - coarse_sin * fine_sin
    sine = coarse_sin * fine_cos + coarse_cos * fine_sin
    table = jnp.stack([cosine, -sine]).reshape(2, bin_count, NLAG)
    return table.astype(jnp.bfloat16)


def select_rows(block, rows):
    channel_ids = jnp.arange(block.shape[0], dtype=rows.dtype)
    one_hot = (rows[:, None] == channel_ids[None, :]).astype(block.dtype)
    return jnp.dot(one_hot, block, preferred_element_type=jnp.float32)


def whiten(raw, scales):
    real_in = raw[:, :, 0].astype(jnp.float32)
    imag_in = raw[:, :, 1].astype(jnp.float32)
    energy = real_in * real_in + imag_in * imag_in
    factor = scales[:, :, 1:2] / jnp.sqrt(energy + scales[:, :, 0:1] + 1e-06)
    whitened = jnp.concatenate([real_in * factor, imag_in * factor], axis=-1)
    return whitened.astype(jnp.bfloat16)


def body(spectra, live_mask, pair_rows, owner_map):
    channels, windows, _, bin_count = spectra.shape
    block_count = lax.axis_size("blk")
    offsets = block_count // 2 + 1
    own_block = lax.axis_index("blk")
    next_raw = shifted(spectra, "blk", -1) if offsets > 1 else spectra
    real_in = spectra[:, :, 0].astype(jnp.float32)
    imag_in = spectra[:, :, 1].astype(jnp.float32)
    energy = real_in * real_in + imag_in * imag_in
    power_sums = pair_sum(jnp.sum(energy, axis=-1), "freq")
    all_bins = bin_count * lax.axis_size("freq")
    mean_power = power_sums / all_bins
    scales = jnp.stack([mean_power, live_mask.astype(jnp.float32)], axis=-1)
    scale_pool = [scales] + [shifted(scales, "blk", -step) for step in range(1, offsets)]
    whitened = whiten(spectra, scales)
    first_bin, whitened = lax.optimization_barrier((lax.axis_index("freq") * bin_count, whitened))
    lag_basis = lag_table(first_bin, bin_count).reshape(2 * bin_count, NLAG)
    lag_basis = jnp.tile(lag_basis, (windows, 1))
    pair_lists = pair_rows[own_block]
    win_count = lax.axis_size("win")
    freq_count = lax.axis_size("freq")
    row_count = pair_rows.shape[-1]
    source_flat = whitened.reshape(channels, windows * 2 * bin_count)
    current = whitened
    reduced = []
    for offset in range(offsets):
        partner_flat = current.reshape(channels, windows * 2 * bin_count)
        source_rows = select_rows(source_flat, pair_lists[offset, 0])
        partner_rows = select_rows(partner_flat, pair_lists[offset, 1])
        source_rows = source_rows.reshape(row_count, windows, 2 * bin_count)
        partner_rows = partner_rows.reshape(row_count, windows, 2 * bin_count)
        source_real = source_rows[..., :bin_count]
        source_imag = source_rows[..., bin_count:]
        partner_real = partner_rows[..., :bin_count]
        partner_imag = partner_rows[..., bin_count:]
        cross_real = source_real * partner_real + source_imag * partner_imag
        cross_imag = source_imag * partner_real - source_real * partner_imag
        cross = jnp.concatenate([cross_real, cross_imag], axis=-1).astype(jnp.bfloat16)
        cross = cross.reshape(row_count, windows * 2 * bin_count)
        correlated = jnp.dot(cross, lag_basis, preferred_element_type=jnp.float32)
        if offset + 2 < offsets:
            correlated, raw_block = lax.optimization_barrier((correlated, next_raw))
            next_raw = shifted(raw_block, "blk", -1)
            current = whiten(raw_block, scale_pool[offset + 1])
            correlated, current = lax.optimization_barrier((correlated, current))
        elif offset + 1 < offsets:
            current = whiten(next_raw, scale_pool[offset + 1])
        reduced.append(slot_reduce(correlated))
    all_windows = windows * win_count
    scale = 1.0 / math.sqrt(all_bins * all_windows)
    own_owners = owner_map[own_block]
    if block_count > 4:
        summed = jnp.stack(reduced, axis=1)
        stacked = (summed * scale).astype(jnp.bfloat16)
        selector = (
            own_owners[None, :] == jnp.arange(block_count, dtype=jnp.int32)[:, None]
        ).astype(jnp.bfloat16)
        send_buffer = jnp.einsum(
            "ok,pkl->opl", selector, stacked, preferred_element_type=jnp.float32
        ).astype(jnp.bfloat16)
        received = lax.all_to_all(send_buffer, "blk", split_axis=0, concat_axis=0, tiled=True)
        return received[None]
    targets = (own_block + jnp.arange(block_count, dtype=jnp.int32)) % block_count
    masks = (own_owners[:, None] == targets[None, :]).astype(jnp.float32)
    send_buffer = None
    for offset, result in enumerate(reduced):
        stacked = (result * scale).astype(jnp.bfloat16).astype(jnp.float32).reshape(-1)
        term = masks[offset][:, None] * stacked[None]
        send_buffer = term if send_buffer is None else send_buffer + term
    send_buffer = send_buffer.astype(jnp.bfloat16)
    parts = [send_buffer[0]]
    for distance in range(1, block_count):
        parts.append(shifted(send_buffer[distance], "blk", distance))
    sources = (own_block - jnp.arange(block_count, dtype=jnp.int32)) % block_count
    placement = (sources[None, :] == jnp.arange(block_count, dtype=jnp.int32)[:, None])
    flat_parts = jnp.stack(parts).reshape(block_count, -1)
    received = jnp.dot(
        placement.astype(jnp.bfloat16), flat_parts, preferred_element_type=jnp.float32
    ).astype(jnp.bfloat16)
    return received.reshape((block_count,) + reduced[0].shape)[None]


def solution(mesh):
    return jax.shard_map(
        body,
        mesh=mesh,
        in_specs=(
            P(("grp", "blk"), "win", None, "freq"),
            P(("grp", "blk"), "win"),
            P("grp", None, None, None),
            P("grp", None),
        ),
        out_specs=P(("grp", "blk"), None, ("win", "freq"), None),
        check_vma=False,
    )
```

```python
import math

import jax
import jax.numpy as jnp
from jax import lax
from jax.sharding import PartitionSpec as P

NLAG = 512
SAMPLES = 12000
LAG_STRIDE = 3


def shifted(value, axis, steps):
    count = lax.axis_size(axis)
    pairs = [(source, (source + steps) % count) for source in range(count)]
    return lax.ppermute(value, axis, pairs)


def pair_sum(value, axis):
    if lax.axis_size(axis) == 2:
        return value + shifted(value, axis, 1)
    return lax.psum(value, axis)


def half_reduce(value, axis):
    count = lax.axis_size(axis)
    if count == 2:
        index = lax.axis_index(axis)
        halves = value.reshape((2, value.shape[0] // 2) + value.shape[1:])
        keep = lax.dynamic_index_in_dim(halves, index, 0, keepdims=False)
        send = lax.dynamic_index_in_dim(halves, 1 - index, 0, keepdims=False)
        return keep + shifted(send, axis, 1)
    return lax.psum_scatter(value, axis, scatter_dimension=0, tiled=True)


def slot_reduce(value):
    if lax.axis_size("win") != 2 or lax.axis_size("freq") != 2:
        return half_reduce(half_reduce(value, "freq"), "win")
    axes = ("win", "freq")
    own = lax.axis_index("win") * 2 + lax.axis_index("freq")
    slots = value.reshape((4, value.shape[0] // 4) + value.shape[1:])
    total = lax.dynamic_index_in_dim(slots, own, 0, keepdims=False)
    for mask in (1, 2, 3):
        send = lax.dynamic_index_in_dim(slots, own ^ mask, 0, keepdims=False)
        pairs = [(source, source ^ mask) for source in range(4)]
        total = total + lax.ppermute(send, axes, pairs)
    return total


def lag_table(first_bin, bin_count):
    lag_numbers = (jnp.arange(NLAG, dtype=jnp.int32) - NLAG // 2) * LAG_STRIDE
    lag_steps = (lag_numbers + SAMPLES) % SAMPLES
    split = 32 if bin_count % 32 == 0 else 1
    fine_bins = first_bin + 1 + jnp.arange(split, dtype=jnp.int32)
    coarse_bins = jnp.arange(bin_count // split, dtype=jnp.int32) * split
    scale = 2.0 * math.pi / SAMPLES
    fine = (fine_bins[:, None] * lag_steps[None, :]) % SAMPLES
    coarse = (coarse_bins[:, None] * lag_steps[None, :]) % SAMPLES
    fine_angle = fine.astype(jnp.float32) * scale
    coarse_angle = coarse.astype(jnp.float32) * scale
    fine_cos, fine_sin = jnp.cos(fine_angle)[None], jnp.sin(fine_angle)[None]
    coarse_cos, coarse_sin = jnp.cos(coarse_angle)[:, None], jnp.sin(coarse_angle)[:, None]
    cosine = coarse_cos * fine_cos - coarse_sin * fine_sin
    sine = coarse_sin * fine_cos + coarse_cos * fine_sin
    table = jnp.stack([cosine, -sine]).reshape(2, bin_count, NLAG)
    return table.astype(jnp.bfloat16)


def select_rows(block, rows):
    channel_ids = jnp.arange(block.shape[0], dtype=rows.dtype)
    one_hot = (rows[:, None] == channel_ids[None, :]).astype(block.dtype)
    return jnp.dot(one_hot, block, preferred_element_type=jnp.float32)


def whiten(raw, scales):
    real_in = raw[:, :, 0].astype(jnp.float32)
    imag_in = raw[:, :, 1].astype(jnp.float32)
    energy = real_in * real_in + imag_in * imag_in
    factor = scales[:, :, 1:2] / jnp.sqrt(energy + scales[:, :, 0:1] + 1e-06)
    whitened = jnp.concatenate([real_in * factor, imag_in * factor], axis=-1)
    return whitened.astype(jnp.bfloat16)


def body(spectra, live_mask, pair_rows, owner_map):
    channels, windows, _, bin_count = spectra.shape
    block_count = lax.axis_size("blk")
    offsets = block_count // 2 + 1
    own_block = lax.axis_index("blk")
    next_raw = shifted(spectra, "blk", -1) if offsets > 1 else spectra
    real_in = spectra[:, :, 0].astype(jnp.float32)
    imag_in = spectra[:, :, 1].astype(jnp.float32)
    energy = real_in * real_in + imag_in * imag_in
    power_sums = pair_sum(jnp.sum(energy, axis=-1), "freq")
    all_bins = bin_count * lax.axis_size("freq")
    mean_power = power_sums / all_bins
    scales = jnp.stack([mean_power, live_mask.astype(jnp.float32)], axis=-1)
    scale_pool = [scales] + [shifted(scales, "blk", -step) for step in range(1, offsets)]
    whitened = whiten(spectra, scales)
    first_bin, whitened = lax.optimization_barrier((lax.axis_index("freq") * bin_count, whitened))
    lag_basis = lag_table(first_bin, bin_count).reshape(2 * bin_count, NLAG)
    lag_basis = jnp.tile(lag_basis, (windows, 1))
    pair_lists = pair_rows[own_block]
    win_count = lax.axis_size("win")
    freq_count = lax.axis_size("freq")
    row_count = pair_rows.shape[-1]
    source_flat = whitened.reshape(channels, windows * 2 * bin_count)
    current = whitened
    reduced = []
    for offset in range(offsets):
        partner_flat = current.reshape(channels, windows * 2 * bin_count)
        source_rows = select_rows(source_flat, pair_lists[offset, 0])
        partner_rows = select_rows(partner_flat, pair_lists[offset, 1])
        source_rows = source_rows.reshape(row_count, windows, 2 * bin_count)
        partner_rows = partner_rows.reshape(row_count, windows, 2 * bin_count)
        source_real = source_rows[..., :bin_count]
        source_imag = source_rows[..., bin_count:]
        partner_real = partner_rows[..., :bin_count]
        partner_imag = partner_rows[..., bin_count:]
        cross_real = source_real * partner_real + source_imag * partner_imag
        cross_imag = source_imag * partner_real - source_real * partner_imag
        cross = jnp.concatenate([cross_real, cross_imag], axis=-1).astype(jnp.bfloat16)
        cross = cross.reshape(row_count, windows * 2 * bin_count)
        correlated = jnp.dot(cross, lag_basis, preferred_element_type=jnp.float32)
        if offset + 2 < offsets:
            correlated, raw_block = lax.optimization_barrier((correlated, next_raw))
            next_raw = shifted(raw_block, "blk", -1)
            current = whiten(raw_block, scale_pool[offset + 1])
            correlated, current = lax.optimization_barrier((correlated, current))
        elif offset + 1 < offsets:
            current = whiten(next_raw, scale_pool[offset + 1])
        reduced.append(slot_reduce(correlated))
    all_windows = windows * win_count
    scale = 1.0 / math.sqrt(all_bins * all_windows)
    own_owners = owner_map[own_block]
    if block_count > 4:
        summed = jnp.stack(reduced, axis=1)
        stacked = (summed * scale).astype(jnp.bfloat16)
        selector = (
            own_owners[None, :] == jnp.arange(block_count, dtype=jnp.int32)[:, None]
        ).astype(jnp.bfloat16)
        send_buffer = jnp.einsum(
            "ok,pkl->opl", selector, stacked, preferred_element_type=jnp.float32
        ).astype(jnp.bfloat16)
        received = lax.all_to_all(send_buffer, "blk", split_axis=0, concat_axis=0, tiled=True)
        return received[None]
    targets = (own_block + jnp.arange(block_count, dtype=jnp.int32)) % block_count
    masks = (own_owners[:, None] == targets[None, :]).astype(jnp.float32)
    send_buffer = None
    for offset, result in enumerate(reduced):
        stacked = (result * scale).astype(jnp.bfloat16).astype(jnp.float32)
        term = masks[offset][:, None, None] * stacked[None]
        send_buffer = term if send_buffer is None else send_buffer + term
    send_buffer = send_buffer.astype(jnp.bfloat16)
    parts = [send_buffer[0]]
    for distance in range(1, block_count):
        parts.append(shifted(send_buffer[distance], "blk", distance))
    sources = (own_block - jnp.arange(block_count, dtype=jnp.int32)) % block_count
    placement = (sources[None, :] == jnp.arange(block_count, dtype=jnp.int32)[:, None])
    weights = placement.astype(jnp.float32)
    received = None
    for distance, part in enumerate(parts):
        term = weights[:, distance][:, None, None] * part.astype(jnp.float32)[None]
        received = term if received is None else received + term
    return received.astype(jnp.bfloat16)[None]


def solution(mesh):
    return jax.shard_map(
        body,
        mesh=mesh,
        in_specs=(
            P(("grp", "blk"), "win", None, "freq"),
            P(("grp", "blk"), "win"),
            P("grp", None, None, None),
            P("grp", None),
        ),
        out_specs=P(("grp", "blk"), None, ("win", "freq"), None),
        check_vma=False,
    )
```

```python
import math

import jax
import jax.numpy as jnp
from jax import lax
from jax.sharding import PartitionSpec as P

NLAG = 512
SAMPLES = 12000
LAG_STRIDE = 3


def shifted(value, axis, steps):
    count = lax.axis_size(axis)
    pairs = [(source, (source + steps) % count) for source in range(count)]
    return lax.ppermute(value, axis, pairs)


def pair_sum(value, axis):
    if lax.axis_size(axis) == 2:
        return value + shifted(value, axis, 1)
    return lax.psum(value, axis)


def half_reduce(value, axis):
    count = lax.axis_size(axis)
    if count == 2:
        index = lax.axis_index(axis)
        halves = value.reshape((2, value.shape[0] // 2) + value.shape[1:])
        keep = lax.dynamic_index_in_dim(halves, index, 0, keepdims=False)
        send = lax.dynamic_index_in_dim(halves, 1 - index, 0, keepdims=False)
        return keep + shifted(send, axis, 1)
    return lax.psum_scatter(value, axis, scatter_dimension=0, tiled=True)


def slot_reduce(value):
    if lax.axis_size("win") != 2 or lax.axis_size("freq") != 2:
        return half_reduce(half_reduce(value, "freq"), "win")
    axes = ("win", "freq")
    own = lax.axis_index("win") * 2 + lax.axis_index("freq")
    slots = value.reshape((4, value.shape[0] // 4) + value.shape[1:])
    total = lax.dynamic_index_in_dim(slots, own, 0, keepdims=False)
    for mask in (1, 2, 3):
        send = lax.dynamic_index_in_dim(slots, own ^ mask, 0, keepdims=False)
        pairs = [(source, source ^ mask) for source in range(4)]
        total = total + lax.ppermute(send, axes, pairs)
    return total


def lag_table(first_bin, bin_count):
    lag_numbers = (jnp.arange(NLAG, dtype=jnp.int32) - NLAG // 2) * LAG_STRIDE
    lag_steps = (lag_numbers + SAMPLES) % SAMPLES
    split = 32 if bin_count % 32 == 0 else 1
    fine_bins = first_bin + 1 + jnp.arange(split, dtype=jnp.int32)
    coarse_bins = jnp.arange(bin_count // split, dtype=jnp.int32) * split
    scale = 2.0 * math.pi / SAMPLES
    fine = (fine_bins[:, None] * lag_steps[None, :]) % SAMPLES
    coarse = (coarse_bins[:, None] * lag_steps[None, :]) % SAMPLES
    fine_angle = fine.astype(jnp.float32) * scale
    coarse_angle = coarse.astype(jnp.float32) * scale
    fine_cos, fine_sin = jnp.cos(fine_angle)[None], jnp.sin(fine_angle)[None]
    coarse_cos, coarse_sin = jnp.cos(coarse_angle)[:, None], jnp.sin(coarse_angle)[:, None]
    cosine = coarse_cos * fine_cos - coarse_sin * fine_sin
    sine = coarse_sin * fine_cos + coarse_cos * fine_sin
    table = jnp.stack([cosine, -sine]).reshape(2, bin_count, NLAG)
    return table.astype(jnp.bfloat16)


def select_rows(block, rows):
    channel_ids = jnp.arange(block.shape[0], dtype=rows.dtype)
    one_hot = (rows[:, None] == channel_ids[None, :]).astype(block.dtype)
    return jnp.dot(one_hot, block, preferred_element_type=jnp.float32)


def correlate(source_flat, partner_flat, rows_s, rows_t, lag_basis, bin_count):
    source_rows = select_rows(source_flat, rows_s)
    partner_rows = select_rows(partner_flat, rows_t)
    width = source_rows.shape[-1]
    source_rows = source_rows.reshape(rows_s.shape[0], -1, 2 * bin_count)
    partner_rows = partner_rows.reshape(rows_t.shape[0], -1, 2 * bin_count)
    source_real = source_rows[..., :bin_count]
    source_imag = source_rows[..., bin_count:]
    partner_real = partner_rows[..., :bin_count]
    partner_imag = partner_rows[..., bin_count:]
    cross_real = source_real * partner_real + source_imag * partner_imag
    cross_imag = source_imag * partner_real - source_real * partner_imag
    cross = jnp.concatenate([cross_real, cross_imag], axis=-1).astype(jnp.bfloat16)
    cross = cross.reshape(rows_s.shape[0], width)
    return jnp.dot(cross, lag_basis, preferred_element_type=jnp.float32)


def whiten(raw, scales):
    real_in = raw[:, :, 0].astype(jnp.float32)
    imag_in = raw[:, :, 1].astype(jnp.float32)
    energy = real_in * real_in + imag_in * imag_in
    factor = scales[:, :, 1:2] / jnp.sqrt(energy + scales[:, :, 0:1] + 1e-06)
    whitened = jnp.concatenate([real_in * factor, imag_in * factor], axis=-1)
    return whitened.astype(jnp.bfloat16)


def body(spectra, live_mask, pair_rows, owner_map):
    channels, windows, _, bin_count = spectra.shape
    block_count = lax.axis_size("blk")
    offsets = block_count // 2 + 1
    own_block = lax.axis_index("blk")
    next_raw = shifted(spectra, "blk", -1) if offsets > 1 else spectra
    real_in = spectra[:, :, 0].astype(jnp.float32)
    imag_in = spectra[:, :, 1].astype(jnp.float32)
    energy = real_in * real_in + imag_in * imag_in
    power_sums = pair_sum(jnp.sum(energy, axis=-1), "freq")
    all_bins = bin_count * lax.axis_size("freq")
    mean_power = power_sums / all_bins
    scales = jnp.stack([mean_power, live_mask.astype(jnp.float32)], axis=-1)
    scale_pool = [scales] + [shifted(scales, "blk", -step) for step in range(1, offsets)]
    whitened = whiten(spectra, scales)
    first_bin, whitened = lax.optimization_barrier((lax.axis_index("freq") * bin_count, whitened))
    lag_basis = lag_table(first_bin, bin_count).reshape(2 * bin_count, NLAG)
    lag_basis = jnp.tile(lag_basis, (windows, 1))
    pair_lists = pair_rows[own_block]
    win_count = lax.axis_size("win")
    freq_count = lax.axis_size("freq")
    row_count = pair_rows.shape[-1]
    source_flat = whitened.reshape(channels, windows * 2 * bin_count)
    current = whitened
    reduced = []
    sliced = win_count == 2 and freq_count == 2 and row_count % 4 == 0
    for offset in range(offsets):
        partner_flat = current.reshape(channels, windows * 2 * bin_count)
        if sliced and offset == offsets - 1:
            slot_rows = row_count // 4
            own_slot = lax.axis_index("win") * 2 + lax.axis_index("freq")
            total = None
            for mask in (3, 2, 1, 0):
                start = (own_slot ^ mask) * slot_rows
                rows_s = lax.dynamic_slice_in_dim(pair_lists[offset, 0], start, slot_rows)
                rows_t = lax.dynamic_slice_in_dim(pair_lists[offset, 1], start, slot_rows)
                part = correlate(source_flat, partner_flat, rows_s, rows_t, lag_basis, bin_count)
                if mask:
                    pairs = [(source, source ^ mask) for source in range(4)]
                    part = lax.ppermute(part, ("win", "freq"), pairs)
                total = part if total is None else total + part
            reduced.append(total)
            break
        correlated = correlate(
            source_flat, partner_flat, pair_lists[offset, 0], pair_lists[offset, 1],
            lag_basis, bin_count,
        )
        if offset + 2 < offsets:
            correlated, raw_block = lax.optimization_barrier((correlated, next_raw))
            next_raw = shifted(raw_block, "blk", -1)
            current = whiten(raw_block, scale_pool[offset + 1])
            correlated, current = lax.optimization_barrier((correlated, current))
        elif offset + 1 < offsets:
            current = whiten(next_raw, scale_pool[offset + 1])
        reduced.append(slot_reduce(correlated))
    all_windows = windows * win_count
    scale = 1.0 / math.sqrt(all_bins * all_windows)
    own_owners = owner_map[own_block]
    if block_count > 4:
        summed = jnp.stack(reduced, axis=1)
        stacked = (summed * scale).astype(jnp.bfloat16)
        selector = (
            own_owners[None, :] == jnp.arange(block_count, dtype=jnp.int32)[:, None]
        ).astype(jnp.bfloat16)
        send_buffer = jnp.einsum(
            "ok,pkl->opl", selector, stacked, preferred_element_type=jnp.float32
        ).astype(jnp.bfloat16)
        received = lax.all_to_all(send_buffer, "blk", split_axis=0, concat_axis=0, tiled=True)
        return received[None]
    targets = (own_block + jnp.arange(block_count, dtype=jnp.int32)) % block_count
    masks = (own_owners[:, None] == targets[None, :]).astype(jnp.float32)
    send_buffer = None
    for offset, result in enumerate(reduced):
        stacked = (result * scale).astype(jnp.bfloat16).astype(jnp.float32)
        term = masks[offset][:, None, None] * stacked[None]
        send_buffer = term if send_buffer is None else send_buffer + term
    send_buffer = send_buffer.astype(jnp.bfloat16)
    parts = [send_buffer[0]]
    for distance in range(1, block_count):
        parts.append(shifted(send_buffer[distance], "blk", distance))
    sources = (own_block - jnp.arange(block_count, dtype=jnp.int32)) % block_count
    placement = (sources[None, :] == jnp.arange(block_count, dtype=jnp.int32)[:, None])
    flat_parts = jnp.stack(parts).reshape(block_count, -1)
    received = jnp.dot(
        placement.astype(jnp.bfloat16), flat_parts, preferred_element_type=jnp.float32
    ).astype(jnp.bfloat16)
    return received.reshape(send_buffer.shape)[None]


def solution(mesh):
    return jax.shard_map(
        body,
        mesh=mesh,
        in_specs=(
            P(("grp", "blk"), "win", None, "freq"),
            P(("grp", "blk"), "win"),
            P("grp", None, None, None),
            P("grp", None),
        ),
        out_specs=P(("grp", "blk"), None, ("win", "freq"), None),
        check_vma=False,
    )
```

```python
import math

import jax
import jax.numpy as jnp
from jax import lax
from jax.sharding import PartitionSpec as P

NLAG = 512
SAMPLES = 12000
LAG_STRIDE = 3


def shifted(value, axis, steps):
    count = lax.axis_size(axis)
    pairs = [(source, (source + steps) % count) for source in range(count)]
    return lax.ppermute(value, axis, pairs)


def pair_sum(value, axis):
    if lax.axis_size(axis) == 2:
        return value + shifted(value, axis, 1)
    return lax.psum(value, axis)


def half_reduce(value, axis):
    count = lax.axis_size(axis)
    if count == 2:
        index = lax.axis_index(axis)
        halves = value.reshape((2, value.shape[0] // 2) + value.shape[1:])
        keep = lax.dynamic_index_in_dim(halves, index, 0, keepdims=False)
        send = lax.dynamic_index_in_dim(halves, 1 - index, 0, keepdims=False)
        return keep + shifted(send, axis, 1)
    return lax.psum_scatter(value, axis, scatter_dimension=0, tiled=True)


def slot_reduce(value):
    if lax.axis_size("win") != 2 or lax.axis_size("freq") != 2:
        return half_reduce(half_reduce(value, "freq"), "win")
    axes = ("win", "freq")
    own = lax.axis_index("win") * 2 + lax.axis_index("freq")
    slots = value.reshape((4, value.shape[0] // 4) + value.shape[1:])
    total = lax.dynamic_index_in_dim(slots, own, 0, keepdims=False)
    for mask in (1, 2, 3):
        send = lax.dynamic_index_in_dim(slots, own ^ mask, 0, keepdims=False)
        pairs = [(source, source ^ mask) for source in range(4)]
        total = total + lax.ppermute(send, axes, pairs)
    return total


def lag_table(first_bin, bin_count):
    lag_numbers = (jnp.arange(NLAG, dtype=jnp.int32) - NLAG // 2) * LAG_STRIDE
    lag_steps = (lag_numbers + SAMPLES) % SAMPLES
    split = 32 if bin_count % 32 == 0 else 1
    fine_bins = first_bin + 1 + jnp.arange(split, dtype=jnp.int32)
    coarse_bins = jnp.arange(bin_count // split, dtype=jnp.int32) * split
    scale = 2.0 * math.pi / SAMPLES
    fine = (fine_bins[:, None] * lag_steps[None, :]) % SAMPLES
    coarse = (coarse_bins[:, None] * lag_steps[None, :]) % SAMPLES
    fine_angle = fine.astype(jnp.float32) * scale
    coarse_angle = coarse.astype(jnp.float32) * scale
    fine_cos, fine_sin = jnp.cos(fine_angle)[None], jnp.sin(fine_angle)[None]
    coarse_cos, coarse_sin = jnp.cos(coarse_angle)[:, None], jnp.sin(coarse_angle)[:, None]
    cosine = coarse_cos * fine_cos - coarse_sin * fine_sin
    sine = coarse_sin * fine_cos + coarse_cos * fine_sin
    table = jnp.stack([cosine, -sine]).reshape(2, bin_count, NLAG)
    return table.astype(jnp.bfloat16)


def select_rows(block, rows):
    channel_ids = jnp.arange(block.shape[0], dtype=rows.dtype)
    one_hot = (rows[:, None] == channel_ids[None, :]).astype(block.dtype)
    return jnp.dot(one_hot, block, preferred_element_type=jnp.float32)


def whiten(raw, scales):
    real_in = raw[:, :, 0].astype(jnp.float32)
    imag_in = raw[:, :, 1].astype(jnp.float32)
    energy = real_in * real_in + imag_in * imag_in
    factor = scales[:, :, 1:2] / jnp.sqrt(energy + scales[:, :, 0:1] + 1e-06)
    whitened = jnp.concatenate([real_in * factor, imag_in * factor], axis=-1)
    return whitened.astype(jnp.bfloat16)


def body(spectra, live_mask, pair_rows, owner_map):
    channels, windows, _, bin_count = spectra.shape
    block_count = lax.axis_size("blk")
    offsets = block_count // 2 + 1
    own_block = lax.axis_index("blk")
    next_raw = shifted(spectra, "blk", -1) if offsets > 1 else spectra
    real_in = spectra[:, :, 0].astype(jnp.float32)
    imag_in = spectra[:, :, 1].astype(jnp.float32)
    energy = real_in * real_in + imag_in * imag_in
    power_sums = pair_sum(jnp.sum(energy, axis=-1), "freq")
    all_bins = bin_count * lax.axis_size("freq")
    mean_power = power_sums / all_bins
    scales = jnp.stack([mean_power, live_mask.astype(jnp.float32)], axis=-1)
    scale_pool = [scales] + [shifted(scales, "blk", -step) for step in range(1, offsets)]
    whitened = whiten(spectra, scales)
    first_bin, whitened = lax.optimization_barrier((lax.axis_index("freq") * bin_count, whitened))
    lag_basis = lag_table(first_bin, bin_count).reshape(2 * bin_count, NLAG)
    lag_basis = jnp.tile(lag_basis, (windows, 1))
    pair_lists = pair_rows[own_block]
    win_count = lax.axis_size("win")
    freq_count = lax.axis_size("freq")
    row_count = pair_rows.shape[-1]
    source_flat = whitened.reshape(channels, windows * 2 * bin_count)
    current = whitened
    reduced = []
    for offset in range(offsets):
        partner_flat = current.reshape(channels, windows * 2 * bin_count)
        source_rows = select_rows(source_flat, pair_lists[offset, 0])
        partner_rows = select_rows(partner_flat, pair_lists[offset, 1])
        source_rows = source_rows.reshape(row_count, windows, 2 * bin_count)
        partner_rows = partner_rows.reshape(row_count, windows, 2 * bin_count)
        source_real = source_rows[..., :bin_count]
        source_imag = source_rows[..., bin_count:]
        partner_real = partner_rows[..., :bin_count]
        partner_imag = partner_rows[..., bin_count:]
        cross_real = source_real * partner_real + source_imag * partner_imag
        cross_imag = source_imag * partner_real - source_real * partner_imag
        cross = jnp.concatenate([cross_real, cross_imag], axis=-1).astype(jnp.bfloat16)
        cross = cross.reshape(row_count, windows * 2 * bin_count)
        correlated = jnp.dot(cross, lag_basis, preferred_element_type=jnp.float32)
        early = correlated
        if offset + 2 < offsets:
            reduced.append(slot_reduce(early))
            correlated, raw_block = lax.optimization_barrier((correlated, next_raw))
            next_raw = shifted(raw_block, "blk", -1)
            current = whiten(raw_block, scale_pool[offset + 1])
            correlated, current = lax.optimization_barrier((correlated, current))
            continue
        elif offset + 1 < offsets:
            current = whiten(next_raw, scale_pool[offset + 1])
        reduced.append(slot_reduce(correlated))
    all_windows = windows * win_count
    scale = 1.0 / math.sqrt(all_bins * all_windows)
    own_owners = owner_map[own_block]
    if block_count > 4:
        summed = jnp.stack(reduced, axis=1)
        stacked = (summed * scale).astype(jnp.bfloat16)
        selector = (
            own_owners[None, :] == jnp.arange(block_count, dtype=jnp.int32)[:, None]
        ).astype(jnp.bfloat16)
        send_buffer = jnp.einsum(
            "ok,pkl->opl", selector, stacked, preferred_element_type=jnp.float32
        ).astype(jnp.bfloat16)
        received = lax.all_to_all(send_buffer, "blk", split_axis=0, concat_axis=0, tiled=True)
        return received[None]
    targets = (own_block + jnp.arange(block_count, dtype=jnp.int32)) % block_count
    masks = (own_owners[:, None] == targets[None, :]).astype(jnp.float32)
    send_buffer = None
    for offset, result in enumerate(reduced):
        stacked = (result * scale).astype(jnp.bfloat16).astype(jnp.float32)
        term = masks[offset][:, None, None] * stacked[None]
        send_buffer = term if send_buffer is None else send_buffer + term
    send_buffer = send_buffer.astype(jnp.bfloat16)
    parts = [send_buffer[0]]
    for distance in range(1, block_count):
        parts.append(shifted(send_buffer[distance], "blk", distance))
    sources = (own_block - jnp.arange(block_count, dtype=jnp.int32)) % block_count
    placement = (sources[None, :] == jnp.arange(block_count, dtype=jnp.int32)[:, None])
    flat_parts = jnp.stack(parts).reshape(block_count, -1)
    received = jnp.dot(
        placement.astype(jnp.bfloat16), flat_parts, preferred_element_type=jnp.float32
    ).astype(jnp.bfloat16)
    return received.reshape(send_buffer.shape)[None]


def solution(mesh):
    return jax.shard_map(
        body,
        mesh=mesh,
        in_specs=(
            P(("grp", "blk"), "win", None, "freq"),
            P(("grp", "blk"), "win"),
            P("grp", None, None, None),
            P("grp", None),
        ),
        out_specs=P(("grp", "blk"), None, ("win", "freq"), None),
        check_vma=False,
    )
```

```python
import math

import jax
import jax.numpy as jnp
from jax import lax
from jax.sharding import PartitionSpec as P

NLAG = 512
SAMPLES = 12000
LAG_STRIDE = 3


def shifted(value, axis, steps):
    count = lax.axis_size(axis)
    pairs = [(source, (source + steps) % count) for source in range(count)]
    return lax.ppermute(value, axis, pairs)


def pair_sum(value, axis):
    if lax.axis_size(axis) == 2:
        return value + shifted(value, axis, 1)
    return lax.psum(value, axis)


def half_reduce(value, axis):
    count = lax.axis_size(axis)
    if count == 2:
        index = lax.axis_index(axis)
        halves = value.reshape((2, value.shape[0] // 2) + value.shape[1:])
        keep = lax.dynamic_index_in_dim(halves, index, 0, keepdims=False)
        send = lax.dynamic_index_in_dim(halves, 1 - index, 0, keepdims=False)
        return keep + shifted(send, axis, 1)
    return lax.psum_scatter(value, axis, scatter_dimension=0, tiled=True)


def slot_reduce(value):
    if lax.axis_size("win") != 2 or lax.axis_size("freq") != 2:
        return half_reduce(half_reduce(value, "freq"), "win")
    axes = ("win", "freq")
    own = lax.axis_index("win") * 2 + lax.axis_index("freq")
    slots = value.reshape((4, value.shape[0] // 4) + value.shape[1:])
    total = lax.dynamic_index_in_dim(slots, own, 0, keepdims=False)
    for mask in (1, 2, 3):
        send = lax.dynamic_index_in_dim(slots, own ^ mask, 0, keepdims=False)
        pairs = [(source, source ^ mask) for source in range(4)]
        total = total + lax.ppermute(send, axes, pairs)
    return total


def lag_table(first_bin, bin_count):
    lag_numbers = (jnp.arange(NLAG, dtype=jnp.int32) - NLAG // 2) * LAG_STRIDE
    lag_steps = (lag_numbers + SAMPLES) % SAMPLES
    split = 32 if bin_count % 32 == 0 else 1
    fine_bins = first_bin + 1 + jnp.arange(split, dtype=jnp.int32)
    coarse_bins = jnp.arange(bin_count // split, dtype=jnp.int32) * split
    scale = 2.0 * math.pi / SAMPLES
    fine = (fine_bins[:, None] * lag_steps[None, :]) % SAMPLES
    coarse = (coarse_bins[:, None] * lag_steps[None, :]) % SAMPLES
    fine_angle = fine.astype(jnp.float32) * scale
    coarse_angle = coarse.astype(jnp.float32) * scale
    fine_cos, fine_sin = jnp.cos(fine_angle)[None], jnp.sin(fine_angle)[None]
    coarse_cos, coarse_sin = jnp.cos(coarse_angle)[:, None], jnp.sin(coarse_angle)[:, None]
    cosine = coarse_cos * fine_cos - coarse_sin * fine_sin
    sine = coarse_sin * fine_cos + coarse_cos * fine_sin
    table = jnp.stack([cosine, -sine]).reshape(2, bin_count, NLAG)
    return table.astype(jnp.bfloat16)


def select_rows(block, rows):
    channel_ids = jnp.arange(block.shape[0], dtype=rows.dtype)
    one_hot = (rows[:, None] == channel_ids[None, :]).astype(block.dtype)
    return jnp.dot(one_hot, block, preferred_element_type=jnp.float32)


def whiten(raw, scales):
    real_in = raw[:, :, 0].astype(jnp.float32)
    imag_in = raw[:, :, 1].astype(jnp.float32)
    energy = real_in * real_in + imag_in * imag_in
    factor = scales[:, :, 1:2] / jnp.sqrt(energy + scales[:, :, 0:1] + 1e-06)
    whitened = jnp.concatenate([real_in * factor, imag_in * factor], axis=-1)
    return whitened.astype(jnp.bfloat16)


def body(spectra, live_mask, pair_rows, owner_map):
    channels, windows, _, bin_count = spectra.shape
    block_count = lax.axis_size("blk")
    offsets = block_count // 2 + 1
    own_block = lax.axis_index("blk")
    next_raw = shifted(spectra, "blk", -1) if offsets > 1 else spectra
    real_in = spectra[:, :, 0].astype(jnp.float32)
    imag_in = spectra[:, :, 1].astype(jnp.float32)
    energy = real_in * real_in + imag_in * imag_in
    power_sums = pair_sum(jnp.sum(energy, axis=-1), "freq")
    all_bins = bin_count * lax.axis_size("freq")
    mean_power = power_sums / all_bins
    scales = jnp.stack([mean_power, live_mask.astype(jnp.float32)], axis=-1)
    scale_pool = [scales] + [shifted(scales, "blk", -step) for step in range(1, offsets)]
    whitened = whiten(spectra, scales)
    first_bin, whitened = lax.optimization_barrier((lax.axis_index("freq") * bin_count, whitened))
    lag_basis = lag_table(first_bin, bin_count).reshape(2 * bin_count, NLAG)
    lag_basis = jnp.tile(lag_basis, (windows, 1))
    pair_lists = pair_rows[own_block]
    win_count = lax.axis_size("win")
    freq_count = lax.axis_size("freq")
    row_count = pair_rows.shape[-1]
    source_flat = whitened.reshape(channels, windows * 2 * bin_count)
    current = whitened
    reduced = []
    for offset in range(offsets):
        partner_flat = current.reshape(channels, windows * 2 * bin_count)
        source_rows = select_rows(source_flat, pair_lists[offset, 0])
        partner_rows = select_rows(partner_flat, pair_lists[offset, 1])
        source_rows = source_rows.reshape(row_count, windows, 2 * bin_count)
        partner_rows = partner_rows.reshape(row_count, windows, 2 * bin_count)
        source_real = source_rows[..., :bin_count]
        source_imag = source_rows[..., bin_count:]
        partner_real = partner_rows[..., :bin_count]
        partner_imag = partner_rows[..., bin_count:]
        cross_real = source_real * partner_real + source_imag * partner_imag
        cross_imag = source_imag * partner_real - source_real * partner_imag
        cross = jnp.concatenate([cross_real, cross_imag], axis=-1).astype(jnp.bfloat16)
        cross = cross.reshape(row_count, windows * 2 * bin_count)
        correlated = jnp.dot(cross, lag_basis, preferred_element_type=jnp.float32)
        if offset + 2 < offsets:
            correlated, raw_block = lax.optimization_barrier((correlated, next_raw))
            if offset == 0:
                current = whiten(raw_block, scale_pool[offset + 1])
            else:
                current = raw_block
            next_raw = shifted(current, "blk", -1)
            correlated, current = lax.optimization_barrier((correlated, current))
        elif offset + 1 < offsets:
            current = next_raw if offset > 0 else whiten(next_raw, scale_pool[offset + 1])
        reduced.append(slot_reduce(correlated))
    all_windows = windows * win_count
    scale = 1.0 / math.sqrt(all_bins * all_windows)
    own_owners = owner_map[own_block]
    if block_count > 4:
        summed = jnp.stack(reduced, axis=1)
        stacked = (summed * scale).astype(jnp.bfloat16)
        selector = (
            own_owners[None, :] == jnp.arange(block_count, dtype=jnp.int32)[:, None]
        ).astype(jnp.bfloat16)
        send_buffer = jnp.einsum(
            "ok,pkl->opl", selector, stacked, preferred_element_type=jnp.float32
        ).astype(jnp.bfloat16)
        received = lax.all_to_all(send_buffer, "blk", split_axis=0, concat_axis=0, tiled=True)
        return received[None]
    targets = (own_block + jnp.arange(block_count, dtype=jnp.int32)) % block_count
    masks = (own_owners[:, None] == targets[None, :]).astype(jnp.float32)
    send_buffer = None
    for offset, result in enumerate(reduced):
        stacked = (result * scale).astype(jnp.bfloat16).astype(jnp.float32)
        term = masks[offset][:, None, None] * stacked[None]
        send_buffer = term if send_buffer is None else send_buffer + term
    send_buffer = send_buffer.astype(jnp.bfloat16)
    parts = [send_buffer[0]]
    for distance in range(1, block_count):
        parts.append(shifted(send_buffer[distance], "blk", distance))
    sources = (own_block - jnp.arange(block_count, dtype=jnp.int32)) % block_count
    placement = (sources[None, :] == jnp.arange(block_count, dtype=jnp.int32)[:, None])
    flat_parts = jnp.stack(parts).reshape(block_count, -1)
    received = jnp.dot(
        placement.astype(jnp.bfloat16), flat_parts, preferred_element_type=jnp.float32
    ).astype(jnp.bfloat16)
    return received.reshape(send_buffer.shape)[None]


def solution(mesh):
    return jax.shard_map(
        body,
        mesh=mesh,
        in_specs=(
            P(("grp", "blk"), "win", None, "freq"),
            P(("grp", "blk"), "win"),
            P("grp", None, None, None),
            P("grp", None),
        ),
        out_specs=P(("grp", "blk"), None, ("win", "freq"), None),
        check_vma=False,
    )
```

```python
import math

import jax
import jax.numpy as jnp
from jax import lax
from jax.sharding import PartitionSpec as P

NLAG = 512
SAMPLES = 12000
LAG_STRIDE = 3


def shifted(value, axis, steps):
    count = lax.axis_size(axis)
    pairs = [(source, (source + steps) % count) for source in range(count)]
    return lax.ppermute(value, axis, pairs)


def pair_sum(value, axis):
    if lax.axis_size(axis) == 2:
        return value + shifted(value, axis, 1)
    return lax.psum(value, axis)


def half_reduce(value, axis):
    count = lax.axis_size(axis)
    if count == 2:
        index = lax.axis_index(axis)
        halves = value.reshape((2, value.shape[0] // 2) + value.shape[1:])
        keep = lax.dynamic_index_in_dim(halves, index, 0, keepdims=False)
        send = lax.dynamic_index_in_dim(halves, 1 - index, 0, keepdims=False)
        return keep + shifted(send, axis, 1)
    return lax.psum_scatter(value, axis, scatter_dimension=0, tiled=True)


def slot_reduce(value):
    if lax.axis_size("win") != 2 or lax.axis_size("freq") != 2:
        return half_reduce(half_reduce(value, "freq"), "win")
    axes = ("win", "freq")
    own = lax.axis_index("win") * 2 + lax.axis_index("freq")
    slots = value.reshape((4, value.shape[0] // 4) + value.shape[1:])
    total = lax.dynamic_index_in_dim(slots, own, 0, keepdims=False)
    for mask in (1, 2, 3):
        send = lax.dynamic_index_in_dim(slots, own ^ mask, 0, keepdims=False)
        pairs = [(source, source ^ mask) for source in range(4)]
        total = total + lax.ppermute(send, axes, pairs)
    return total


def lag_table(first_bin, bin_count):
    lag_numbers = (jnp.arange(NLAG, dtype=jnp.int32) - NLAG // 2) * LAG_STRIDE
    lag_steps = (lag_numbers + SAMPLES) % SAMPLES
    split = 32 if bin_count % 32 == 0 else 1
    fine_bins = first_bin + 1 + jnp.arange(split, dtype=jnp.int32)
    coarse_bins = jnp.arange(bin_count // split, dtype=jnp.int32) * split
    scale = 2.0 * math.pi / SAMPLES
    fine = (fine_bins[:, None] * lag_steps[None, :]) % SAMPLES
    coarse = (coarse_bins[:, None] * lag_steps[None, :]) % SAMPLES
    fine_angle = fine.astype(jnp.float32) * scale
    coarse_angle = coarse.astype(jnp.float32) * scale
    fine_cos, fine_sin = jnp.cos(fine_angle)[None], jnp.sin(fine_angle)[None]
    coarse_cos, coarse_sin = jnp.cos(coarse_angle)[:, None], jnp.sin(coarse_angle)[:, None]
    cosine = coarse_cos * fine_cos - coarse_sin * fine_sin
    sine = coarse_sin * fine_cos + coarse_cos * fine_sin
    table = jnp.stack([cosine, -sine]).reshape(2, bin_count, NLAG)
    return table.astype(jnp.bfloat16)


def select_rows(block, rows):
    channel_ids = jnp.arange(block.shape[0], dtype=rows.dtype)
    one_hot = (rows[:, None] == channel_ids[None, :]).astype(block.dtype)
    return jnp.dot(one_hot, block, preferred_element_type=jnp.float32)


def whiten(raw, scales):
    real_in = raw[:, :, 0].astype(jnp.float32)
    imag_in = raw[:, :, 1].astype(jnp.float32)
    energy = real_in * real_in + imag_in * imag_in
    factor = scales[:, :, 1:2] / jnp.sqrt(energy + scales[:, :, 0:1] + 1e-06)
    whitened = jnp.concatenate([real_in * factor, imag_in * factor], axis=-1)
    return whitened.astype(jnp.bfloat16)


def whiten_rows(raw, scales, rows):
    channel_ids = jnp.arange(raw.shape[0], dtype=rows.dtype)
    one_hot = rows[:, None] == channel_ids[None, :]
    picked = jnp.dot(
        one_hot.astype(raw.dtype), raw.reshape(raw.shape[0], -1),
        preferred_element_type=jnp.float32,
    ).reshape((rows.shape[0],) + raw.shape[1:])
    picked_scales = jnp.dot(
        one_hot.astype(jnp.float32), scales.reshape(scales.shape[0], -1),
        precision=lax.Precision.HIGHEST, preferred_element_type=jnp.float32,
    ).reshape((rows.shape[0],) + scales.shape[1:])
    real_in, imag_in = picked[:, :, 0], picked[:, :, 1]
    energy = real_in * real_in + imag_in * imag_in
    factor = picked_scales[:, :, 1:2] / jnp.sqrt(energy + picked_scales[:, :, 0:1] + 1e-06)
    whitened = jnp.concatenate([real_in * factor, imag_in * factor], axis=-1)
    whitened = lax.reduce_precision(whitened, exponent_bits=8, mantissa_bits=7)
    return whitened.reshape(rows.shape[0], -1)


def body(spectra, live_mask, pair_rows, owner_map):
    channels, windows, _, bin_count = spectra.shape
    block_count = lax.axis_size("blk")
    offsets = block_count // 2 + 1
    own_block = lax.axis_index("blk")
    next_raw = shifted(spectra, "blk", -1) if offsets > 1 else spectra
    real_in = spectra[:, :, 0].astype(jnp.float32)
    imag_in = spectra[:, :, 1].astype(jnp.float32)
    energy = real_in * real_in + imag_in * imag_in
    power_sums = pair_sum(jnp.sum(energy, axis=-1), "freq")
    all_bins = bin_count * lax.axis_size("freq")
    mean_power = power_sums / all_bins
    scales = jnp.stack([mean_power, live_mask.astype(jnp.float32)], axis=-1)
    scale_pool = [scales] + [shifted(scales, "blk", -step) for step in range(1, offsets)]
    whitened = whiten(spectra, scales)
    first_bin, whitened = lax.optimization_barrier((lax.axis_index("freq") * bin_count, whitened))
    lag_basis = lag_table(first_bin, bin_count).reshape(2 * bin_count, NLAG)
    lag_basis = jnp.tile(lag_basis, (windows, 1))
    pair_lists = pair_rows[own_block]
    win_count = lax.axis_size("win")
    freq_count = lax.axis_size("freq")
    row_count = pair_rows.shape[-1]
    source_flat = whitened.reshape(channels, windows * 2 * bin_count)
    current = whitened
    reduced = []
    for offset in range(offsets):
        source_rows = select_rows(source_flat, pair_lists[offset, 0])
        if current is None:
            partner_rows = whiten_rows(last_raw, last_scales, pair_lists[offset, 1])
        else:
            partner_flat = current.reshape(channels, windows * 2 * bin_count)
            partner_rows = select_rows(partner_flat, pair_lists[offset, 1])
        source_rows = source_rows.reshape(row_count, windows, 2 * bin_count)
        partner_rows = partner_rows.reshape(row_count, windows, 2 * bin_count)
        source_real = source_rows[..., :bin_count]
        source_imag = source_rows[..., bin_count:]
        partner_real = partner_rows[..., :bin_count]
        partner_imag = partner_rows[..., bin_count:]
        cross_real = source_real * partner_real + source_imag * partner_imag
        cross_imag = source_imag * partner_real - source_real * partner_imag
        cross = jnp.concatenate([cross_real, cross_imag], axis=-1).astype(jnp.bfloat16)
        cross = cross.reshape(row_count, windows * 2 * bin_count)
        correlated = jnp.dot(cross, lag_basis, preferred_element_type=jnp.float32)
        if offset + 2 < offsets:
            correlated, raw_block = lax.optimization_barrier((correlated, next_raw))
            next_raw = shifted(raw_block, "blk", -1)
            current = whiten(raw_block, scale_pool[offset + 1])
            correlated, current = lax.optimization_barrier((correlated, current))
        elif offset + 1 < offsets:
            current = None
            last_raw, last_scales = next_raw, scale_pool[offset + 1]
        reduced.append(slot_reduce(correlated))
    all_windows = windows * win_count
    scale = 1.0 / math.sqrt(all_bins * all_windows)
    own_owners = owner_map[own_block]
    if block_count > 4:
        summed = jnp.stack(reduced, axis=1)
        stacked = (summed * scale).astype(jnp.bfloat16)
        selector = (
            own_owners[None, :] == jnp.arange(block_count, dtype=jnp.int32)[:, None]
        ).astype(jnp.bfloat16)
        send_buffer = jnp.einsum(
            "ok,pkl->opl", selector, stacked, preferred_element_type=jnp.float32
        ).astype(jnp.bfloat16)
        received = lax.all_to_all(send_buffer, "blk", split_axis=0, concat_axis=0, tiled=True)
        return received[None]
    targets = (own_block + jnp.arange(block_count, dtype=jnp.int32)) % block_count
    masks = (own_owners[:, None] == targets[None, :]).astype(jnp.float32)
    send_buffer = None
    for offset, result in enumerate(reduced):
        stacked = (result * scale).astype(jnp.bfloat16).astype(jnp.float32)
        term = masks[offset][:, None, None] * stacked[None]
        send_buffer = term if send_buffer is None else send_buffer + term
    send_buffer = send_buffer.astype(jnp.bfloat16)
    parts = [send_buffer[0]]
    for distance in range(1, block_count):
        parts.append(shifted(send_buffer[distance], "blk", distance))
    sources = (own_block - jnp.arange(block_count, dtype=jnp.int32)) % block_count
    placement = (sources[None, :] == jnp.arange(block_count, dtype=jnp.int32)[:, None])
    flat_parts = jnp.stack(parts).reshape(block_count, -1)
    received = jnp.dot(
        placement.astype(jnp.bfloat16), flat_parts, preferred_element_type=jnp.float32
    ).astype(jnp.bfloat16)
    return received.reshape(send_buffer.shape)[None]


def solution(mesh):
    return jax.shard_map(
        body,
        mesh=mesh,
        in_specs=(
            P(("grp", "blk"), "win", None, "freq"),
            P(("grp", "blk"), "win"),
            P("grp", None, None, None),
            P("grp", None),
        ),
        out_specs=P(("grp", "blk"), None, ("win", "freq"), None),
        check_vma=False,
    )
```

```python
import math

import jax
import jax.numpy as jnp
from jax import lax
from jax.sharding import PartitionSpec as P

NLAG = 512
SAMPLES = 12000
LAG_STRIDE = 3


def shifted(value, axis, steps):
    count = lax.axis_size(axis)
    pairs = [(source, (source + steps) % count) for source in range(count)]
    return lax.ppermute(value, axis, pairs)


def pair_sum(value, axis):
    if lax.axis_size(axis) == 2:
        return value + shifted(value, axis, 1)
    return lax.psum(value, axis)


def half_reduce(value, axis):
    count = lax.axis_size(axis)
    if count == 2:
        index = lax.axis_index(axis)
        halves = value.reshape((2, value.shape[0] // 2) + value.shape[1:])
        keep = lax.dynamic_index_in_dim(halves, index, 0, keepdims=False)
        send = lax.dynamic_index_in_dim(halves, 1 - index, 0, keepdims=False)
        return keep + shifted(send, axis, 1)
    return lax.psum_scatter(value, axis, scatter_dimension=0, tiled=True)


def slot_reduce(value):
    if lax.axis_size("win") != 2 or lax.axis_size("freq") != 2:
        return half_reduce(half_reduce(value, "freq"), "win")
    axes = ("win", "freq")
    own = lax.axis_index("win") * 2 + lax.axis_index("freq")
    slots = value.reshape((4, value.shape[0] // 4) + value.shape[1:])
    total = lax.dynamic_index_in_dim(slots, own, 0, keepdims=False)
    for mask in (1, 2, 3):
        send = lax.dynamic_index_in_dim(slots, own ^ mask, 0, keepdims=False)
        pairs = [(source, source ^ mask) for source in range(4)]
        total = total + lax.ppermute(send, axes, pairs)
    return total


def lag_table(first_bin, bin_count):
    lag_numbers = (jnp.arange(NLAG, dtype=jnp.int32) - NLAG // 2) * LAG_STRIDE
    lag_steps = (lag_numbers + SAMPLES) % SAMPLES
    split = 32 if bin_count % 32 == 0 else 1
    fine_bins = first_bin + 1 + jnp.arange(split, dtype=jnp.int32)
    coarse_bins = jnp.arange(bin_count // split, dtype=jnp.int32) * split
    scale = 2.0 * math.pi / SAMPLES
    fine = (fine_bins[:, None] * lag_steps[None, :]) % SAMPLES
    coarse = (coarse_bins[:, None] * lag_steps[None, :]) % SAMPLES
    fine_angle = fine.astype(jnp.float32) * scale
    coarse_angle = coarse.astype(jnp.float32) * scale
    fine_cos, fine_sin = jnp.cos(fine_angle)[None], jnp.sin(fine_angle)[None]
    coarse_cos, coarse_sin = jnp.cos(coarse_angle)[:, None], jnp.sin(coarse_angle)[:, None]
    cosine = coarse_cos * fine_cos - coarse_sin * fine_sin
    sine = coarse_sin * fine_cos + coarse_cos * fine_sin
    table = jnp.stack([cosine, -sine]).reshape(2, bin_count, NLAG)
    return table.astype(jnp.bfloat16)


def select_rows(block, rows):
    channel_ids = jnp.arange(block.shape[0], dtype=rows.dtype)
    one_hot = (rows[:, None] == channel_ids[None, :]).astype(block.dtype)
    return jnp.dot(one_hot, block, preferred_element_type=jnp.float32)


def whiten(raw, scales):
    real_in = raw[:, :, 0].astype(jnp.float32)
    imag_in = raw[:, :, 1].astype(jnp.float32)
    energy = real_in * real_in + imag_in * imag_in
    factor = scales[:, :, 1:2] / jnp.sqrt(energy + scales[:, :, 0:1] + 1e-06)
    whitened = jnp.concatenate([real_in * factor, imag_in * factor], axis=-1)
    return whitened.astype(jnp.bfloat16)


def body(spectra, live_mask, pair_rows, owner_map):
    channels, windows, _, bin_count = spectra.shape
    block_count = lax.axis_size("blk")
    offsets = block_count // 2 + 1
    own_block = lax.axis_index("blk")
    next_raw = shifted(spectra, "blk", -1) if offsets > 1 else spectra
    real_in = spectra[:, :, 0].astype(jnp.float32)
    imag_in = spectra[:, :, 1].astype(jnp.float32)
    energy = real_in * real_in + imag_in * imag_in
    power_sums = pair_sum(jnp.sum(energy, axis=-1), "freq")
    all_bins = bin_count * lax.axis_size("freq")
    mean_power = power_sums / all_bins
    scales = jnp.stack([mean_power, live_mask.astype(jnp.float32)], axis=-1)
    scale_pool = [scales] + [shifted(scales, "blk", -step) for step in range(1, offsets)]
    whitened = whiten(spectra, scales)
    first_bin, whitened = lax.optimization_barrier((lax.axis_index("freq") * bin_count, whitened))
    lag_basis = lag_table(first_bin, bin_count).reshape(2 * bin_count, NLAG)
    lag_basis = jnp.tile(lag_basis, (windows, 1))
    pair_lists = pair_rows[own_block]
    win_count = lax.axis_size("win")
    freq_count = lax.axis_size("freq")
    row_count = pair_rows.shape[-1]
    source_flat = whitened.reshape(channels, windows * 2 * bin_count)
    current = whitened
    reduced = []
    for offset in range(offsets):
        partner_flat = current.reshape(channels, windows * 2 * bin_count)
        source_rows = select_rows(source_flat, pair_lists[offset, 0])
        partner_rows = select_rows(partner_flat, pair_lists[offset, 1])
        source_rows = source_rows.reshape(row_count, windows, 2 * bin_count)
        partner_rows = partner_rows.reshape(row_count, windows, 2 * bin_count)
        source_real = source_rows[..., :bin_count]
        source_imag = source_rows[..., bin_count:]
        partner_real = partner_rows[..., :bin_count]
        partner_imag = partner_rows[..., bin_count:]
        cross_real = source_real * partner_real + source_imag * partner_imag
        cross_imag = source_imag * partner_real - source_real * partner_imag
        cross = jnp.concatenate([cross_real, cross_imag], axis=-1).astype(jnp.bfloat16)
        cross = cross.reshape(row_count, windows * 2 * bin_count)
        correlated = jnp.dot(cross, lag_basis, preferred_element_type=jnp.float32)
        if offset + 2 < offsets:
            correlated, raw_block = lax.optimization_barrier((correlated, next_raw))
            if offset == 0:
                current = whiten(raw_block, scale_pool[offset + 1])
            else:
                current = raw_block
            next_raw = shifted(current, "blk", -1)
            correlated, current = lax.optimization_barrier((correlated, current))
        elif offset + 1 < offsets:
            current = next_raw if offset > 0 else whiten(next_raw, scale_pool[offset + 1])
        reduced.append(slot_reduce(correlated))
    all_windows = windows * win_count
    scale = 1.0 / math.sqrt(all_bins * all_windows)
    own_owners = owner_map[own_block]
    if block_count > 4:
        summed = jnp.stack(reduced, axis=1)
        stacked = (summed * scale).astype(jnp.bfloat16)
        selector = (
            own_owners[None, :] == jnp.arange(block_count, dtype=jnp.int32)[:, None]
        ).astype(jnp.bfloat16)
        send_buffer = jnp.einsum(
            "ok,pkl->opl", selector, stacked, preferred_element_type=jnp.float32
        ).astype(jnp.bfloat16)
        received = lax.all_to_all(send_buffer, "blk", split_axis=0, concat_axis=0, tiled=True)
        return received[None]
    targets = (own_block + jnp.arange(block_count, dtype=jnp.int32)) % block_count
    masks = (own_owners[:, None] == targets[None, :]).astype(jnp.float32)
    send_buffer = None
    for offset, result in enumerate(reduced):
        stacked = (result * scale).astype(jnp.bfloat16).astype(jnp.float32)
        term = masks[offset][:, None, None] * stacked[None]
        send_buffer = term if send_buffer is None else send_buffer + term
    send_buffer = send_buffer.astype(jnp.bfloat16)
    parts = [send_buffer[0]]
    for distance in range(1, block_count):
        parts.append(shifted(send_buffer[distance], "blk", distance))
    sources = (own_block - jnp.arange(block_count, dtype=jnp.int32)) % block_count
    placement = (sources[None, :] == jnp.arange(block_count, dtype=jnp.int32)[:, None])
    weights = placement.astype(jnp.float32)
    received = None
    for distance, part in enumerate(parts):
        term = weights[:, distance][:, None, None] * part.astype(jnp.float32)[None]
        received = term if received is None else received + term
    return received.astype(jnp.bfloat16)[None]


def solution(mesh):
    return jax.shard_map(
        body,
        mesh=mesh,
        in_specs=(
            P(("grp", "blk"), "win", None, "freq"),
            P(("grp", "blk"), "win"),
            P("grp", None, None, None),
            P("grp", None),
        ),
        out_specs=P(("grp", "blk"), None, ("win", "freq"), None),
        check_vma=False,
    )
```

```python
import math

import jax
import jax.numpy as jnp
from jax import lax
from jax.sharding import PartitionSpec as P

NLAG = 512
SAMPLES = 12000
LAG_STRIDE = 3


def shifted(value, axis, steps):
    count = lax.axis_size(axis)
    pairs = [(source, (source + steps) % count) for source in range(count)]
    return lax.ppermute(value, axis, pairs)


def pair_sum(value, axis):
    if lax.axis_size(axis) == 2:
        return value + shifted(value, axis, 1)
    return lax.psum(value, axis)


def half_reduce(value, axis):
    count = lax.axis_size(axis)
    if count == 2:
        index = lax.axis_index(axis)
        halves = value.reshape((2, value.shape[0] // 2) + value.shape[1:])
        keep = lax.dynamic_index_in_dim(halves, index, 0, keepdims=False)
        send = lax.dynamic_index_in_dim(halves, 1 - index, 0, keepdims=False)
        return keep + shifted(send, axis, 1)
    return lax.psum_scatter(value, axis, scatter_dimension=0, tiled=True)


def slot_reduce(value):
    if lax.axis_size("win") != 2 or lax.axis_size("freq") != 2:
        return half_reduce(half_reduce(value, "freq"), "win")
    axes = ("win", "freq")
    own = lax.axis_index("win") * 2 + lax.axis_index("freq")
    slots = value.reshape((4, value.shape[0] // 4) + value.shape[1:])
    total = lax.dynamic_index_in_dim(slots, own, 0, keepdims=False)
    for mask in (3, 2, 1):
        send = lax.dynamic_index_in_dim(slots, own ^ mask, 0, keepdims=False)
        pairs = [(source, source ^ mask) for source in range(4)]
        total = total + lax.ppermute(send, axes, pairs)
    return total


def lag_table(first_bin, bin_count):
    lag_numbers = (jnp.arange(NLAG, dtype=jnp.int32) - NLAG // 2) * LAG_STRIDE
    lag_steps = (lag_numbers + SAMPLES) % SAMPLES
    split = 32 if bin_count % 32 == 0 else 1
    fine_bins = first_bin + 1 + jnp.arange(split, dtype=jnp.int32)
    coarse_bins = jnp.arange(bin_count // split, dtype=jnp.int32) * split
    scale = 2.0 * math.pi / SAMPLES
    fine = (fine_bins[:, None] * lag_steps[None, :]) % SAMPLES
    coarse = (coarse_bins[:, None] * lag_steps[None, :]) % SAMPLES
    fine_angle = fine.astype(jnp.float32) * scale
    coarse_angle = coarse.astype(jnp.float32) * scale
    fine_cos, fine_sin = jnp.cos(fine_angle)[None], jnp.sin(fine_angle)[None]
    coarse_cos, coarse_sin = jnp.cos(coarse_angle)[:, None], jnp.sin(coarse_angle)[:, None]
    cosine = coarse_cos * fine_cos - coarse_sin * fine_sin
    sine = coarse_sin * fine_cos + coarse_cos * fine_sin
    table = jnp.stack([cosine, -sine]).reshape(2, bin_count, NLAG)
    return table.astype(jnp.bfloat16)


def select_rows(block, rows):
    channel_ids = jnp.arange(block.shape[0], dtype=rows.dtype)
    one_hot = (rows[:, None] == channel_ids[None, :]).astype(block.dtype)
    return jnp.dot(one_hot, block, preferred_element_type=jnp.float32)


def whiten(raw, scales):
    real_in = raw[:, :, 0].astype(jnp.float32)
    imag_in = raw[:, :, 1].astype(jnp.float32)
    energy = real_in * real_in + imag_in * imag_in
    factor = scales[:, :, 1:2] / jnp.sqrt(energy + scales[:, :, 0:1] + 1e-06)
    whitened = jnp.concatenate([real_in * factor, imag_in * factor], axis=-1)
    return whitened.astype(jnp.bfloat16)


def body(spectra, live_mask, pair_rows, owner_map):
    channels, windows, _, bin_count = spectra.shape
    block_count = lax.axis_size("blk")
    offsets = block_count // 2 + 1
    own_block = lax.axis_index("blk")
    next_raw = shifted(spectra, "blk", -1) if offsets > 1 else spectra
    real_in = spectra[:, :, 0].astype(jnp.float32)
    imag_in = spectra[:, :, 1].astype(jnp.float32)
    energy = real_in * real_in + imag_in * imag_in
    power_sums = pair_sum(jnp.sum(energy, axis=-1), "freq")
    all_bins = bin_count * lax.axis_size("freq")
    mean_power = power_sums / all_bins
    scales = jnp.stack([mean_power, live_mask.astype(jnp.float32)], axis=-1)
    scale_pool = [scales] + [shifted(scales, "blk", -step) for step in range(1, offsets)]
    whitened = whiten(spectra, scales)
    first_bin, whitened = lax.optimization_barrier((lax.axis_index("freq") * bin_count, whitened))
    lag_basis = lag_table(first_bin, bin_count).reshape(2 * bin_count, NLAG)
    lag_basis = jnp.tile(lag_basis, (windows, 1))
    pair_lists = pair_rows[own_block]
    win_count = lax.axis_size("win")
    freq_count = lax.axis_size("freq")
    row_count = pair_rows.shape[-1]
    source_flat = whitened.reshape(channels, windows * 2 * bin_count)
    current = whitened
    reduced = []
    for offset in range(offsets):
        partner_flat = current.reshape(channels, windows * 2 * bin_count)
        source_rows = select_rows(source_flat, pair_lists[offset, 0])
        partner_rows = select_rows(partner_flat, pair_lists[offset, 1])
        source_rows = source_rows.reshape(row_count, windows, 2 * bin_count)
        partner_rows = partner_rows.reshape(row_count, windows, 2 * bin_count)
        source_real = source_rows[..., :bin_count]
        source_imag = source_rows[..., bin_count:]
        partner_real = partner_rows[..., :bin_count]
        partner_imag = partner_rows[..., bin_count:]
        cross_real = source_real * partner_real + source_imag * partner_imag
        cross_imag = source_imag * partner_real - source_real * partner_imag
        cross = jnp.concatenate([cross_real, cross_imag], axis=-1).astype(jnp.bfloat16)
        cross = cross.reshape(row_count, windows * 2 * bin_count)
        correlated = jnp.dot(cross, lag_basis, preferred_element_type=jnp.float32)
        if offset + 2 < offsets:
            correlated, raw_block = lax.optimization_barrier((correlated, next_raw))
            if offset == 0:
                current = whiten(raw_block, scale_pool[offset + 1])
            else:
                current = raw_block
            next_raw = shifted(current, "blk", -1)
            correlated, current = lax.optimization_barrier((correlated, current))
        elif offset + 1 < offsets:
            current = next_raw if offset > 0 else whiten(next_raw, scale_pool[offset + 1])
        reduced.append(slot_reduce(correlated))
    all_windows = windows * win_count
    scale = 1.0 / math.sqrt(all_bins * all_windows)
    own_owners = owner_map[own_block]
    if block_count > 4:
        summed = jnp.stack(reduced, axis=1)
        stacked = (summed * scale).astype(jnp.bfloat16)
        selector = (
            own_owners[None, :] == jnp.arange(block_count, dtype=jnp.int32)[:, None]
        ).astype(jnp.bfloat16)
        send_buffer = jnp.einsum(
            "ok,pkl->opl", selector, stacked, preferred_element_type=jnp.float32
        ).astype(jnp.bfloat16)
        received = lax.all_to_all(send_buffer, "blk", split_axis=0, concat_axis=0, tiled=True)
        return received[None]
    targets = (own_block + jnp.arange(block_count, dtype=jnp.int32)) % block_count
    masks = (own_owners[:, None] == targets[None, :]).astype(jnp.float32)
    send_buffer = None
    for offset, result in enumerate(reduced):
        stacked = (result * scale).astype(jnp.bfloat16).astype(jnp.float32)
        term = masks[offset][:, None, None] * stacked[None]
        send_buffer = term if send_buffer is None else send_buffer + term
    send_buffer = send_buffer.astype(jnp.bfloat16)
    parts = [send_buffer[0]]
    for distance in range(1, block_count):
        parts.append(shifted(send_buffer[distance], "blk", distance))
    sources = (own_block - jnp.arange(block_count, dtype=jnp.int32)) % block_count
    placement = (sources[None, :] == jnp.arange(block_count, dtype=jnp.int32)[:, None])
    weights = placement.astype(jnp.float32)
    received = None
    for distance, part in enumerate(parts):
        term = weights[:, distance][:, None, None] * part.astype(jnp.float32)[None]
        received = term if received is None else received + term
    return received.astype(jnp.bfloat16)[None]


def solution(mesh):
    return jax.shard_map(
        body,
        mesh=mesh,
        in_specs=(
            P(("grp", "blk"), "win", None, "freq"),
            P(("grp", "blk"), "win"),
            P("grp", None, None, None),
            P("grp", None),
        ),
        out_specs=P(("grp", "blk"), None, ("win", "freq"), None),
        check_vma=False,
    )
```
